32 devices in a mesh: parts: 2 (over y), pix: 4 (over z), ang: 2 (over x), sl: 2 (over core).
Axes of the slice: x: 2, y: 2, z: 4, core: 2. Of those that a mesh axis runs over, the one named last changes fastest.
Arguments:
- volume: float32 [512, 1024], P(('parts', 'pix'), 'sl'), parts along dimension 0, may hold values from 0 to 2
- sinogram: float32 [4, 32, 1024], P(('parts', 'ang'), 'pix', 'sl'), parts along dimension 0, may hold values from 0 to 5632
- table: bfloat16 [32, 4096], replicated, may hold values from 0.015 to 1
- blk_ray: int32 [2, 4, 1408], P('ang', 'pix'), may hold values from 0 to 31, as said below
- blk_pix: int32 [2, 4, 1408], P('ang', 'pix'), may hold values from 0 to 63, as said below
Outputs:
- volume_out: float32 [512, 1024], P(('parts', 'pix'), 'sl'), parts along dimension 0
- residual: float32 [4, 32, 1024], P(('parts', 'ang'), 'pix', 'sl'), parts along dimension 0
The draws below stay inside these ranges and needn't reach their ends.
There are 2 independent parts, one for each index of `parts`. The reference program is written for one: setup_inputs(seed, part) draws one part's arguments, and reference() takes and returns one part's arrays. A program takes and returns all parts, laid end to end along the dimension named above; an argument that names none is the same for every part. Nothing has to cross between parts.
Inputs may be any that keep to these rules, and one draw needn't show every extreme that they name: `blk_ray`: entry [g, p, b] is a ray tile of group g. The blocks of each (g, p) name every ray tile from 8 * p to 8 * p + 7, and at most 4 distinct ray tiles of any other such range of 8 tiles; in each group some range has exactly 4 of its tiles named by every other p. `blk_pix`: the blocks of each (g, p) name every pixel tile from 0 to 63.
All inputs are finite; a program needn't handle non-finite values.
Results may differ from the reference program's by a relative error of at most 0.0003.
Values may be sent and summed in bfloat16 or wider, within the bound.
No kernel may reach another device: no remote copies, remote signals or barrier semaphores. Data moves between devices by JAX's collectives and lax.ppermute only.
A program may use at most 64 MiB of HBM per device.

```python
from functools import partial
import jax
import jax.numpy as jnp
from jax import lax

TILE = 64
KINDS = 32
CAP = 4
ITERS = 2
SL_DEV = 8
PT_DEV = 64
RT_DEV = 8
PER_KIND = 44
NBD = 1408
S = 16
RT_G = 32
PIX_TILES = 256
N_PIX = 4
N_ANG = 2
N_SL = 2


def lists_for_device(device_key, busy_owner, device):
    sub_keys = jax.random.split(device_key, 4)
    owners = jnp.arange(N_PIX, dtype=jnp.int32)
    counts = jax.random.randint(sub_keys[0], (N_PIX,), 0, CAP + 1).astype(jnp.int32)
    full_owner = (busy_owner + (device == busy_owner).astype(jnp.int32)) % N_PIX
    counts = jnp.where(owners == full_owner, CAP, counts)
    counts = jnp.where(owners == device, RT_DEV, counts)
    random_bits = jax.random.randint(sub_keys[1], (N_PIX, RT_DEV), 0, 1048576) * RT_DEV
    random_bits = random_bits + jnp.arange(RT_DEV, dtype=jnp.int32)[None, :]
    local_order = jnp.argsort(random_bits, axis=1).astype(jnp.int32)
    tile_ids = owners[:, None] * RT_DEV + local_order
    live_slot = jnp.arange(RT_DEV, dtype=jnp.int32)[None, :] < counts[:, None]
    shuffled = jax.random.permutation(sub_keys[2], N_PIX * RT_DEV).astype(jnp.int32).reshape(N_PIX, RT_DEV)
    slot_score = (1 - live_slot.astype(jnp.int32)) * (N_PIX * RT_DEV) + shuffled
    slot_order = jnp.argsort(slot_score.reshape(-1)).astype(jnp.int32)
    live_count = jnp.sum(live_slot.astype(jnp.int32))
    chosen = jax.random.permutation(sub_keys[3], NBD).astype(jnp.int32) % live_count
    return jnp.take(tile_ids.reshape(-1), jnp.take(slot_order, chosen)).astype(jnp.int32)


def draw_blk_ray(key, part):
    busy_owners = jax.random.randint(jax.random.fold_in(key, 7001), (N_ANG,), 0, N_PIX).astype(jnp.int32)
    groups = jnp.arange(N_ANG, dtype=jnp.int32)
    devices = jnp.arange(N_PIX, dtype=jnp.int32)

    def per_group(group_index):
        group_key = jax.random.fold_in(jax.random.fold_in(key, 7002), group_index)

        def per_device(device):
            return lists_for_device(jax.random.fold_in(group_key, device), busy_owners[group_index], device)
        return jax.vmap(per_device)(devices)
    return jax.vmap(per_group)(groups)


def draw_blk_pix(key, part):
    flat_keys = jax.random.split(jax.random.fold_in(key, 7003), N_ANG * N_PIX)

    def per_device(device_key):
        sub_keys = jax.random.split(device_key, 3)
        weights = jax.random.randint(sub_keys[0], (PT_DEV,), 1, 9).astype(jnp.int32)
        weights = weights * weights
        bounds = jnp.cumsum(weights).astype(jnp.int32)
        picks = jax.random.randint(sub_keys[1], (NBD - PT_DEV,), 0, bounds[PT_DEV - 1]).astype(jnp.int32)
        extra = jnp.searchsorted(bounds, picks, side='right').astype(jnp.int32)
        ids = jnp.concatenate([jnp.arange(PT_DEV, dtype=jnp.int32), extra], axis=0)
        order = jax.random.permutation(sub_keys[2], NBD).astype(jnp.int32)
        return jnp.take(ids, order).astype(jnp.int32)
    return jax.vmap(per_device)(flat_keys).reshape(N_ANG, N_PIX, NBD)


def draw_table(key, part):
    shifts = jax.random.randint(jax.random.fold_in(key, 7101), (KINDS,), -2, 3).astype(jnp.int32)
    rows = jnp.arange(TILE, dtype=jnp.int32)[None, :, None]
    cols = jnp.arange(TILE, dtype=jnp.int32)[None, None, :]
    near = jnp.abs(rows - cols - shifts[:, None, None]) <= 2
    base = jax.random.uniform(jax.random.fold_in(key, 7102), (KINDS, TILE, TILE), jnp.float32)
    band = 0.6 + 0.4 * base
    outside = 0.02 + 0.06 * base
    values = jnp.where(near, band, outside)
    return values.reshape(KINDS, TILE * TILE).astype(jnp.bfloat16)


def draw_sinogram(key, part):
    level = (4 + TILE // 16) * NBD / RT_DEV
    width = S * TILE
    position = (jnp.arange(width, dtype=jnp.int32) % TILE).astype(jnp.float32)
    ramp = 2.0 * position / (TILE - 1) - 1.0
    rough = jax.random.uniform(jax.random.fold_in(key, 7201), (width,), jnp.float32, -1.0, 1.0)
    profile = 1.0 + 0.5 * (0.6 * ramp + 0.4 * rough)
    tile_level = jax.random.uniform(jax.random.fold_in(key, 7202), (N_ANG, RT_G, 1), jnp.float32, 0.8, 1.2)
    noise = jnp.clip(0.08 * jax.random.normal(jax.random.fold_in(key, 7203), (N_ANG, RT_G, width), jnp.float32), -0.25, 0.25)
    values = level * tile_level * profile[None, None, :] * (1.0 + noise)
    return values.astype(jnp.float32)


def block_scale(stream_key, extent, pieces, low, top_value):
    gain, own = 1.0, jax.random.fold_in(stream_key, 6)
    for axis_at, shards_of in pieces:
        draws = jnp.exp(jax.random.uniform(jax.random.fold_in(own, axis_at), (shards_of,), jnp.float32, low / len(pieces), top_value / len(pieces)))
        gain = gain * jnp.repeat(draws, extent[axis_at] // shards_of).reshape([-1 if axis == axis_at else 1 for axis in range(len(extent))])
    return gain


def setup_inputs(seed: int = 0, part: int = 0) -> dict:
    streams_of = jax.random.split(jax.random.key(seed), 6)
    part_keys = jax.random.split(jax.random.fold_in(streams_of[5], part), 6)
    return {
        "volume": jnp.clip(2.0 * jax.random.uniform(part_keys[0], (PIX_TILES, S * TILE), jnp.float32) ** block_scale(part_keys[0], (PIX_TILES, S * TILE), ((0, 4), (1, 2)), -0.2, 0.2), 0.0, 2.0),
        "sinogram": draw_sinogram(jax.random.fold_in(jax.random.fold_in(streams_of[5], part), 71), part),
        "table": draw_table(jax.random.fold_in(streams_of[5], 71), part),
        "blk_ray": draw_blk_ray(jax.random.fold_in(streams_of[5], 71), part),
        "blk_pix": draw_blk_pix(jax.random.fold_in(streams_of[5], 71), part),
    }


def reference(volume, sinogram, table, blk_ray, blk_pix):
    pattern = table.astype(jnp.float32).reshape(KINDS, TILE, TILE)
    slices = SL_DEV * N_SL
    ray_total = RT_DEV * N_PIX
    pixel_total = PT_DEV * N_PIX
    offsets = (jnp.arange(N_PIX, dtype=jnp.int32) * PT_DEV)[None, :, None]
    pixel_global = (blk_pix + offsets).astype(jnp.int32)
    row_block = jnp.broadcast_to(jnp.sum(pattern, axis=2)[:, None, :], (KINDS, PER_KIND, TILE)).reshape(NBD, TILE)
    col_block = jnp.broadcast_to(jnp.sum(pattern, axis=1)[:, None, :], (KINDS, PER_KIND, TILE)).reshape(NBD, TILE)
    ray_global = (jnp.arange(N_ANG, dtype=jnp.int32)[:, None, None] * ray_total + blk_ray).astype(jnp.int32)
    row_data = jnp.broadcast_to(row_block[None, None], (N_ANG, N_PIX, NBD, TILE)).reshape(-1, TILE)
    col_data = jnp.broadcast_to(col_block[None, None], (N_ANG, N_PIX, NBD, TILE)).reshape(-1, TILE)
    ray_weight = jax.ops.segment_sum(row_data, ray_global.reshape(-1), N_ANG * ray_total).reshape(N_ANG, ray_total, TILE)
    pixel_weight = jax.ops.segment_sum(col_data, pixel_global.reshape(-1), pixel_total)
    groups = jnp.arange(N_ANG, dtype=jnp.int32)

    def project_group(low_tiles, group_index):
        picked = jnp.take(low_tiles, pixel_global[group_index].reshape(-1), axis=0)
        picked = picked.reshape(N_PIX, KINDS, PER_KIND, slices, TILE)
        images = jnp.einsum("pkbsj,kij->pkbsi", picked, pattern).reshape(N_PIX * NBD, slices * TILE)
        return jax.ops.segment_sum(images, blk_ray[group_index].reshape(-1), ray_total)

    def back_group(scaled_low, group_index):
        ray_rows = scaled_low[group_index].reshape(ray_total, slices, TILE)
        picked = jnp.take(ray_rows, blk_ray[group_index].reshape(-1), axis=0)
        picked = picked.reshape(N_PIX, KINDS, PER_KIND, slices, TILE)
        images = jnp.einsum("pkbsi,kij->pkbsj", picked, pattern).reshape(N_PIX * NBD, slices * TILE)
        return jax.ops.segment_sum(images, pixel_global[group_index].reshape(-1), pixel_total)

    current = volume
    scaled = sinogram
    for iteration in range(ITERS):
        low_volume = lax.optimization_barrier(current.astype(jnp.bfloat16)).astype(jnp.float32)
        low_tiles = low_volume.reshape(pixel_total, slices, TILE)
        projection = lax.map(partial(project_group, low_tiles), groups)
        scaled = (sinogram - projection) / jnp.tile(ray_weight, (1, 1, slices))
        scaled_low = lax.optimization_barrier(scaled.astype(jnp.bfloat16)).astype(jnp.float32)
        update = jnp.sum(lax.map(partial(back_group, scaled_low), groups), axis=0)
        current = current + update / jnp.tile(pixel_weight, (1, slices))
    return current, scaled
```

```python
import jax
import jax.numpy as jnp
from jax import lax
from jax.sharding import PartitionSpec as P

TILE = 64
KINDS = 32
ITERS = 2
PER_KIND = 44


def project_local(low_volume, pattern, pixel_list, ray_list, ray_total):
    tiles_dev = low_volume.shape[0]
    slices = low_volume.shape[1] // TILE
    low_tiles = low_volume.reshape(tiles_dev, slices, TILE)
    kinds_each = KINDS // 4

    def project_one_group(running, inputs):
        patterns, pix_ids, ray_ids = inputs
        picked = jnp.take(low_tiles, pix_ids, axis=0).reshape(kinds_each, PER_KIND, slices, TILE)
        images = jnp.einsum("kbsj,kij->kbsi", picked, patterns, preferred_element_type=jnp.float32)
        images = images.reshape(kinds_each * PER_KIND, slices * TILE)
        return (running + jax.ops.segment_sum(images, ray_ids, ray_total), None)

    inputs = (
        pattern.reshape(4, kinds_each, TILE, TILE),
        pixel_list.reshape(4, -1),
        ray_list.reshape(4, -1),
    )
    initial = jnp.zeros((ray_total, slices * TILE), jnp.float32)
    running, unused = lax.scan(project_one_group, initial, inputs)
    return running


def back_local(row_table, pattern, pixel_list, row_index, tiles_dev):
    slices = row_table.shape[1] // TILE
    table_tiles = row_table.reshape(row_table.shape[0], slices, TILE)
    kinds_each = KINDS // 4

    def back_one_group(running, inputs):
        patterns, pix_ids, row_ids = inputs
        picked = jnp.take(table_tiles, row_ids, axis=0).reshape(kinds_each, PER_KIND, slices, TILE)
        images = jnp.einsum("kbsi,kij->kbsj", picked, patterns, preferred_element_type=jnp.float32)
        images = images.reshape(kinds_each * PER_KIND, slices * TILE)
        return (running + jax.ops.segment_sum(images, pix_ids, tiles_dev), None)

    inputs = (
        pattern.reshape(4, kinds_each, TILE, TILE),
        pixel_list.reshape(4, -1),
        row_index.reshape(4, -1),
    )
    initial = jnp.zeros((tiles_dev, slices * TILE), jnp.float32)
    running, unused = lax.scan(back_one_group, initial, inputs)
    return running


def per_device_base(volume, sinogram, table, blk_ray, blk_pix):
    pix_count = lax.axis_size("pix")
    tiles_dev = volume.shape[0]
    row_width = volume.shape[1]
    slices = row_width // TILE
    rays_dev = sinogram.shape[1]
    ray_total = rays_dev * pix_count
    ray_list = blk_ray.reshape(-1)
    pixel_list = blk_pix.reshape(-1)
    pattern = table.reshape(KINDS, TILE, TILE)
    pattern_wide = table.astype(jnp.float32).reshape(KINDS, TILE, TILE)
    row_block = jnp.broadcast_to(
        jnp.sum(pattern_wide, axis=2)[:, None, :], (KINDS, PER_KIND, TILE)
    ).reshape(-1, TILE)
    col_block = jnp.broadcast_to(
        jnp.sum(pattern_wide, axis=1)[:, None, :], (KINDS, PER_KIND, TILE)
    ).reshape(-1, TILE)
    row_part = jax.ops.segment_sum(row_block, ray_list, ray_total)
    col_part = jax.ops.segment_sum(col_block, pixel_list, tiles_dev)
    measured = sinogram[0]
    col_weight = lax.psum(col_part, "ang")
    current = volume
    scaled = measured
    for iteration in range(ITERS):
        low_volume = current.astype(jnp.bfloat16)
        partial_rows = project_local(low_volume, pattern, pixel_list, ray_list, ray_total)
        if iteration == 0:
            summed, row_weight = (
                lax.psum_scatter(partial_rows, "pix", scatter_dimension=0, tiled=True),
                lax.psum_scatter(row_part, "pix", scatter_dimension=0, tiled=True),
            )
        else:
            summed = lax.psum_scatter(partial_rows, "pix", scatter_dimension=0, tiled=True)
        scaled = (measured - summed) / jnp.tile(row_weight, (1, slices))
        scaled_low = scaled.astype(jnp.bfloat16)
        row_table = lax.all_gather(scaled_low, "pix", axis=0, tiled=True)
        back_sum = back_local(row_table, pattern, pixel_list, ray_list, tiles_dev)
        summed_update = lax.psum(back_sum, "ang")
        current = current + summed_update / jnp.tile(col_weight, (1, slices))
    return (current, scaled[None])


def split3(x):
    hi = lax.reduce_precision(x, exponent_bits=8, mantissa_bits=7)
    rest = x - hi
    mid = lax.reduce_precision(rest, exponent_bits=8, mantissa_bits=7)
    low = rest - mid
    return (hi.astype(jnp.bfloat16), mid.astype(jnp.bfloat16), low.astype(jnp.bfloat16))


def per_device_split(volume, sinogram, table, blk_ray, blk_pix, n_pix, n_ang):
    n_grp = n_pix * n_ang
    tiles_dev = volume.shape[0]
    slices = volume.shape[1] // TILE
    per_dev = slices // n_grp
    rays_dev = sinogram.shape[1]
    nbd = blk_ray.shape[-1]
    ray_total = rays_dev * n_pix
    pix_total = tiles_dev * n_pix
    width = per_dev * TILE

    vol_send = volume.reshape(tiles_dev, n_grp, width).transpose(1, 0, 2)
    sino_send = sinogram[0].reshape(rays_dev, n_grp, width).transpose(1, 0, 2)
    lists = jnp.stack([blk_ray.reshape(-1), blk_pix.reshape(-1)]).astype(jnp.float32)
    list_rows = (2 * nbd + width - 1) // width
    lists = jnp.pad(lists.reshape(-1), (0, list_rows * width - 2 * nbd)).reshape(list_rows, width)
    list_send = jnp.broadcast_to(lists[None], (n_grp, list_rows, width))
    send = jnp.concatenate([vol_send, sino_send, list_send], axis=1)
    recv = lax.all_to_all(send, ("pix", "ang"), 0, 0, tiled=False)
    recv = recv.reshape(n_pix, n_ang, tiles_dev + rays_dev + list_rows, width)

    current = recv[:, 0, :tiles_dev].reshape(pix_total, width)
    measured = recv[:, :, tiles_dev:tiles_dev + rays_dev].transpose(1, 0, 2, 3).reshape(n_ang, ray_total, width)
    got = recv[:, :, tiles_dev + rays_dev:].reshape(n_pix, n_ang, -1)[:, :, :2 * nbd]
    got = got.reshape(n_pix, n_ang, 2, nbd).transpose(2, 1, 0, 3).astype(jnp.int32)
    ray_ids = got[0].reshape(n_ang, n_pix, KINDS, nbd // KINDS)
    pix_ids = got[1].reshape(n_ang, n_pix, KINDS, nbd // KINDS)

    one_ray = (ray_ids[..., None] == jnp.arange(ray_total, dtype=jnp.int32)).astype(jnp.bfloat16)
    one_pix = (pix_ids[..., None] == jnp.arange(tiles_dev, dtype=jnp.int32)).astype(jnp.bfloat16)
    counts = jnp.einsum("gpkbv,gpkbu->gkvpu", one_ray, one_pix, preferred_element_type=jnp.float32)
    counts = counts.reshape(n_ang, KINDS, ray_total, pix_total)
    count_low = counts.astype(jnp.bfloat16)
    ray_count = jnp.sum(counts, axis=3)
    pix_count = jnp.sum(counts, axis=2)

    pattern = table.reshape(KINDS, TILE, TILE)
    pattern_wide = pattern.astype(jnp.float32)
    hi = lax.Precision.HIGHEST
    ray_weight = jnp.einsum("gkv,ki->gvi", ray_count, jnp.sum(pattern_wide, axis=2), precision=hi)
    pixel_weight = jnp.einsum("gku,kj->uj", pix_count, jnp.sum(pattern_wide, axis=1), precision=hi)
    ray_weight = jnp.tile(ray_weight, (1, 1, per_dev))
    pixel_weight = jnp.tile(pixel_weight, (1, per_dev))

    cur = current.reshape(pix_total, per_dev, TILE)
    meas = measured.reshape(n_ang, ray_total, per_dev, TILE)
    rw = ray_weight.reshape(n_ang, ray_total, per_dev, TILE)
    pw = pixel_weight.reshape(pix_total, per_dev, TILE)
    scaled = meas
    for iteration in range(ITERS):
        low = cur.astype(jnp.bfloat16)
        gathered = jnp.einsum("gkvu,usj->gkvsj", count_low, low, preferred_element_type=jnp.float32)
        proj = sum(
            jnp.einsum("gkvsj,kij->gvsi", part, pattern, preferred_element_type=jnp.float32)
            for part in split3(gathered)
        )
        scaled = (meas - proj) / rw
        scaled_low = scaled.astype(jnp.bfloat16)
        spread = jnp.einsum("gvsi,kij->gkvsj", scaled_low, pattern, preferred_element_type=jnp.float32)
        update = sum(
            jnp.einsum("gkvu,gkvsj->usj", count_low, part, preferred_element_type=jnp.float32)
            for part in split3(spread)
        )
        cur = cur + update / pw

    vol_back = cur.reshape(n_pix, tiles_dev, width)
    vol_back = jnp.broadcast_to(vol_back[:, None], (n_pix, n_ang, tiles_dev, width))
    res_back = scaled.reshape(n_ang, n_pix, rays_dev, width).transpose(1, 0, 2, 3)
    back = jnp.concatenate([vol_back, res_back], axis=2).reshape(n_grp, tiles_dev + rays_dev, width)
    got_back = lax.all_to_all(back, ("pix", "ang"), 0, 0, tiled=False)
    vol_out = got_back[:, :tiles_dev].transpose(1, 0, 2).reshape(tiles_dev, slices * TILE)
    res_out = got_back[:, tiles_dev:].transpose(1, 0, 2).reshape(1, rays_dev, slices * TILE)
    return (vol_out, res_out)


def solution(mesh):
    n_pix = mesh.shape["pix"]
    n_ang = mesh.shape["ang"]

    def body(volume, sinogram, table, blk_ray, blk_pix):
        if (volume.shape[1] // TILE) % (n_pix * n_ang) == 0:
            return per_device_split(volume, sinogram, table, blk_ray, blk_pix, n_pix, n_ang)
        return per_device_base(volume, sinogram, table, blk_ray, blk_pix)

    return jax.shard_map(
        body,
        mesh=mesh,
        in_specs=(
            P(("parts", "pix"), "sl"),
            P(("parts", "ang"), "pix", "sl"),
            P(),
            P("ang", "pix", None),
            P("ang", "pix", None),
        ),
        out_specs=(P(("parts", "pix"), "sl"), P(("parts", "ang"), "pix", "sl")),
        check_vma=False,
    )
```

```python
import jax
import jax.numpy as jnp
from jax import lax
from jax.sharding import PartitionSpec as P

TILE = 64
KINDS = 32
ITERS = 2
PER_KIND = 44


def project_local(low_volume, pattern, pixel_list, ray_list, ray_total):
    tiles_dev = low_volume.shape[0]
    slices = low_volume.shape[1] // TILE
    low_tiles = low_volume.reshape(tiles_dev, slices, TILE)
    kinds_each = KINDS // 4

    def project_one_group(running, inputs):
        patterns, pix_ids, ray_ids = inputs
        picked = jnp.take(low_tiles, pix_ids, axis=0).reshape(kinds_each, PER_KIND, slices, TILE)
        images = jnp.einsum("kbsj,kij->kbsi", picked, patterns, preferred_element_type=jnp.float32)
        images = images.reshape(kinds_each * PER_KIND, slices * TILE)
        return (running + jax.ops.segment_sum(images, ray_ids, ray_total), None)

    inputs = (
        pattern.reshape(4, kinds_each, TILE, TILE),
        pixel_list.reshape(4, -1),
        ray_list.reshape(4, -1),
    )
    initial = jnp.zeros((ray_total, slices * TILE), jnp.float32)
    running, unused = lax.scan(project_one_group, initial, inputs)
    return running


def back_local(row_table, pattern, pixel_list, row_index, tiles_dev):
    slices = row_table.shape[1] // TILE
    table_tiles = row_table.reshape(row_table.shape[0], slices, TILE)
    kinds_each = KINDS // 4

    def back_one_group(running, inputs):
        patterns, pix_ids, row_ids = inputs
        picked = jnp.take(table_tiles, row_ids, axis=0).reshape(kinds_each, PER_KIND, slices, TILE)
        images = jnp.einsum("kbsi,kij->kbsj", picked, patterns, preferred_element_type=jnp.float32)
        images = images.reshape(kinds_each * PER_KIND, slices * TILE)
        return (running + jax.ops.segment_sum(images, pix_ids, tiles_dev), None)

    inputs = (
        pattern.reshape(4, kinds_each, TILE, TILE),
        pixel_list.reshape(4, -1),
        row_index.reshape(4, -1),
    )
    initial = jnp.zeros((tiles_dev, slices * TILE), jnp.float32)
    running, unused = lax.scan(back_one_group, initial, inputs)
    return running


def per_device_base(volume, sinogram, table, blk_ray, blk_pix):
    pix_count = lax.axis_size("pix")
    tiles_dev = volume.shape[0]
    row_width = volume.shape[1]
    slices = row_width // TILE
    rays_dev = sinogram.shape[1]
    ray_total = rays_dev * pix_count
    ray_list = blk_ray.reshape(-1)
    pixel_list = blk_pix.reshape(-1)
    pattern = table.reshape(KINDS, TILE, TILE)
    pattern_wide = table.astype(jnp.float32).reshape(KINDS, TILE, TILE)
    row_block = jnp.broadcast_to(
        jnp.sum(pattern_wide, axis=2)[:, None, :], (KINDS, PER_KIND, TILE)
    ).reshape(-1, TILE)
    col_block = jnp.broadcast_to(
        jnp.sum(pattern_wide, axis=1)[:, None, :], (KINDS, PER_KIND, TILE)
    ).reshape(-1, TILE)
    row_part = jax.ops.segment_sum(row_block, ray_list, ray_total)
    col_part = jax.ops.segment_sum(col_block, pixel_list, tiles_dev)
    measured = sinogram[0]
    col_weight = lax.psum(col_part, "ang")
    current = volume
    scaled = measured
    for iteration in range(ITERS):
        low_volume = current.astype(jnp.bfloat16)
        partial_rows = project_local(low_volume, pattern, pixel_list, ray_list, ray_total)
        if iteration == 0:
            summed, row_weight = (
                lax.psum_scatter(partial_rows, "pix", scatter_dimension=0, tiled=True),
                lax.psum_scatter(row_part, "pix", scatter_dimension=0, tiled=True),
            )
        else:
            summed = lax.psum_scatter(partial_rows, "pix", scatter_dimension=0, tiled=True)
        scaled = (measured - summed) / jnp.tile(row_weight, (1, slices))
        scaled_low = scaled.astype(jnp.bfloat16)
        row_table = lax.all_gather(scaled_low, "pix", axis=0, tiled=True)
        back_sum = back_local(row_table, pattern, pixel_list, ray_list, tiles_dev)
        summed_update = lax.psum(back_sum, "ang")
        current = current + summed_update / jnp.tile(col_weight, (1, slices))
    return (current, scaled[None])


def split3(x):
    hi = lax.reduce_precision(x, exponent_bits=8, mantissa_bits=7)
    rest = x - hi
    mid = lax.reduce_precision(rest, exponent_bits=8, mantissa_bits=7)
    low = rest - mid
    return (hi.astype(jnp.bfloat16), mid.astype(jnp.bfloat16), low.astype(jnp.bfloat16))


def per_device_split(volume, sinogram, table, blk_ray, blk_pix, n_pix, n_ang):
    n_grp = n_pix * n_ang
    tiles_dev = volume.shape[0]
    slices = volume.shape[1] // TILE
    per_dev = slices // n_grp
    rays_dev = sinogram.shape[1]
    nbd = blk_ray.shape[-1]
    ray_total = rays_dev * n_pix
    pix_total = tiles_dev * n_pix
    width = per_dev * TILE

    vol_send = volume.reshape(tiles_dev, n_grp, width).transpose(1, 0, 2)
    sino_send = sinogram[0].reshape(rays_dev, n_grp, width).transpose(1, 0, 2)
    lists = jnp.stack([blk_ray.reshape(-1), blk_pix.reshape(-1)]).astype(jnp.float32)
    list_rows = (2 * nbd + width - 1) // width
    lists = jnp.pad(lists.reshape(-1), (0, list_rows * width - 2 * nbd)).reshape(list_rows, width)
    list_send = jnp.broadcast_to(lists[None], (n_grp, list_rows, width))
    send = jnp.concatenate([vol_send, sino_send, list_send], axis=1)
    recv = lax.all_to_all(send, ("pix", "ang"), 0, 0, tiled=False)
    recv = recv.reshape(n_pix, n_ang, tiles_dev + rays_dev + list_rows, width)

    current = recv[:, 0, :tiles_dev].reshape(pix_total, width)
    measured = recv[:, :, tiles_dev:tiles_dev + rays_dev].transpose(1, 0, 2, 3).reshape(n_ang, ray_total, width)
    got = recv[:, :, tiles_dev + rays_dev:].reshape(n_pix, n_ang, -1)[:, :, :2 * nbd]
    got = got.reshape(n_pix, n_ang, 2, nbd).transpose(2, 1, 0, 3).astype(jnp.int32)
    per_kind = nbd // KINDS
    offsets = (jnp.arange(n_pix, dtype=jnp.int32) * tiles_dev)[None, :, None, None]
    ray_ids = got[0].reshape(n_ang, n_pix, KINDS, per_kind)
    pix_ids = got[1].reshape(n_ang, n_pix, KINDS, per_kind) + offsets
    ray_ids = ray_ids.transpose(0, 2, 1, 3).reshape(n_ang, KINDS, n_pix * per_kind)
    pix_ids = pix_ids.transpose(0, 2, 1, 3).reshape(n_ang, KINDS, n_pix * per_kind)

    one_ray = (ray_ids[..., None] == jnp.arange(ray_total, dtype=jnp.int32)).astype(jnp.bfloat16)
    one_pix = (pix_ids[..., None] == jnp.arange(pix_total, dtype=jnp.int32)).astype(jnp.bfloat16)
    count_low = jnp.einsum(
        "gkbv,gkbu->gkvu", one_ray, one_pix, preferred_element_type=jnp.float32
    ).astype(jnp.bfloat16)
    ray_count = jnp.sum(one_ray.astype(jnp.float32), axis=2)
    pix_count = jnp.sum(one_pix.astype(jnp.float32), axis=2)

    pattern = table.reshape(KINDS, TILE, TILE)
    pattern_wide = pattern.astype(jnp.float32)
    hi = lax.Precision.HIGHEST
    ray_weight = jnp.einsum("gkv,ki->gvi", ray_count, jnp.sum(pattern_wide, axis=2), precision=hi)
    pixel_weight = jnp.einsum("gku,kj->uj", pix_count, jnp.sum(pattern_wide, axis=1), precision=hi)
    ray_weight = jnp.tile(ray_weight, (1, 1, per_dev))
    pixel_weight = jnp.tile(pixel_weight, (1, per_dev))

    cur = current.reshape(pix_total, per_dev, TILE)
    meas = measured.reshape(n_ang, ray_total, per_dev, TILE)
    rw = ray_weight.reshape(n_ang, ray_total, per_dev, TILE)
    pw = pixel_weight.reshape(pix_total, per_dev, TILE)
    scaled = meas
    for iteration in range(ITERS):
        low = cur.astype(jnp.bfloat16)
        gathered = jnp.einsum("gkvu,usj->gkvsj", count_low, low, preferred_element_type=jnp.float32)
        proj = sum(
            jnp.einsum("gkvsj,kij->gvsi", part, pattern, preferred_element_type=jnp.float32)
            for part in split3(gathered)
        )
        scaled = (meas - proj) / rw
        scaled_low = scaled.astype(jnp.bfloat16)
        spread = jnp.einsum("gvsi,kij->gkvsj", scaled_low, pattern, preferred_element_type=jnp.float32)
        update = sum(
            jnp.einsum("gkvu,gkvsj->usj", count_low, part, preferred_element_type=jnp.float32)
            for part in split3(spread)
        )
        cur = cur + update / pw

    vol_back = cur.reshape(n_pix, tiles_dev, width)
    vol_back = jnp.broadcast_to(vol_back[:, None], (n_pix, n_ang, tiles_dev, width))
    res_back = scaled.reshape(n_ang, n_pix, rays_dev, width).transpose(1, 0, 2, 3)
    back = jnp.concatenate([vol_back, res_back], axis=2).reshape(n_grp, tiles_dev + rays_dev, width)
    got_back = lax.all_to_all(back, ("pix", "ang"), 0, 0, tiled=False)
    vol_out = got_back[:, :tiles_dev].transpose(1, 0, 2).reshape(tiles_dev, slices * TILE)
    res_out = got_back[:, tiles_dev:].transpose(1, 0, 2).reshape(1, rays_dev, slices * TILE)
    return (vol_out, res_out)


def solution(mesh):
    n_pix = mesh.shape["pix"]
    n_ang = mesh.shape["ang"]

    def body(volume, sinogram, table, blk_ray, blk_pix):
        if (volume.shape[1] // TILE) % (n_pix * n_ang) == 0:
            return per_device_split(volume, sinogram, table, blk_ray, blk_pix, n_pix, n_ang)
        return per_device_base(volume, sinogram, table, blk_ray, blk_pix)

    return jax.shard_map(
        body,
        mesh=mesh,
        in_specs=(
            P(("parts", "pix"), "sl"),
            P(("parts", "ang"), "pix", "sl"),
            P(),
            P("ang", "pix", None),
            P("ang", "pix", None),
        ),
        out_specs=(P(("parts", "pix"), "sl"), P(("parts", "ang"), "pix", "sl")),
        check_vma=False,
    )
```

```python
import jax
import jax.numpy as jnp
from jax import lax
from jax.sharding import PartitionSpec as P

TILE = 64
KINDS = 32
ITERS = 2
PER_KIND = 44


def project_local(low_volume, pattern, pixel_list, ray_list, ray_total):
    tiles_dev = low_volume.shape[0]
    slices = low_volume.shape[1] // TILE
    low_tiles = low_volume.reshape(tiles_dev, slices, TILE)
    kinds_each = KINDS // 4

    def project_one_group(running, inputs):
        patterns, pix_ids, ray_ids = inputs
        picked = jnp.take(low_tiles, pix_ids, axis=0).reshape(kinds_each, PER_KIND, slices, TILE)
        images = jnp.einsum("kbsj,kij->kbsi", picked, patterns, preferred_element_type=jnp.float32)
        images = images.reshape(kinds_each * PER_KIND, slices * TILE)
        return (running + jax.ops.segment_sum(images, ray_ids, ray_total), None)

    inputs = (
        pattern.reshape(4, kinds_each, TILE, TILE),
        pixel_list.reshape(4, -1),
        ray_list.reshape(4, -1),
    )
    initial = jnp.zeros((ray_total, slices * TILE), jnp.float32)
    running, unused = lax.scan(project_one_group, initial, inputs)
    return running


def back_local(row_table, pattern, pixel_list, row_index, tiles_dev):
    slices = row_table.shape[1] // TILE
    table_tiles = row_table.reshape(row_table.shape[0], slices, TILE)
    kinds_each = KINDS // 4

    def back_one_group(running, inputs):
        patterns, pix_ids, row_ids = inputs
        picked = jnp.take(table_tiles, row_ids, axis=0).reshape(kinds_each, PER_KIND, slices, TILE)
        images = jnp.einsum("kbsi,kij->kbsj", picked, patterns, preferred_element_type=jnp.float32)
        images = images.reshape(kinds_each * PER_KIND, slices * TILE)
        return (running + jax.ops.segment_sum(images, pix_ids, tiles_dev), None)

    inputs = (
        pattern.reshape(4, kinds_each, TILE, TILE),
        pixel_list.reshape(4, -1),
        row_index.reshape(4, -1),
    )
    initial = jnp.zeros((tiles_dev, slices * TILE), jnp.float32)
    running, unused = lax.scan(back_one_group, initial, inputs)
    return running


def per_device_base(volume, sinogram, table, blk_ray, blk_pix):
    pix_count = lax.axis_size("pix")
    tiles_dev = volume.shape[0]
    row_width = volume.shape[1]
    slices = row_width // TILE
    rays_dev = sinogram.shape[1]
    ray_total = rays_dev * pix_count
    ray_list = blk_ray.reshape(-1)
    pixel_list = blk_pix.reshape(-1)
    pattern = table.reshape(KINDS, TILE, TILE)
    pattern_wide = table.astype(jnp.float32).reshape(KINDS, TILE, TILE)
    row_block = jnp.broadcast_to(
        jnp.sum(pattern_wide, axis=2)[:, None, :], (KINDS, PER_KIND, TILE)
    ).reshape(-1, TILE)
    col_block = jnp.broadcast_to(
        jnp.sum(pattern_wide, axis=1)[:, None, :], (KINDS, PER_KIND, TILE)
    ).reshape(-1, TILE)
    row_part = jax.ops.segment_sum(row_block, ray_list, ray_total)
    col_part = jax.ops.segment_sum(col_block, pixel_list, tiles_dev)
    measured = sinogram[0]
    col_weight = lax.psum(col_part, "ang")
    current = volume
    scaled = measured
    for iteration in range(ITERS):
        low_volume = current.astype(jnp.bfloat16)
        partial_rows = project_local(low_volume, pattern, pixel_list, ray_list, ray_total)
        if iteration == 0:
            summed, row_weight = (
                lax.psum_scatter(partial_rows, "pix", scatter_dimension=0, tiled=True),
                lax.psum_scatter(row_part, "pix", scatter_dimension=0, tiled=True),
            )
        else:
            summed = lax.psum_scatter(partial_rows, "pix", scatter_dimension=0, tiled=True)
        scaled = (measured - summed) / jnp.tile(row_weight, (1, slices))
        scaled_low = scaled.astype(jnp.bfloat16)
        row_table = lax.all_gather(scaled_low, "pix", axis=0, tiled=True)
        back_sum = back_local(row_table, pattern, pixel_list, ray_list, tiles_dev)
        summed_update = lax.psum(back_sum, "ang")
        current = current + summed_update / jnp.tile(col_weight, (1, slices))
    return (current, scaled[None])


def split3(x):
    hi = lax.reduce_precision(x, exponent_bits=8, mantissa_bits=7)
    rest = x - hi
    mid = lax.reduce_precision(rest, exponent_bits=8, mantissa_bits=7)
    return jnp.stack([hi, mid, rest - mid]).astype(jnp.bfloat16)


def per_device_split(volume, sinogram, table, blk_ray, blk_pix, n_pix, n_ang):
    n_grp = n_pix * n_ang
    tiles_dev = volume.shape[0]
    slices = volume.shape[1] // TILE
    per_dev = slices // n_grp
    rays_dev = sinogram.shape[1]
    nbd = blk_ray.shape[-1]
    ray_total = rays_dev * n_pix
    pix_total = tiles_dev * n_pix
    width = per_dev * TILE
    per_kind = nbd // KINDS

    lists = jnp.stack([blk_ray.reshape(-1), blk_pix.reshape(-1)]).astype(jnp.float32)
    list_rows = (2 * nbd + width - 1) // width
    lists = jnp.pad(lists.reshape(-1), (0, list_rows * width - 2 * nbd)).reshape(list_rows, 1, width)
    send = jnp.concatenate(
        [
            volume.reshape(tiles_dev, n_grp, width),
            sinogram[0].reshape(rays_dev, n_grp, width),
            jnp.broadcast_to(lists, (list_rows, n_grp, width)),
        ],
        axis=0,
    )
    recv = lax.all_to_all(send, ("pix", "ang"), 1, 1, tiled=False)
    recv = recv.reshape(tiles_dev + rays_dev + list_rows, n_pix, n_ang, width)

    current = recv[:tiles_dev, :, 0].transpose(1, 0, 2).reshape(pix_total, width)
    measured = recv[tiles_dev:tiles_dev + rays_dev].transpose(2, 1, 0, 3).reshape(n_ang * ray_total, width)
    got = recv[tiles_dev + rays_dev:].transpose(2, 1, 0, 3).reshape(n_ang, n_pix, list_rows * width)
    got = got[:, :, :2 * nbd].reshape(n_ang, n_pix, 2, KINDS, per_kind).astype(jnp.int32)
    offsets = (jnp.arange(n_pix, dtype=jnp.int32) * tiles_dev)[None, :, None, None]
    ray_ids = got[:, :, 0].transpose(0, 2, 1, 3).reshape(n_ang, KINDS, n_pix * per_kind)
    pix_ids = (got[:, :, 1] + offsets).transpose(0, 2, 1, 3).reshape(n_ang, KINDS, n_pix * per_kind)

    one_ray = (ray_ids[..., None] == jnp.arange(ray_total, dtype=jnp.int32)).astype(jnp.bfloat16)
    one_pix = (pix_ids[..., None] == jnp.arange(pix_total, dtype=jnp.int32)).astype(jnp.bfloat16)
    count_low = jnp.einsum(
        "gkbv,gkbu->gkvu", one_ray, one_pix, preferred_element_type=jnp.float32
    ).astype(jnp.bfloat16)
    counts = count_low.astype(jnp.float32)
    ray_count = jnp.sum(counts, axis=3)
    pix_count = jnp.sum(counts, axis=2)
    count_rows = count_low.reshape(n_ang * KINDS * ray_total, pix_total)

    pattern = table.reshape(KINDS, TILE, TILE)
    pattern_wide = pattern.astype(jnp.float32)
    hi = lax.Precision.HIGHEST
    ray_weight = jnp.einsum("gkv,ki->gvi", ray_count, jnp.sum(pattern_wide, axis=2), precision=hi)
    pixel_weight = jnp.einsum("gku,kj->uj", pix_count, jnp.sum(pattern_wide, axis=1), precision=hi)
    ray_weight = jnp.tile(ray_weight.reshape(n_ang * ray_total, TILE), (1, per_dev))
    pixel_weight = jnp.tile(pixel_weight, (1, per_dev))
    pattern_kj_i = pattern.transpose(0, 2, 1).reshape(KINDS * TILE, TILE)
    pattern_i_kj = pattern.transpose(1, 0, 2).reshape(TILE, KINDS * TILE)

    rows = n_ang * ray_total * per_dev
    cur = current.reshape(pix_total, per_dev, TILE)
    meas = measured.reshape(rows, TILE)
    rw = ray_weight.reshape(rows, TILE)
    pw = pixel_weight.reshape(pix_total, per_dev, TILE)
    scaled = meas
    for iteration in range(ITERS):
        low = cur.astype(jnp.bfloat16).reshape(pix_total, width)
        gathered = jnp.dot(count_rows, low, preferred_element_type=jnp.float32)
        gathered = gathered.reshape(n_ang, KINDS, ray_total, per_dev, TILE)
        parts = split3(gathered).transpose(0, 1, 3, 4, 2, 5).reshape(3 * rows, KINDS * TILE)
        proj = jnp.dot(parts, pattern_kj_i, preferred_element_type=jnp.float32)
        proj = jnp.sum(proj.reshape(3, rows, TILE), axis=0)
        scaled = (meas - proj) / rw
        scaled_low = scaled.astype(jnp.bfloat16)
        spread = jnp.dot(scaled_low, pattern_i_kj, preferred_element_type=jnp.float32)
        spread = spread.reshape(n_ang, ray_total, per_dev, KINDS, TILE)
        parts = split3(spread).transpose(1, 4, 2, 3, 0, 5).reshape(n_ang * KINDS * ray_total, per_dev * 3 * TILE)
        update = lax.dot_general(count_rows, parts, (((0,), (0,)), ((), ())), preferred_element_type=jnp.float32)
        update = jnp.sum(update.reshape(pix_total, per_dev, 3, TILE), axis=2)
        cur = cur + update / pw

    vol_back = jnp.broadcast_to(cur.reshape(n_pix, 1, tiles_dev, width), (n_pix, n_ang, tiles_dev, width))
    res_back = scaled.reshape(n_ang, n_pix, rays_dev, width).transpose(1, 0, 2, 3)
    back = jnp.concatenate([vol_back, res_back], axis=2).reshape(n_grp, tiles_dev + rays_dev, width)
    back = back.transpose(1, 0, 2)
    got_back = lax.all_to_all(back, ("pix", "ang"), 1, 1, tiled=False)
    vol_out = got_back[:tiles_dev].reshape(tiles_dev, slices * TILE)
    res_out = got_back[tiles_dev:].reshape(1, rays_dev, slices * TILE)
    return (vol_out, res_out)


def solution(mesh):
    n_pix = mesh.shape["pix"]
    n_ang = mesh.shape["ang"]

    def body(volume, sinogram, table, blk_ray, blk_pix):
        if (volume.shape[1] // TILE) % (n_pix * n_ang) == 0:
            return per_device_split(volume, sinogram, table, blk_ray, blk_pix, n_pix, n_ang)
        return per_device_base(volume, sinogram, table, blk_ray, blk_pix)

    return jax.shard_map(
        body,
        mesh=mesh,
        in_specs=(
            P(("parts", "pix"), "sl"),
            P(("parts", "ang"), "pix", "sl"),
            P(),
            P("ang", "pix", None),
            P("ang", "pix", None),
        ),
        out_specs=(P(("parts", "pix"), "sl"), P(("parts", "ang"), "pix", "sl")),
        check_vma=False,
    )
```

```python
import jax
import jax.numpy as jnp
from jax import lax
from jax.sharding import PartitionSpec as P

TILE = 64
KINDS = 32
ITERS = 2
PER_KIND = 44


def project_local(low_volume, pattern, pixel_list, ray_list, ray_total):
    tiles_dev = low_volume.shape[0]
    slices = low_volume.shape[1] // TILE
    low_tiles = low_volume.reshape(tiles_dev, slices, TILE)
    kinds_each = KINDS // 4

    def project_one_group(running, inputs):
        patterns, pix_ids, ray_ids = inputs
        picked = jnp.take(low_tiles, pix_ids, axis=0).reshape(kinds_each, PER_KIND, slices, TILE)
        images = jnp.einsum("kbsj,kij->kbsi", picked, patterns, preferred_element_type=jnp.float32)
        images = images.reshape(kinds_each * PER_KIND, slices * TILE)
        return (running + jax.ops.segment_sum(images, ray_ids, ray_total), None)

    inputs = (
        pattern.reshape(4, kinds_each, TILE, TILE),
        pixel_list.reshape(4, -1),
        ray_list.reshape(4, -1),
    )
    initial = jnp.zeros((ray_total, slices * TILE), jnp.float32)
    running, unused = lax.scan(project_one_group, initial, inputs)
    return running


def back_local(row_table, pattern, pixel_list, row_index, tiles_dev):
    slices = row_table.shape[1] // TILE
    table_tiles = row_table.reshape(row_table.shape[0], slices, TILE)
    kinds_each = KINDS // 4

    def back_one_group(running, inputs):
        patterns, pix_ids, row_ids = inputs
        picked = jnp.take(table_tiles, row_ids, axis=0).reshape(kinds_each, PER_KIND, slices, TILE)
        images = jnp.einsum("kbsi,kij->kbsj", picked, patterns, preferred_element_type=jnp.float32)
        images = images.reshape(kinds_each * PER_KIND, slices * TILE)
        return (running + jax.ops.segment_sum(images, pix_ids, tiles_dev), None)

    inputs = (
        pattern.reshape(4, kinds_each, TILE, TILE),
        pixel_list.reshape(4, -1),
        row_index.reshape(4, -1),
    )
    initial = jnp.zeros((tiles_dev, slices * TILE), jnp.float32)
    running, unused = lax.scan(back_one_group, initial, inputs)
    return running


def per_device_base(volume, sinogram, table, blk_ray, blk_pix):
    pix_count = lax.axis_size("pix")
    tiles_dev = volume.shape[0]
    row_width = volume.shape[1]
    slices = row_width // TILE
    rays_dev = sinogram.shape[1]
    ray_total = rays_dev * pix_count
    ray_list = blk_ray.reshape(-1)
    pixel_list = blk_pix.reshape(-1)
    pattern = table.reshape(KINDS, TILE, TILE)
    pattern_wide = table.astype(jnp.float32).reshape(KINDS, TILE, TILE)
    row_block = jnp.broadcast_to(
        jnp.sum(pattern_wide, axis=2)[:, None, :], (KINDS, PER_KIND, TILE)
    ).reshape(-1, TILE)
    col_block = jnp.broadcast_to(
        jnp.sum(pattern_wide, axis=1)[:, None, :], (KINDS, PER_KIND, TILE)
    ).reshape(-1, TILE)
    row_part = jax.ops.segment_sum(row_block, ray_list, ray_total)
    col_part = jax.ops.segment_sum(col_block, pixel_list, tiles_dev)
    measured = sinogram[0]
    col_weight = lax.psum(col_part, "ang")
    current = volume
    scaled = measured
    for iteration in range(ITERS):
        low_volume = current.astype(jnp.bfloat16)
        partial_rows = project_local(low_volume, pattern, pixel_list, ray_list, ray_total)
        if iteration == 0:
            summed, row_weight = (
                lax.psum_scatter(partial_rows, "pix", scatter_dimension=0, tiled=True),
                lax.psum_scatter(row_part, "pix", scatter_dimension=0, tiled=True),
            )
        else:
            summed = lax.psum_scatter(partial_rows, "pix", scatter_dimension=0, tiled=True)
        scaled = (measured - summed) / jnp.tile(row_weight, (1, slices))
        scaled_low = scaled.astype(jnp.bfloat16)
        row_table = lax.all_gather(scaled_low, "pix", axis=0, tiled=True)
        back_sum = back_local(row_table, pattern, pixel_list, ray_list, tiles_dev)
        summed_update = lax.psum(back_sum, "ang")
        current = current + summed_update / jnp.tile(col_weight, (1, slices))
    return (current, scaled[None])


def split2(x):
    hi = lax.reduce_precision(x, exponent_bits=8, mantissa_bits=7)
    return (hi.astype(jnp.bfloat16), (x - hi).astype(jnp.bfloat16))


def per_device_split(volume, sinogram, table, blk_ray, blk_pix, n_pix, n_ang):
    n_grp = n_pix * n_ang
    tiles_dev = volume.shape[0]
    slices = volume.shape[1] // TILE
    per_dev = slices // n_grp
    rays_dev = sinogram.shape[1]
    nbd = blk_ray.shape[-1]
    ray_total = rays_dev * n_pix
    pix_total = tiles_dev * n_pix
    width = per_dev * TILE

    vol_send = volume.reshape(tiles_dev, n_grp, width).transpose(1, 0, 2)
    sino_send = sinogram[0].reshape(rays_dev, n_grp, width).transpose(1, 0, 2)
    lists = jnp.stack([blk_ray.reshape(-1), blk_pix.reshape(-1)]).astype(jnp.float32)
    list_rows = (2 * nbd + width - 1) // width
    lists = jnp.pad(lists.reshape(-1), (0, list_rows * width - 2 * nbd)).reshape(list_rows, width)
    list_send = jnp.broadcast_to(lists[None], (n_grp, list_rows, width))
    send = jnp.concatenate([vol_send, sino_send, list_send], axis=1)
    recv = lax.all_to_all(send, ("pix", "ang"), 0, 0, tiled=False)
    recv = recv.reshape(n_pix, n_ang, tiles_dev + rays_dev + list_rows, width)

    current = recv[:, 0, :tiles_dev].reshape(pix_total, width)
    measured = recv[:, :, tiles_dev:tiles_dev + rays_dev].transpose(1, 0, 2, 3).reshape(n_ang, ray_total, width)
    got = recv[:, :, tiles_dev + rays_dev:].reshape(n_pix, n_ang, -1)[:, :, :2 * nbd]
    got = got.reshape(n_pix, n_ang, 2, nbd).transpose(2, 1, 0, 3).astype(jnp.int32)
    per_kind = nbd // KINDS
    offsets = (jnp.arange(n_pix, dtype=jnp.int32) * tiles_dev)[None, :, None, None]
    ray_ids = got[0].reshape(n_ang, n_pix, KINDS, per_kind)
    pix_ids = got[1].reshape(n_ang, n_pix, KINDS, per_kind) + offsets
    ray_ids = ray_ids.transpose(0, 2, 1, 3).reshape(n_ang, KINDS, n_pix * per_kind)
    pix_ids = pix_ids.transpose(0, 2, 1, 3).reshape(n_ang, KINDS, n_pix * per_kind)

    one_ray = (ray_ids[..., None] == jnp.arange(ray_total, dtype=jnp.int32)).astype(jnp.bfloat16)
    one_pix = (pix_ids[..., None] == jnp.arange(pix_total, dtype=jnp.int32)).astype(jnp.bfloat16)
    count_low = jnp.einsum(
        "gkbv,gkbu->gkvu", one_ray, one_pix, preferred_element_type=jnp.float32
    ).astype(jnp.bfloat16)
    count_low = lax.optimization_barrier(count_low)
    ray_count = jnp.sum(count_low.astype(jnp.float32), axis=3)
    pix_count = jnp.sum(count_low.astype(jnp.float32), axis=2)

    pattern = table.reshape(KINDS, TILE, TILE)
    pattern_wide = pattern.astype(jnp.float32)
    hi = lax.Precision.HIGHEST
    ray_weight = jnp.einsum("gkv,ki->gvi", ray_count, jnp.sum(pattern_wide, axis=2), precision=hi)
    pixel_weight = jnp.einsum("gku,kj->uj", pix_count, jnp.sum(pattern_wide, axis=1), precision=hi)
    ray_weight = jnp.tile(ray_weight, (1, 1, per_dev))
    pixel_weight = jnp.tile(pixel_weight, (1, per_dev))

    cur = current.reshape(pix_total, per_dev, TILE)
    meas = measured.reshape(n_ang, ray_total, per_dev, TILE)
    rw = ray_weight.reshape(n_ang, ray_total, per_dev, TILE)
    pw = pixel_weight.reshape(pix_total, per_dev, TILE)
    scaled = meas
    for iteration in range(ITERS):
        low = cur.astype(jnp.bfloat16)
        gathered = jnp.einsum("gkvu,usj->gkvsj", count_low, low, preferred_element_type=jnp.float32)
        proj = sum(
            jnp.einsum("gkvsj,kij->gvsi", part, pattern, preferred_element_type=jnp.float32)
            for part in split2(gathered)
        )
        scaled = (meas - proj) / rw
        scaled_low = scaled.astype(jnp.bfloat16)
        spread = jnp.einsum("gvsi,kij->gkvsj", scaled_low, pattern, preferred_element_type=jnp.float32)
        update = sum(
            jnp.einsum("gkvu,gkvsj->usj", count_low, part, preferred_element_type=jnp.float32)
            for part in split2(spread)
        )
        cur = cur + update / pw

    vol_back = cur.reshape(n_pix, tiles_dev, width)
    vol_back = jnp.broadcast_to(vol_back[:, None], (n_pix, n_ang, tiles_dev, width))
    res_back = scaled.reshape(n_ang, n_pix, rays_dev, width).transpose(1, 0, 2, 3)
    back = jnp.concatenate([vol_back, res_back], axis=2).reshape(n_grp, tiles_dev + rays_dev, width)
    got_back = lax.all_to_all(back, ("pix", "ang"), 0, 0, tiled=False)
    vol_out = got_back[:, :tiles_dev].transpose(1, 0, 2).reshape(tiles_dev, slices * TILE)
    res_out = got_back[:, tiles_dev:].transpose(1, 0, 2).reshape(1, rays_dev, slices * TILE)
    return (vol_out, res_out)


def solution(mesh):
    n_pix = mesh.shape["pix"]
    n_ang = mesh.shape["ang"]

    def body(volume, sinogram, table, blk_ray, blk_pix):
        if (volume.shape[1] // TILE) % (n_pix * n_ang) == 0:
            return per_device_split(volume, sinogram, table, blk_ray, blk_pix, n_pix, n_ang)
        return per_device_base(volume, sinogram, table, blk_ray, blk_pix)

    return jax.shard_map(
        body,
        mesh=mesh,
        in_specs=(
            P(("parts", "pix"), "sl"),
            P(("parts", "ang"), "pix", "sl"),
            P(),
            P("ang", "pix", None),
            P("ang", "pix", None),
        ),
        out_specs=(P(("parts", "pix"), "sl"), P(("parts", "ang"), "pix", "sl")),
        check_vma=False,
    )
```

```python
import jax
import jax.numpy as jnp
from jax import lax
from jax.sharding import PartitionSpec as P

TILE = 64
KINDS = 32
ITERS = 2
PER_KIND = 44


def project_local(low_volume, pattern, pixel_list, ray_list, ray_total):
    tiles_dev = low_volume.shape[0]
    slices = low_volume.shape[1] // TILE
    low_tiles = low_volume.reshape(tiles_dev, slices, TILE)
    kinds_each = KINDS // 4

    def project_one_group(running, inputs):
        patterns, pix_ids, ray_ids = inputs
        picked = jnp.take(low_tiles, pix_ids, axis=0).reshape(kinds_each, PER_KIND, slices, TILE)
        images = jnp.einsum("kbsj,kij->kbsi", picked, patterns, preferred_element_type=jnp.float32)
        images = images.reshape(kinds_each * PER_KIND, slices * TILE)
        return (running + jax.ops.segment_sum(images, ray_ids, ray_total), None)

    inputs = (
        pattern.reshape(4, kinds_each, TILE, TILE),
        pixel_list.reshape(4, -1),
        ray_list.reshape(4, -1),
    )
    initial = jnp.zeros((ray_total, slices * TILE), jnp.float32)
    running, unused = lax.scan(project_one_group, initial, inputs)
    return running


def back_local(row_table, pattern, pixel_list, row_index, tiles_dev):
    slices = row_table.shape[1] // TILE
    table_tiles = row_table.reshape(row_table.shape[0], slices, TILE)
    kinds_each = KINDS // 4

    def back_one_group(running, inputs):
        patterns, pix_ids, row_ids = inputs
        picked = jnp.take(table_tiles, row_ids, axis=0).reshape(kinds_each, PER_KIND, slices, TILE)
        images = jnp.einsum("kbsi,kij->kbsj", picked, patterns, preferred_element_type=jnp.float32)
        images = images.reshape(kinds_each * PER_KIND, slices * TILE)
        return (running + jax.ops.segment_sum(images, pix_ids, tiles_dev), None)

    inputs = (
        pattern.reshape(4, kinds_each, TILE, TILE),
        pixel_list.reshape(4, -1),
        row_index.reshape(4, -1),
    )
    initial = jnp.zeros((tiles_dev, slices * TILE), jnp.float32)
    running, unused = lax.scan(back_one_group, initial, inputs)
    return running


def per_device_base(volume, sinogram, table, blk_ray, blk_pix):
    pix_count = lax.axis_size("pix")
    tiles_dev = volume.shape[0]
    row_width = volume.shape[1]
    slices = row_width // TILE
    rays_dev = sinogram.shape[1]
    ray_total = rays_dev * pix_count
    ray_list = blk_ray.reshape(-1)
    pixel_list = blk_pix.reshape(-1)
    pattern = table.reshape(KINDS, TILE, TILE)
    pattern_wide = table.astype(jnp.float32).reshape(KINDS, TILE, TILE)
    row_block = jnp.broadcast_to(
        jnp.sum(pattern_wide, axis=2)[:, None, :], (KINDS, PER_KIND, TILE)
    ).reshape(-1, TILE)
    col_block = jnp.broadcast_to(
        jnp.sum(pattern_wide, axis=1)[:, None, :], (KINDS, PER_KIND, TILE)
    ).reshape(-1, TILE)
    row_part = jax.ops.segment_sum(row_block, ray_list, ray_total)
    col_part = jax.ops.segment_sum(col_block, pixel_list, tiles_dev)
    measured = sinogram[0]
    col_weight = lax.psum(col_part, "ang")
    current = volume
    scaled = measured
    for iteration in range(ITERS):
        low_volume = current.astype(jnp.bfloat16)
        partial_rows = project_local(low_volume, pattern, pixel_list, ray_list, ray_total)
        if iteration == 0:
            summed, row_weight = (
                lax.psum_scatter(partial_rows, "pix", scatter_dimension=0, tiled=True),
                lax.psum_scatter(row_part, "pix", scatter_dimension=0, tiled=True),
            )
        else:
            summed = lax.psum_scatter(partial_rows, "pix", scatter_dimension=0, tiled=True)
        scaled = (measured - summed) / jnp.tile(row_weight, (1, slices))
        scaled_low = scaled.astype(jnp.bfloat16)
        row_table = lax.all_gather(scaled_low, "pix", axis=0, tiled=True)
        back_sum = back_local(row_table, pattern, pixel_list, ray_list, tiles_dev)
        summed_update = lax.psum(back_sum, "ang")
        current = current + summed_update / jnp.tile(col_weight, (1, slices))
    return (current, scaled[None])


def split2(x):
    hi = lax.reduce_precision(x, exponent_bits=8, mantissa_bits=7)
    return (hi.astype(jnp.bfloat16), (x - hi).astype(jnp.bfloat16))


def per_device_split(volume, sinogram, table, blk_ray, blk_pix, n_pix, n_ang):
    n_grp = n_pix * n_ang
    tiles_dev = volume.shape[0]
    slices = volume.shape[1] // TILE
    per_dev = slices // n_grp
    rays_dev = sinogram.shape[1]
    nbd = blk_ray.shape[-1]
    ray_total = rays_dev * n_pix
    pix_total = tiles_dev * n_pix
    width = per_dev * TILE

    vol_send = volume.reshape(tiles_dev, n_grp, width).transpose(1, 0, 2)
    sino_send = sinogram[0].reshape(rays_dev, n_grp, width).transpose(1, 0, 2)
    lists = jnp.stack([blk_ray.reshape(-1), blk_pix.reshape(-1)]).astype(jnp.float32)
    list_rows = (2 * nbd + width - 1) // width
    lists = jnp.pad(lists.reshape(-1), (0, list_rows * width - 2 * nbd)).reshape(list_rows, width)
    list_send = jnp.broadcast_to(lists[None], (n_grp, list_rows, width))
    send = jnp.concatenate([vol_send, sino_send, list_send], axis=1)
    recv = lax.all_to_all(send, ("pix", "ang"), 0, 0, tiled=False)
    recv = recv.reshape(n_pix, n_ang, tiles_dev + rays_dev + list_rows, width)

    current = recv[:, 0, :tiles_dev].reshape(pix_total, width)
    measured = recv[:, :, tiles_dev:tiles_dev + rays_dev].transpose(1, 0, 2, 3).reshape(n_ang, ray_total, width)
    got = recv[:, :, tiles_dev + rays_dev:].reshape(n_pix, n_ang, -1)[:, :, :2 * nbd]
    got = got.reshape(n_pix, n_ang, 2, nbd).transpose(2, 1, 0, 3).astype(jnp.int32)
    per_kind = nbd // KINDS
    offsets = (jnp.arange(n_pix, dtype=jnp.int32) * tiles_dev)[None, :, None, None]
    ray_ids = got[0].reshape(n_ang, n_pix, KINDS, per_kind)
    pix_ids = got[1].reshape(n_ang, n_pix, KINDS, per_kind) + offsets
    ray_ids = ray_ids.transpose(0, 2, 1, 3).reshape(n_ang, KINDS, n_pix * per_kind)
    pix_ids = pix_ids.transpose(0, 2, 1, 3).reshape(n_ang, KINDS, n_pix * per_kind)

    one_ray = (ray_ids[..., None] == jnp.arange(ray_total, dtype=jnp.int32)).astype(jnp.bfloat16)
    one_pix = (pix_ids[..., None] == jnp.arange(pix_total, dtype=jnp.int32)).astype(jnp.bfloat16)
    count_low = jnp.einsum(
        "gkbv,gkbu->gkvu", one_ray, one_pix, preferred_element_type=jnp.float32
    ).astype(jnp.bfloat16)
    count_low = lax.optimization_barrier(count_low)
    counts = count_low.astype(jnp.float32)
    ray_count = jnp.sum(counts, axis=3)
    pix_count = jnp.sum(counts, axis=2)

    pattern = table.reshape(KINDS, TILE, TILE)
    pattern_wide = pattern.astype(jnp.float32)
    hi = lax.Precision.HIGHEST
    ray_weight = jnp.einsum("gkv,ki->gvi", ray_count, jnp.sum(pattern_wide, axis=2), precision=hi)
    pixel_weight = jnp.einsum("gku,kj->uj", pix_count, jnp.sum(pattern_wide, axis=1), precision=hi)
    ray_weight = jnp.tile(ray_weight, (1, 1, per_dev))
    pixel_weight = jnp.tile(pixel_weight, (1, per_dev))

    cur = current.reshape(pix_total, per_dev, TILE)
    meas = measured.reshape(n_ang, ray_total, per_dev, TILE)
    rw = ray_weight.reshape(n_ang, ray_total, per_dev, TILE)
    pw = pixel_weight.reshape(pix_total, per_dev, TILE)
    scaled = meas
    for iteration in range(ITERS):
        low = cur.astype(jnp.bfloat16)
        gathered = jnp.einsum("gkvu,usj->gkvsj", count_low, low, preferred_element_type=jnp.float32)
        proj = jnp.einsum(
            "gkvsj,kij->gvsi", gathered, pattern_wide, precision=lax.Precision.HIGH,
            preferred_element_type=jnp.float32,
        )
        scaled = (meas - proj) / rw
        scaled_low = scaled.astype(jnp.bfloat16)
        spread = jnp.einsum("gvsi,kij->gkvsj", scaled_low, pattern, preferred_element_type=jnp.float32)
        update = jnp.einsum(
            "gkvu,gkvsj->usj", counts, spread, precision=lax.Precision.HIGH,
            preferred_element_type=jnp.float32,
        )
        cur = cur + update / pw

    vol_back = cur.reshape(n_pix, tiles_dev, width)
    vol_back = jnp.broadcast_to(vol_back[:, None], (n_pix, n_ang, tiles_dev, width))
    res_back = scaled.reshape(n_ang, n_pix, rays_dev, width).transpose(1, 0, 2, 3)
    back = jnp.concatenate([vol_back, res_back], axis=2).reshape(n_grp, tiles_dev + rays_dev, width)
    got_back = lax.all_to_all(back, ("pix", "ang"), 0, 0, tiled=False)
    vol_out = got_back[:, :tiles_dev].transpose(1, 0, 2).reshape(tiles_dev, slices * TILE)
    res_out = got_back[:, tiles_dev:].transpose(1, 0, 2).reshape(1, rays_dev, slices * TILE)
    return (vol_out, res_out)


def solution(mesh):
    n_pix = mesh.shape["pix"]
    n_ang = mesh.shape["ang"]

    def body(volume, sinogram, table, blk_ray, blk_pix):
        if (volume.shape[1] // TILE) % (n_pix * n_ang) == 0:
            return per_device_split(volume, sinogram, table, blk_ray, blk_pix, n_pix, n_ang)
        return per_device_base(volume, sinogram, table, blk_ray, blk_pix)

    return jax.shard_map(
        body,
        mesh=mesh,
        in_specs=(
            P(("parts", "pix"), "sl"),
            P(("parts", "ang"), "pix", "sl"),
            P(),
            P("ang", "pix", None),
            P("ang", "pix", None),
        ),
        out_specs=(P(("parts", "pix"), "sl"), P(("parts", "ang"), "pix", "sl")),
        check_vma=False,
    )
```

```python
import jax
import jax.numpy as jnp
from jax import lax
from jax.sharding import PartitionSpec as P
from jax.experimental import pallas as pl
from jax.experimental.pallas import tpu as pltpu

TILE = 64
KINDS = 32
ITERS = 2
PER_KIND = 44


def project_local(low_volume, pattern, pixel_list, ray_list, ray_total):
    tiles_dev = low_volume.shape[0]
    slices = low_volume.shape[1] // TILE
    low_tiles = low_volume.reshape(tiles_dev, slices, TILE)
    kinds_each = KINDS // 4

    def project_one_group(running, inputs):
        patterns, pix_ids, ray_ids = inputs
        picked = jnp.take(low_tiles, pix_ids, axis=0).reshape(kinds_each, PER_KIND, slices, TILE)
        images = jnp.einsum("kbsj,kij->kbsi", picked, patterns, preferred_element_type=jnp.float32)
        images = images.reshape(kinds_each * PER_KIND, slices * TILE)
        return (running + jax.ops.segment_sum(images, ray_ids, ray_total), None)

    inputs = (
        pattern.reshape(4, kinds_each, TILE, TILE),
        pixel_list.reshape(4, -1),
        ray_list.reshape(4, -1),
    )
    initial = jnp.zeros((ray_total, slices * TILE), jnp.float32)
    running, unused = lax.scan(project_one_group, initial, inputs)
    return running


def back_local(row_table, pattern, pixel_list, row_index, tiles_dev):
    slices = row_table.shape[1] // TILE
    table_tiles = row_table.reshape(row_table.shape[0], slices, TILE)
    kinds_each = KINDS // 4

    def back_one_group(running, inputs):
        patterns, pix_ids, row_ids = inputs
        picked = jnp.take(table_tiles, row_ids, axis=0).reshape(kinds_each, PER_KIND, slices, TILE)
        images = jnp.einsum("kbsi,kij->kbsj", picked, patterns, preferred_element_type=jnp.float32)
        images = images.reshape(kinds_each * PER_KIND, slices * TILE)
        return (running + jax.ops.segment_sum(images, pix_ids, tiles_dev), None)

    inputs = (
        pattern.reshape(4, kinds_each, TILE, TILE),
        pixel_list.reshape(4, -1),
        row_index.reshape(4, -1),
    )
    initial = jnp.zeros((tiles_dev, slices * TILE), jnp.float32)
    running, unused = lax.scan(back_one_group, initial, inputs)
    return running


def per_device_base(volume, sinogram, table, blk_ray, blk_pix):
    pix_count = lax.axis_size("pix")
    tiles_dev = volume.shape[0]
    row_width = volume.shape[1]
    slices = row_width // TILE
    rays_dev = sinogram.shape[1]
    ray_total = rays_dev * pix_count
    ray_list = blk_ray.reshape(-1)
    pixel_list = blk_pix.reshape(-1)
    pattern = table.reshape(KINDS, TILE, TILE)
    pattern_wide = table.astype(jnp.float32).reshape(KINDS, TILE, TILE)
    row_block = jnp.broadcast_to(
        jnp.sum(pattern_wide, axis=2)[:, None, :], (KINDS, PER_KIND, TILE)
    ).reshape(-1, TILE)
    col_block = jnp.broadcast_to(
        jnp.sum(pattern_wide, axis=1)[:, None, :], (KINDS, PER_KIND, TILE)
    ).reshape(-1, TILE)
    row_part = jax.ops.segment_sum(row_block, ray_list, ray_total)
    col_part = jax.ops.segment_sum(col_block, pixel_list, tiles_dev)
    measured = sinogram[0]
    col_weight = lax.psum(col_part, "ang")
    current = volume
    scaled = measured
    for iteration in range(ITERS):
        low_volume = current.astype(jnp.bfloat16)
        partial_rows = project_local(low_volume, pattern, pixel_list, ray_list, ray_total)
        if iteration == 0:
            summed, row_weight = (
                lax.psum_scatter(partial_rows, "pix", scatter_dimension=0, tiled=True),
                lax.psum_scatter(row_part, "pix", scatter_dimension=0, tiled=True),
            )
        else:
            summed = lax.psum_scatter(partial_rows, "pix", scatter_dimension=0, tiled=True)
        scaled = (measured - summed) / jnp.tile(row_weight, (1, slices))
        scaled_low = scaled.astype(jnp.bfloat16)
        row_table = lax.all_gather(scaled_low, "pix", axis=0, tiled=True)
        back_sum = back_local(row_table, pattern, pixel_list, ray_list, tiles_dev)
        summed_update = lax.psum(back_sum, "ang")
        current = current + summed_update / jnp.tile(col_weight, (1, slices))
    return (current, scaled[None])


def pack_kernel(vol_ref, sino_ref, list_ref, out_ref):
    n_dest = out_ref.shape[0]
    tiles = vol_ref.shape[0]
    rays = sino_ref.shape[0]
    width = out_ref.shape[2]
    lists = list_ref[...]
    for q in range(n_dest):
        out_ref[q, 0:tiles, :] = vol_ref[:, q * width:(q + 1) * width]
        out_ref[q, tiles:tiles + rays, :] = sino_ref[:, q * width:(q + 1) * width]
        out_ref[q, tiles + rays:, :] = lists


def pack_send(volume, sino, lists, n_dest):
    tiles, total = volume.shape
    rows = tiles + sino.shape[0] + lists.shape[0]
    return pl.pallas_call(
        pack_kernel,
        out_shape=jax.ShapeDtypeStruct((n_dest, rows, total // n_dest), jnp.float32),
    )(volume, sino, lists)


def split2(x):
    hi = lax.reduce_precision(x, exponent_bits=8, mantissa_bits=7)
    return (hi.astype(jnp.bfloat16), (x - hi).astype(jnp.bfloat16))


def per_device_split(volume, sinogram, table, blk_ray, blk_pix, n_pix, n_ang):
    n_grp = n_pix * n_ang
    tiles_dev = volume.shape[0]
    slices = volume.shape[1] // TILE
    per_dev = slices // n_grp
    rays_dev = sinogram.shape[1]
    nbd = blk_ray.shape[-1]
    ray_total = rays_dev * n_pix
    pix_total = tiles_dev * n_pix
    width = per_dev * TILE

    lists = jnp.stack([blk_ray.reshape(-1), blk_pix.reshape(-1)]).astype(jnp.float32)
    list_rows = (2 * nbd + width - 1) // width
    lists = jnp.pad(lists.reshape(-1), (0, list_rows * width - 2 * nbd)).reshape(list_rows, width)
    send = pack_send(volume, sinogram[0], lists, n_grp)
    recv = lax.all_to_all(send, ("pix", "ang"), 0, 0, tiled=False)
    recv = recv.reshape(n_pix, n_ang, tiles_dev + rays_dev + list_rows, width)

    current = recv[:, 0, :tiles_dev].reshape(pix_total, width)
    measured = recv[:, :, tiles_dev:tiles_dev + rays_dev].transpose(1, 0, 2, 3).reshape(n_ang, ray_total, width)
    got = recv[:, :, tiles_dev + rays_dev:].reshape(n_pix, n_ang, -1)[:, :, :2 * nbd]
    got = got.reshape(n_pix, n_ang, 2, nbd).transpose(2, 1, 0, 3).astype(jnp.int32)
    per_kind = nbd // KINDS
    offsets = (jnp.arange(n_pix, dtype=jnp.int32) * tiles_dev)[None, :, None, None]
    ray_ids = got[0].reshape(n_ang, n_pix, KINDS, per_kind)
    pix_ids = got[1].reshape(n_ang, n_pix, KINDS, per_kind) + offsets
    ray_ids = ray_ids.transpose(0, 2, 1, 3).reshape(n_ang, KINDS, n_pix * per_kind)
    pix_ids = pix_ids.transpose(0, 2, 1, 3).reshape(n_ang, KINDS, n_pix * per_kind)

    one_ray = (ray_ids[..., None] == jnp.arange(ray_total, dtype=jnp.int32)).astype(jnp.bfloat16)
    one_pix = (pix_ids[..., None] == jnp.arange(pix_total, dtype=jnp.int32)).astype(jnp.bfloat16)
    count_low = jnp.einsum(
        "gkbv,gkbu->gkvu", one_ray, one_pix, preferred_element_type=jnp.float32
    ).astype(jnp.bfloat16)
    count_low = lax.optimization_barrier(count_low)
    counts = count_low.astype(jnp.float32)
    ray_count = jnp.sum(counts, axis=3)
    pix_count = jnp.sum(counts, axis=2)

    pattern = table.reshape(KINDS, TILE, TILE)
    pattern_wide = pattern.astype(jnp.float32)
    hi = lax.Precision.HIGHEST
    ray_weight = jnp.einsum("gkv,ki->gvi", ray_count, jnp.sum(pattern_wide, axis=2), precision=hi)
    pixel_weight = jnp.einsum("gku,kj->uj", pix_count, jnp.sum(pattern_wide, axis=1), precision=hi)
    ray_weight = jnp.tile(ray_weight, (1, 1, per_dev))
    pixel_weight = jnp.tile(pixel_weight, (1, per_dev))

    cur = current.reshape(pix_total, per_dev, TILE)
    meas = measured.reshape(n_ang, ray_total, per_dev, TILE)
    rw = ray_weight.reshape(n_ang, ray_total, per_dev, TILE)
    pw = pixel_weight.reshape(pix_total, per_dev, TILE)
    scaled = meas
    for iteration in range(ITERS):
        low = cur.astype(jnp.bfloat16)
        gathered = jnp.einsum("gkvu,usj->gkvsj", count_low, low, preferred_element_type=jnp.float32)
        proj = jnp.einsum(
            "gkvsj,kij->gvsi", gathered, pattern_wide, precision=lax.Precision.HIGH,
            preferred_element_type=jnp.float32,
        )
        scaled = (meas - proj) / rw
        scaled_low = scaled.astype(jnp.bfloat16)
        spread = jnp.einsum("gvsi,kij->gkvsj", scaled_low, pattern, preferred_element_type=jnp.float32)
        update = jnp.einsum(
            "gkvu,gkvsj->usj", counts, spread, precision=lax.Precision.HIGH,
            preferred_element_type=jnp.float32,
        )
        cur = cur + update / pw

    vol_back = cur.reshape(n_pix, tiles_dev, width)
    vol_back = jnp.broadcast_to(vol_back[:, None], (n_pix, n_ang, tiles_dev, width))
    res_back = scaled.reshape(n_ang, n_pix, rays_dev, width).transpose(1, 0, 2, 3)
    back = jnp.concatenate([vol_back, res_back], axis=2).reshape(n_grp, tiles_dev + rays_dev, width)
    got_back = lax.all_to_all(back, ("pix", "ang"), 0, 0, tiled=False)
    vol_out = got_back[:, :tiles_dev].transpose(1, 0, 2).reshape(tiles_dev, slices * TILE)
    res_out = got_back[:, tiles_dev:].transpose(1, 0, 2).reshape(1, rays_dev, slices * TILE)
    return (vol_out, res_out)


def solution(mesh):
    n_pix = mesh.shape["pix"]
    n_ang = mesh.shape["ang"]

    def body(volume, sinogram, table, blk_ray, blk_pix):
        if (volume.shape[1] // TILE) % (n_pix * n_ang) == 0:
            return per_device_split(volume, sinogram, table, blk_ray, blk_pix, n_pix, n_ang)
        return per_device_base(volume, sinogram, table, blk_ray, blk_pix)

    return jax.shard_map(
        body,
        mesh=mesh,
        in_specs=(
            P(("parts", "pix"), "sl"),
            P(("parts", "ang"), "pix", "sl"),
            P(),
            P("ang", "pix", None),
            P("ang", "pix", None),
        ),
        out_specs=(P(("parts", "pix"), "sl"), P(("parts", "ang"), "pix", "sl")),
        check_vma=False,
    )
```

```python
import jax
import jax.numpy as jnp
from jax import lax
from jax.sharding import PartitionSpec as P

TILE = 64
KINDS = 32
ITERS = 2
PER_KIND = 44


def project_local(low_volume, pattern, pixel_list, ray_list, ray_total):
    tiles_dev = low_volume.shape[0]
    slices = low_volume.shape[1] // TILE
    low_tiles = low_volume.reshape(tiles_dev, slices, TILE)
    kinds_each = KINDS // 4

    def project_one_group(running, inputs):
        patterns, pix_ids, ray_ids = inputs
        picked = jnp.take(low_tiles, pix_ids, axis=0).reshape(kinds_each, PER_KIND, slices, TILE)
        images = jnp.einsum("kbsj,kij->kbsi", picked, patterns, preferred_element_type=jnp.float32)
        images = images.reshape(kinds_each * PER_KIND, slices * TILE)
        return (running + jax.ops.segment_sum(images, ray_ids, ray_total), None)

    inputs = (
        pattern.reshape(4, kinds_each, TILE, TILE),
        pixel_list.reshape(4, -1),
        ray_list.reshape(4, -1),
    )
    initial = jnp.zeros((ray_total, slices * TILE), jnp.float32)
    running, unused = lax.scan(project_one_group, initial, inputs)
    return running


def back_local(row_table, pattern, pixel_list, row_index, tiles_dev):
    slices = row_table.shape[1] // TILE
    table_tiles = row_table.reshape(row_table.shape[0], slices, TILE)
    kinds_each = KINDS // 4

    def back_one_group(running, inputs):
        patterns, pix_ids, row_ids = inputs
        picked = jnp.take(table_tiles, row_ids, axis=0).reshape(kinds_each, PER_KIND, slices, TILE)
        images = jnp.einsum("kbsi,kij->kbsj", picked, patterns, preferred_element_type=jnp.float32)
        images = images.reshape(kinds_each * PER_KIND, slices * TILE)
        return (running + jax.ops.segment_sum(images, pix_ids, tiles_dev), None)

    inputs = (
        pattern.reshape(4, kinds_each, TILE, TILE),
        pixel_list.reshape(4, -1),
        row_index.reshape(4, -1),
    )
    initial = jnp.zeros((tiles_dev, slices * TILE), jnp.float32)
    running, unused = lax.scan(back_one_group, initial, inputs)
    return running


def per_device_base(volume, sinogram, table, blk_ray, blk_pix):
    pix_count = lax.axis_size("pix")
    tiles_dev = volume.shape[0]
    row_width = volume.shape[1]
    slices = row_width // TILE
    rays_dev = sinogram.shape[1]
    ray_total = rays_dev * pix_count
    ray_list = blk_ray.reshape(-1)
    pixel_list = blk_pix.reshape(-1)
    pattern = table.reshape(KINDS, TILE, TILE)
    pattern_wide = table.astype(jnp.float32).reshape(KINDS, TILE, TILE)
    row_block = jnp.broadcast_to(
        jnp.sum(pattern_wide, axis=2)[:, None, :], (KINDS, PER_KIND, TILE)
    ).reshape(-1, TILE)
    col_block = jnp.broadcast_to(
        jnp.sum(pattern_wide, axis=1)[:, None, :], (KINDS, PER_KIND, TILE)
    ).reshape(-1, TILE)
    row_part = jax.ops.segment_sum(row_block, ray_list, ray_total)
    col_part = jax.ops.segment_sum(col_block, pixel_list, tiles_dev)
    measured = sinogram[0]
    col_weight = lax.psum(col_part, "ang")
    current = volume
    scaled = measured
    for iteration in range(ITERS):
        low_volume = current.astype(jnp.bfloat16)
        partial_rows = project_local(low_volume, pattern, pixel_list, ray_list, ray_total)
        if iteration == 0:
            summed, row_weight = (
                lax.psum_scatter(partial_rows, "pix", scatter_dimension=0, tiled=True),
                lax.psum_scatter(row_part, "pix", scatter_dimension=0, tiled=True),
            )
        else:
            summed = lax.psum_scatter(partial_rows, "pix", scatter_dimension=0, tiled=True)
        scaled = (measured - summed) / jnp.tile(row_weight, (1, slices))
        scaled_low = scaled.astype(jnp.bfloat16)
        row_table = lax.all_gather(scaled_low, "pix", axis=0, tiled=True)
        back_sum = back_local(row_table, pattern, pixel_list, ray_list, tiles_dev)
        summed_update = lax.psum(back_sum, "ang")
        current = current + summed_update / jnp.tile(col_weight, (1, slices))
    return (current, scaled[None])


def split2(x):
    hi = lax.reduce_precision(x, exponent_bits=8, mantissa_bits=7)
    return (hi.astype(jnp.bfloat16), (x - hi).astype(jnp.bfloat16))


def per_device_split(volume, sinogram, table, blk_ray, blk_pix, n_pix, n_ang):
    n_grp = n_pix * n_ang
    tiles_dev = volume.shape[0]
    slices = volume.shape[1] // TILE
    per_dev = slices // n_grp
    rays_dev = sinogram.shape[1]
    nbd = blk_ray.shape[-1]
    ray_total = rays_dev * n_pix
    pix_total = tiles_dev * n_pix
    width = per_dev * TILE

    lists = jnp.stack([blk_ray.reshape(-1), blk_pix.reshape(-1)])
    list_send = jnp.broadcast_to(lists[None], (n_grp, 2, nbd))
    got = lax.all_to_all(list_send, ("pix", "ang"), 0, 0, tiled=False)
    got = got.reshape(n_pix, n_ang, 2, nbd).transpose(2, 1, 0, 3)

    vol_send = volume.reshape(tiles_dev, n_grp, width).transpose(1, 0, 2)
    sino_send = sinogram[0].reshape(rays_dev, n_grp, width).transpose(1, 0, 2)
    send = jnp.concatenate([vol_send, sino_send], axis=1)
    recv = lax.all_to_all(send, ("pix", "ang"), 0, 0, tiled=False)
    recv = recv.reshape(n_pix, n_ang, tiles_dev + rays_dev, width)

    current = recv[:, 0, :tiles_dev].reshape(pix_total, width)
    measured = recv[:, :, tiles_dev:].transpose(1, 0, 2, 3).reshape(n_ang, ray_total, width)
    per_kind = nbd // KINDS
    offsets = (jnp.arange(n_pix, dtype=jnp.int32) * tiles_dev)[None, :, None, None]
    ray_ids = got[0].reshape(n_ang, n_pix, KINDS, per_kind)
    pix_ids = got[1].reshape(n_ang, n_pix, KINDS, per_kind) + offsets
    ray_ids = ray_ids.transpose(0, 2, 1, 3).reshape(n_ang, KINDS, n_pix * per_kind)
    pix_ids = pix_ids.transpose(0, 2, 1, 3).reshape(n_ang, KINDS, n_pix * per_kind)

    one_ray = (ray_ids[..., None] == jnp.arange(ray_total, dtype=jnp.int32)).astype(jnp.bfloat16)
    one_pix = (pix_ids[..., None] == jnp.arange(pix_total, dtype=jnp.int32)).astype(jnp.bfloat16)
    count_low = jnp.einsum(
        "gkbv,gkbu->gkvu", one_ray, one_pix, preferred_element_type=jnp.float32
    ).astype(jnp.bfloat16)
    count_low = lax.optimization_barrier(count_low)
    counts = count_low.astype(jnp.float32)
    ray_count = jnp.sum(counts, axis=3)
    pix_count = jnp.sum(counts, axis=2)

    pattern = table.reshape(KINDS, TILE, TILE)
    pattern_wide = pattern.astype(jnp.float32)
    hi = lax.Precision.HIGHEST
    ray_weight = jnp.einsum("gkv,ki->gvi", ray_count, jnp.sum(pattern_wide, axis=2), precision=hi)
    pixel_weight = jnp.einsum("gku,kj->uj", pix_count, jnp.sum(pattern_wide, axis=1), precision=hi)
    ray_weight = jnp.tile(ray_weight, (1, 1, per_dev))
    pixel_weight = jnp.tile(pixel_weight, (1, per_dev))

    cur = current.reshape(pix_total, per_dev, TILE)
    meas = measured.reshape(n_ang, ray_total, per_dev, TILE)
    rw = ray_weight.reshape(n_ang, ray_total, per_dev, TILE)
    pw = pixel_weight.reshape(pix_total, per_dev, TILE)
    scaled = meas
    for iteration in range(ITERS):
        low = cur.astype(jnp.bfloat16)
        gathered = jnp.einsum("gkvu,usj->gkvsj", count_low, low, preferred_element_type=jnp.float32)
        proj = jnp.einsum(
            "gkvsj,kij->gvsi", gathered, pattern_wide, precision=lax.Precision.HIGH,
            preferred_element_type=jnp.float32,
        )
        scaled = (meas - proj) / rw
        scaled_low = scaled.astype(jnp.bfloat16)
        spread = jnp.einsum("gvsi,kij->gkvsj", scaled_low, pattern, preferred_element_type=jnp.float32)
        update = jnp.einsum(
            "gkvu,gkvsj->usj", counts, spread, precision=lax.Precision.HIGH,
            preferred_element_type=jnp.float32,
        )
        cur = cur + update / pw

    vol_back = cur.reshape(n_pix, tiles_dev, width)
    vol_back = jnp.broadcast_to(vol_back[:, None], (n_pix, n_ang, tiles_dev, width))
    res_back = scaled.reshape(n_ang, n_pix, rays_dev, width).transpose(1, 0, 2, 3)
    back = jnp.concatenate([vol_back, res_back], axis=2).reshape(n_grp, tiles_dev + rays_dev, width)
    got_back = lax.all_to_all(back, ("pix", "ang"), 0, 0, tiled=False)
    vol_out = got_back[:, :tiles_dev].transpose(1, 0, 2).reshape(tiles_dev, slices * TILE)
    res_out = got_back[:, tiles_dev:].transpose(1, 0, 2).reshape(1, rays_dev, slices * TILE)
    return (vol_out, res_out)


def solution(mesh):
    n_pix = mesh.shape["pix"]
    n_ang = mesh.shape["ang"]

    def body(volume, sinogram, table, blk_ray, blk_pix):
        if (volume.shape[1] // TILE) % (n_pix * n_ang) == 0:
            return per_device_split(volume, sinogram, table, blk_ray, blk_pix, n_pix, n_ang)
        return per_device_base(volume, sinogram, table, blk_ray, blk_pix)

    return jax.shard_map(
        body,
        mesh=mesh,
        in_specs=(
            P(("parts", "pix"), "sl"),
            P(("parts", "ang"), "pix", "sl"),
            P(),
            P("ang", "pix", None),
            P("ang", "pix", None),
        ),
        out_specs=(P(("parts", "pix"), "sl"), P(("parts", "ang"), "pix", "sl")),
        check_vma=False,
    )
```

```python
import jax
import jax.numpy as jnp
from jax import lax
from jax.sharding import PartitionSpec as P

TILE = 64
KINDS = 32
ITERS = 2
PER_KIND = 44


def project_local(low_volume, pattern, pixel_list, ray_list, ray_total):
    tiles_dev = low_volume.shape[0]
    slices = low_volume.shape[1] // TILE
    low_tiles = low_volume.reshape(tiles_dev, slices, TILE)
    kinds_each = KINDS // 4

    def project_one_group(running, inputs):
        patterns, pix_ids, ray_ids = inputs
        picked = jnp.take(low_tiles, pix_ids, axis=0).reshape(kinds_each, PER_KIND, slices, TILE)
        images = jnp.einsum("kbsj,kij->kbsi", picked, patterns, preferred_element_type=jnp.float32)
        images = images.reshape(kinds_each * PER_KIND, slices * TILE)
        return (running + jax.ops.segment_sum(images, ray_ids, ray_total), None)

    inputs = (
        pattern.reshape(4, kinds_each, TILE, TILE),
        pixel_list.reshape(4, -1),
        ray_list.reshape(4, -1),
    )
    initial = jnp.zeros((ray_total, slices * TILE), jnp.float32)
    running, unused = lax.scan(project_one_group, initial, inputs)
    return running


def back_local(row_table, pattern, pixel_list, row_index, tiles_dev):
    slices = row_table.shape[1] // TILE
    table_tiles = row_table.reshape(row_table.shape[0], slices, TILE)
    kinds_each = KINDS // 4

    def back_one_group(running, inputs):
        patterns, pix_ids, row_ids = inputs
        picked = jnp.take(table_tiles, row_ids, axis=0).reshape(kinds_each, PER_KIND, slices, TILE)
        images = jnp.einsum("kbsi,kij->kbsj", picked, patterns, preferred_element_type=jnp.float32)
        images = images.reshape(kinds_each * PER_KIND, slices * TILE)
        return (running + jax.ops.segment_sum(images, pix_ids, tiles_dev), None)

    inputs = (
        pattern.reshape(4, kinds_each, TILE, TILE),
        pixel_list.reshape(4, -1),
        row_index.reshape(4, -1),
    )
    initial = jnp.zeros((tiles_dev, slices * TILE), jnp.float32)
    running, unused = lax.scan(back_one_group, initial, inputs)
    return running


def per_device_base(volume, sinogram, table, blk_ray, blk_pix):
    pix_count = lax.axis_size("pix")
    tiles_dev = volume.shape[0]
    row_width = volume.shape[1]
    slices = row_width // TILE
    rays_dev = sinogram.shape[1]
    ray_total = rays_dev * pix_count
    ray_list = blk_ray.reshape(-1)
    pixel_list = blk_pix.reshape(-1)
    pattern = table.reshape(KINDS, TILE, TILE)
    pattern_wide = table.astype(jnp.float32).reshape(KINDS, TILE, TILE)
    row_block = jnp.broadcast_to(
        jnp.sum(pattern_wide, axis=2)[:, None, :], (KINDS, PER_KIND, TILE)
    ).reshape(-1, TILE)
    col_block = jnp.broadcast_to(
        jnp.sum(pattern_wide, axis=1)[:, None, :], (KINDS, PER_KIND, TILE)
    ).reshape(-1, TILE)
    row_part = jax.ops.segment_sum(row_block, ray_list, ray_total)
    col_part = jax.ops.segment_sum(col_block, pixel_list, tiles_dev)
    measured = sinogram[0]
    col_weight = lax.psum(col_part, "ang")
    current = volume
    scaled = measured
    for iteration in range(ITERS):
        low_volume = current.astype(jnp.bfloat16)
        partial_rows = project_local(low_volume, pattern, pixel_list, ray_list, ray_total)
        if iteration == 0:
            summed, row_weight = (
                lax.psum_scatter(partial_rows, "pix", scatter_dimension=0, tiled=True),
                lax.psum_scatter(row_part, "pix", scatter_dimension=0, tiled=True),
            )
        else:
            summed = lax.psum_scatter(partial_rows, "pix", scatter_dimension=0, tiled=True)
        scaled = (measured - summed) / jnp.tile(row_weight, (1, slices))
        scaled_low = scaled.astype(jnp.bfloat16)
        row_table = lax.all_gather(scaled_low, "pix", axis=0, tiled=True)
        back_sum = back_local(row_table, pattern, pixel_list, ray_list, tiles_dev)
        summed_update = lax.psum(back_sum, "ang")
        current = current + summed_update / jnp.tile(col_weight, (1, slices))
    return (current, scaled[None])


def split2(x):
    hi = lax.reduce_precision(x, exponent_bits=8, mantissa_bits=7)
    return (hi.astype(jnp.bfloat16), (x - hi).astype(jnp.bfloat16))


def per_device_split(volume, sinogram, table, blk_ray, blk_pix, n_pix, n_ang):
    n_grp = n_pix * n_ang
    tiles_dev = volume.shape[0]
    slices = volume.shape[1] // TILE
    per_dev = slices // n_pix
    rays_dev = sinogram.shape[1]
    nbd = blk_ray.shape[-1]
    ray_total = rays_dev * n_pix
    pix_total = tiles_dev * n_pix
    width = per_dev * TILE

    vol_send = volume.reshape(tiles_dev, n_pix, width).transpose(1, 0, 2)
    vol_send = jnp.broadcast_to(vol_send[:, None], (n_pix, n_ang, tiles_dev, width))
    sino_send = sinogram[0].reshape(rays_dev, n_pix, width).transpose(1, 0, 2)
    sino_send = jnp.broadcast_to(sino_send[:, None], (n_pix, n_ang, rays_dev, width))
    lists = jnp.stack([blk_ray.reshape(-1), blk_pix.reshape(-1)]).astype(jnp.float32)
    list_rows = (2 * nbd + width - 1) // width
    lists = jnp.pad(lists.reshape(-1), (0, list_rows * width - 2 * nbd)).reshape(list_rows, width)
    list_send = jnp.broadcast_to(lists, (n_pix, n_ang, list_rows, width))
    send = jnp.concatenate([vol_send, sino_send, list_send], axis=2).reshape(n_grp, -1, width)
    recv = lax.all_to_all(send, ("pix", "ang"), 0, 0, tiled=False)
    recv = recv.reshape(n_pix, n_ang, tiles_dev + rays_dev + list_rows, width)

    current = recv[:, 0, :tiles_dev].reshape(pix_total, width)
    measured = recv[:, :, tiles_dev:tiles_dev + rays_dev].transpose(1, 0, 2, 3).reshape(n_ang, ray_total, width)
    got = recv[:, :, tiles_dev + rays_dev:].reshape(n_pix, n_ang, -1)[:, :, :2 * nbd]
    got = got.reshape(n_pix, n_ang, 2, nbd).transpose(2, 1, 0, 3).astype(jnp.int32)
    per_kind = nbd // KINDS
    offsets = (jnp.arange(n_pix, dtype=jnp.int32) * tiles_dev)[None, :, None, None]
    ray_ids = got[0].reshape(n_ang, n_pix, KINDS, per_kind)
    pix_ids = got[1].reshape(n_ang, n_pix, KINDS, per_kind) + offsets
    ray_ids = ray_ids.transpose(0, 2, 1, 3).reshape(n_ang, KINDS, n_pix * per_kind)
    pix_ids = pix_ids.transpose(0, 2, 1, 3).reshape(n_ang, KINDS, n_pix * per_kind)

    one_ray = (ray_ids[..., None] == jnp.arange(ray_total, dtype=jnp.int32)).astype(jnp.bfloat16)
    one_pix = (pix_ids[..., None] == jnp.arange(pix_total, dtype=jnp.int32)).astype(jnp.bfloat16)
    count_low = jnp.einsum(
        "gkbv,gkbu->gkvu", one_ray, one_pix, preferred_element_type=jnp.float32
    ).astype(jnp.bfloat16)
    count_low = lax.optimization_barrier(count_low)
    counts = count_low.astype(jnp.float32)
    ray_count = jnp.sum(counts, axis=3)
    pix_count = jnp.sum(counts, axis=2)

    pattern = table.reshape(KINDS, TILE, TILE)
    pattern_wide = pattern.astype(jnp.float32)
    hi = lax.Precision.HIGHEST
    ray_weight = jnp.einsum("gkv,ki->gvi", ray_count, jnp.sum(pattern_wide, axis=2), precision=hi)
    pixel_weight = jnp.einsum("gku,kj->uj", pix_count, jnp.sum(pattern_wide, axis=1), precision=hi)
    ray_weight = jnp.tile(ray_weight, (1, 1, per_dev))
    pixel_weight = jnp.tile(pixel_weight, (1, per_dev))

    cur = current.reshape(pix_total, per_dev, TILE)
    meas = measured.reshape(n_ang, ray_total, per_dev, TILE)
    rw = ray_weight.reshape(n_ang, ray_total, per_dev, TILE)
    pw = pixel_weight.reshape(pix_total, per_dev, TILE)
    scaled = meas
    for iteration in range(ITERS):
        low = cur.astype(jnp.bfloat16)
        gathered = jnp.einsum("gkvu,usj->gkvsj", count_low, low, preferred_element_type=jnp.float32)
        proj = jnp.einsum(
            "gkvsj,kij->gvsi", gathered, pattern_wide, precision=lax.Precision.HIGH,
            preferred_element_type=jnp.float32,
        )
        scaled = (meas - proj) / rw
        scaled_low = scaled.astype(jnp.bfloat16)
        spread = jnp.einsum("gvsi,kij->gkvsj", scaled_low, pattern, preferred_element_type=jnp.float32)
        update = jnp.einsum(
            "gkvu,gkvsj->usj", counts, spread, precision=lax.Precision.HIGH,
            preferred_element_type=jnp.float32,
        )
        cur = cur + update / pw

    own_group = lax.axis_index("ang")
    vol_back = cur.reshape(n_pix, tiles_dev, width)
    res_back = lax.dynamic_index_in_dim(scaled, own_group, 0, keepdims=False)
    res_back = res_back.reshape(n_pix, rays_dev, width)
    back = jnp.concatenate([vol_back, res_back], axis=1)
    got_back = lax.all_to_all(back, "pix", 0, 0, tiled=False)
    vol_out = got_back[:, :tiles_dev].transpose(1, 0, 2).reshape(tiles_dev, slices * TILE)
    res_out = got_back[:, tiles_dev:].transpose(1, 0, 2).reshape(1, rays_dev, slices * TILE)
    return (vol_out, res_out)


def solution(mesh):
    n_pix = mesh.shape["pix"]
    n_ang = mesh.shape["ang"]

    def body(volume, sinogram, table, blk_ray, blk_pix):
        if (volume.shape[1] // TILE) % n_pix == 0:
            return per_device_split(volume, sinogram, table, blk_ray, blk_pix, n_pix, n_ang)
        return per_device_base(volume, sinogram, table, blk_ray, blk_pix)

    return jax.shard_map(
        body,
        mesh=mesh,
        in_specs=(
            P(("parts", "pix"), "sl"),
            P(("parts", "ang"), "pix", "sl"),
            P(),
            P("ang", "pix", None),
            P("ang", "pix", None),
        ),
        out_specs=(P(("parts", "pix"), "sl"), P(("parts", "ang"), "pix", "sl")),
        check_vma=False,
    )
```

```python
import jax
import jax.numpy as jnp
from jax import lax
from jax.sharding import PartitionSpec as P

TILE = 64
KINDS = 32
ITERS = 2
PER_KIND = 44


def project_local(low_volume, pattern, pixel_list, ray_list, ray_total):
    tiles_dev = low_volume.shape[0]
    slices = low_volume.shape[1] // TILE
    low_tiles = low_volume.reshape(tiles_dev, slices, TILE)
    kinds_each = KINDS // 4

    def project_one_group(running, inputs):
        patterns, pix_ids, ray_ids = inputs
        picked = jnp.take(low_tiles, pix_ids, axis=0).reshape(kinds_each, PER_KIND, slices, TILE)
        images = jnp.einsum("kbsj,kij->kbsi", picked, patterns, preferred_element_type=jnp.float32)
        images = images.reshape(kinds_each * PER_KIND, slices * TILE)
        return (running + jax.ops.segment_sum(images, ray_ids, ray_total), None)

    inputs = (
        pattern.reshape(4, kinds_each, TILE, TILE),
        pixel_list.reshape(4, -1),
        ray_list.reshape(4, -1),
    )
    initial = jnp.zeros((ray_total, slices * TILE), jnp.float32)
    running, unused = lax.scan(project_one_group, initial, inputs)
    return running


def back_local(row_table, pattern, pixel_list, row_index, tiles_dev):
    slices = row_table.shape[1] // TILE
    table_tiles = row_table.reshape(row_table.shape[0], slices, TILE)
    kinds_each = KINDS // 4

    def back_one_group(running, inputs):
        patterns, pix_ids, row_ids = inputs
        picked = jnp.take(table_tiles, row_ids, axis=0).reshape(kinds_each, PER_KIND, slices, TILE)
        images = jnp.einsum("kbsi,kij->kbsj", picked, patterns, preferred_element_type=jnp.float32)
        images = images.reshape(kinds_each * PER_KIND, slices * TILE)
        return (running + jax.ops.segment_sum(images, pix_ids, tiles_dev), None)

    inputs = (
        pattern.reshape(4, kinds_each, TILE, TILE),
        pixel_list.reshape(4, -1),
        row_index.reshape(4, -1),
    )
    initial = jnp.zeros((tiles_dev, slices * TILE), jnp.float32)
    running, unused = lax.scan(back_one_group, initial, inputs)
    return running


def per_device_base(volume, sinogram, table, blk_ray, blk_pix):
    pix_count = lax.axis_size("pix")
    tiles_dev = volume.shape[0]
    row_width = volume.shape[1]
    slices = row_width // TILE
    rays_dev = sinogram.shape[1]
    ray_total = rays_dev * pix_count
    ray_list = blk_ray.reshape(-1)
    pixel_list = blk_pix.reshape(-1)
    pattern = table.reshape(KINDS, TILE, TILE)
    pattern_wide = table.astype(jnp.float32).reshape(KINDS, TILE, TILE)
    row_block = jnp.broadcast_to(
        jnp.sum(pattern_wide, axis=2)[:, None, :], (KINDS, PER_KIND, TILE)
    ).reshape(-1, TILE)
    col_block = jnp.broadcast_to(
        jnp.sum(pattern_wide, axis=1)[:, None, :], (KINDS, PER_KIND, TILE)
    ).reshape(-1, TILE)
    row_part = jax.ops.segment_sum(row_block, ray_list, ray_total)
    col_part = jax.ops.segment_sum(col_block, pixel_list, tiles_dev)
    measured = sinogram[0]
    col_weight = lax.psum(col_part, "ang")
    current = volume
    scaled = measured
    for iteration in range(ITERS):
        low_volume = current.astype(jnp.bfloat16)
        partial_rows = project_local(low_volume, pattern, pixel_list, ray_list, ray_total)
        if iteration == 0:
            summed, row_weight = (
                lax.psum_scatter(partial_rows, "pix", scatter_dimension=0, tiled=True),
                lax.psum_scatter(row_part, "pix", scatter_dimension=0, tiled=True),
            )
        else:
            summed = lax.psum_scatter(partial_rows, "pix", scatter_dimension=0, tiled=True)
        scaled = (measured - summed) / jnp.tile(row_weight, (1, slices))
        scaled_low = scaled.astype(jnp.bfloat16)
        row_table = lax.all_gather(scaled_low, "pix", axis=0, tiled=True)
        back_sum = back_local(row_table, pattern, pixel_list, ray_list, tiles_dev)
        summed_update = lax.psum(back_sum, "ang")
        current = current + summed_update / jnp.tile(col_weight, (1, slices))
    return (current, scaled[None])


def split2(x):
    hi = lax.reduce_precision(x, exponent_bits=8, mantissa_bits=7)
    return (hi.astype(jnp.bfloat16), (x - hi).astype(jnp.bfloat16))


def per_device_split(volume, sinogram, table, blk_ray, blk_pix, n_pix, n_ang):
    n_grp = n_pix * n_ang
    tiles_dev = volume.shape[0]
    slices = volume.shape[1] // TILE
    per_dev = slices // n_grp
    rays_dev = sinogram.shape[1]
    nbd = blk_ray.shape[-1]
    ray_total = rays_dev * n_pix
    pix_total = tiles_dev * n_pix
    width = per_dev * TILE

    vol_send = volume.reshape(tiles_dev, n_grp, width).transpose(1, 0, 2)
    sino_send = sinogram[0].reshape(rays_dev, n_grp, width).transpose(1, 0, 2)
    lists = jnp.stack([blk_ray.reshape(-1), blk_pix.reshape(-1)]).astype(jnp.float32)
    list_rows = (2 * nbd + width - 1) // width
    lists = jnp.pad(lists.reshape(-1), (0, list_rows * width - 2 * nbd)).reshape(list_rows, width)
    list_send = jnp.broadcast_to(lists[None], (n_grp, list_rows, width))
    send = jnp.concatenate([vol_send, sino_send, list_send], axis=1)
    recv = lax.all_to_all(send, ("pix", "ang"), 0, 0, tiled=False)
    recv = recv.reshape(n_pix, n_ang, tiles_dev + rays_dev + list_rows, width)

    current = recv[:, 0, :tiles_dev].reshape(pix_total, width)
    measured = recv[:, :, tiles_dev:tiles_dev + rays_dev].transpose(1, 0, 2, 3).reshape(n_ang, ray_total, width)
    got = recv[:, :, tiles_dev + rays_dev:].reshape(n_pix, n_ang, -1)[:, :, :2 * nbd]
    got = got.reshape(n_pix, n_ang, 2, nbd).transpose(2, 1, 0, 3).astype(jnp.int32)
    per_kind = nbd // KINDS
    offsets = (jnp.arange(n_pix, dtype=jnp.int32) * tiles_dev)[None, :, None, None]
    ray_ids = got[0].reshape(n_ang, n_pix, KINDS, per_kind)
    pix_ids = got[1].reshape(n_ang, n_pix, KINDS, per_kind) + offsets
    ray_ids = ray_ids.transpose(0, 2, 1, 3).reshape(n_ang, KINDS, n_pix * per_kind)
    pix_ids = pix_ids.transpose(0, 2, 1, 3).reshape(n_ang, KINDS, n_pix * per_kind)

    one_ray = (ray_ids[..., None] == jnp.arange(ray_total, dtype=jnp.int32)).astype(jnp.bfloat16)
    one_pix = (pix_ids[..., None] == jnp.arange(pix_total, dtype=jnp.int32)).astype(jnp.bfloat16)
    count_low = jnp.einsum(
        "gkbv,gkbu->gkvu", one_ray, one_pix, preferred_element_type=jnp.float32
    ).astype(jnp.bfloat16)
    count_low = lax.optimization_barrier(count_low)
    counts = count_low.astype(jnp.float32)
    ray_count = jnp.sum(counts, axis=3)
    pix_count = jnp.sum(counts, axis=2)

    pattern = table.reshape(KINDS, TILE, TILE)
    pattern_wide = pattern.astype(jnp.float32)
    hi = lax.Precision.HIGHEST
    ray_weight = jnp.einsum("gkv,ki->gvi", ray_count, jnp.sum(pattern_wide, axis=2), precision=hi)
    pixel_weight = jnp.einsum("gku,kj->uj", pix_count, jnp.sum(pattern_wide, axis=1), precision=hi)
    ray_weight = jnp.tile(ray_weight, (1, 1, per_dev))
    pixel_weight = jnp.tile(pixel_weight, (1, per_dev))

    cur = current.reshape(pix_total, per_dev, TILE)
    meas = measured.reshape(n_ang, ray_total, per_dev, TILE)
    rw = ray_weight.reshape(n_ang, ray_total, per_dev, TILE)
    pw = pixel_weight.reshape(pix_total, per_dev, TILE)
    scaled = meas
    for iteration in range(ITERS):
        low = cur.astype(jnp.bfloat16)
        gathered = jnp.einsum("gkvu,usj->gkvsj", count_low, low, preferred_element_type=jnp.float32)
        proj = jnp.einsum(
            "gkvsj,kij->gvsi", gathered, pattern_wide, precision=lax.Precision.HIGHEST,
            preferred_element_type=jnp.float32,
        )
        scaled = (meas - proj) / rw
        scaled_low = scaled.astype(jnp.bfloat16)
        spread = jnp.einsum("gvsi,kij->gkvsj", scaled_low, pattern, preferred_element_type=jnp.float32)
        update = jnp.einsum(
            "gkvu,gkvsj->usj", counts, spread, precision=lax.Precision.HIGH,
            preferred_element_type=jnp.float32,
        )
        cur = cur + update / pw

    vol_back = cur.reshape(n_pix, tiles_dev, width)
    vol_back = jnp.broadcast_to(vol_back[:, None], (n_pix, n_ang, tiles_dev, width))
    res_back = scaled.reshape(n_ang, n_pix, rays_dev, width).transpose(1, 0, 2, 3)
    back = jnp.concatenate([vol_back, res_back], axis=2).reshape(n_grp, tiles_dev + rays_dev, width)
    got_back = lax.all_to_all(back, ("pix", "ang"), 0, 0, tiled=False)
    vol_out = got_back[:, :tiles_dev].transpose(1, 0, 2).reshape(tiles_dev, slices * TILE)
    res_out = got_back[:, tiles_dev:].transpose(1, 0, 2).reshape(1, rays_dev, slices * TILE)
    return (vol_out, res_out)


def solution(mesh):
    n_pix = mesh.shape["pix"]
    n_ang = mesh.shape["ang"]

    def body(volume, sinogram, table, blk_ray, blk_pix):
        if (volume.shape[1] // TILE) % (n_pix * n_ang) == 0:
            return per_device_split(volume, sinogram, table, blk_ray, blk_pix, n_pix, n_ang)
        return per_device_base(volume, sinogram, table, blk_ray, blk_pix)

    return jax.shard_map(
        body,
        mesh=mesh,
        in_specs=(
            P(("parts", "pix"), "sl"),
            P(("parts", "ang"), "pix", "sl"),
            P(),
            P("ang", "pix", None),
            P("ang", "pix", None),
        ),
        out_specs=(P(("parts", "pix"), "sl"), P(("parts", "ang"), "pix", "sl")),
        check_vma=False,
    )
```

```python
import jax
import jax.numpy as jnp
from jax import lax
from jax.sharding import PartitionSpec as P

TILE = 64
KINDS = 32
ITERS = 2
PER_KIND = 44


def project_local(low_volume, pattern, pixel_list, ray_list, ray_total):
    tiles_dev = low_volume.shape[0]
    slices = low_volume.shape[1] // TILE
    low_tiles = low_volume.reshape(tiles_dev, slices, TILE)
    kinds_each = KINDS // 4

    def project_one_group(running, inputs):
        patterns, pix_ids, ray_ids = inputs
        picked = jnp.take(low_tiles, pix_ids, axis=0).reshape(kinds_each, PER_KIND, slices, TILE)
        images = jnp.einsum("kbsj,kij->kbsi", picked, patterns, preferred_element_type=jnp.float32)
        images = images.reshape(kinds_each * PER_KIND, slices * TILE)
        return (running + jax.ops.segment_sum(images, ray_ids, ray_total), None)

    inputs = (
        pattern.reshape(4, kinds_each, TILE, TILE),
        pixel_list.reshape(4, -1),
        ray_list.reshape(4, -1),
    )
    initial = jnp.zeros((ray_total, slices * TILE), jnp.float32)
    running, unused = lax.scan(project_one_group, initial, inputs)
    return running


def back_local(row_table, pattern, pixel_list, row_index, tiles_dev):
    slices = row_table.shape[1] // TILE
    table_tiles = row_table.reshape(row_table.shape[0], slices, TILE)
    kinds_each = KINDS // 4

    def back_one_group(running, inputs):
        patterns, pix_ids, row_ids = inputs
        picked = jnp.take(table_tiles, row_ids, axis=0).reshape(kinds_each, PER_KIND, slices, TILE)
        images = jnp.einsum("kbsi,kij->kbsj", picked, patterns, preferred_element_type=jnp.float32)
        images = images.reshape(kinds_each * PER_KIND, slices * TILE)
        return (running + jax.ops.segment_sum(images, pix_ids, tiles_dev), None)

    inputs = (
        pattern.reshape(4, kinds_each, TILE, TILE),
        pixel_list.reshape(4, -1),
        row_index.reshape(4, -1),
    )
    initial = jnp.zeros((tiles_dev, slices * TILE), jnp.float32)
    running, unused = lax.scan(back_one_group, initial, inputs)
    return running


def per_device_base(volume, sinogram, table, blk_ray, blk_pix):
    pix_count = lax.axis_size("pix")
    tiles_dev = volume.shape[0]
    row_width = volume.shape[1]
    slices = row_width // TILE
    rays_dev = sinogram.shape[1]
    ray_total = rays_dev * pix_count
    ray_list = blk_ray.reshape(-1)
    pixel_list = blk_pix.reshape(-1)
    pattern = table.reshape(KINDS, TILE, TILE)
    pattern_wide = table.astype(jnp.float32).reshape(KINDS, TILE, TILE)
    row_block = jnp.broadcast_to(
        jnp.sum(pattern_wide, axis=2)[:, None, :], (KINDS, PER_KIND, TILE)
    ).reshape(-1, TILE)
    col_block = jnp.broadcast_to(
        jnp.sum(pattern_wide, axis=1)[:, None, :], (KINDS, PER_KIND, TILE)
    ).reshape(-1, TILE)
    row_part = jax.ops.segment_sum(row_block, ray_list, ray_total)
    col_part = jax.ops.segment_sum(col_block, pixel_list, tiles_dev)
    measured = sinogram[0]
    col_weight = lax.psum(col_part, "ang")
    current = volume
    scaled = measured
    for iteration in range(ITERS):
        low_volume = current.astype(jnp.bfloat16)
        partial_rows = project_local(low_volume, pattern, pixel_list, ray_list, ray_total)
        if iteration == 0:
            summed, row_weight = (
                lax.psum_scatter(partial_rows, "pix", scatter_dimension=0, tiled=True),
                lax.psum_scatter(row_part, "pix", scatter_dimension=0, tiled=True),
            )
        else:
            summed = lax.psum_scatter(partial_rows, "pix", scatter_dimension=0, tiled=True)
        scaled = (measured - summed) / jnp.tile(row_weight, (1, slices))
        scaled_low = scaled.astype(jnp.bfloat16)
        row_table = lax.all_gather(scaled_low, "pix", axis=0, tiled=True)
        back_sum = back_local(row_table, pattern, pixel_list, ray_list, tiles_dev)
        summed_update = lax.psum(back_sum, "ang")
        current = current + summed_update / jnp.tile(col_weight, (1, slices))
    return (current, scaled[None])


def split2(x):
    hi = lax.reduce_precision(x, exponent_bits=8, mantissa_bits=7)
    return (hi.astype(jnp.bfloat16), (x - hi).astype(jnp.bfloat16))


def per_device_split(volume, sinogram, table, blk_ray, blk_pix, n_pix, n_ang):
    n_grp = n_pix * n_ang
    tiles_dev = volume.shape[0]
    slices = volume.shape[1] // TILE
    per_dev = slices // n_grp
    rays_dev = sinogram.shape[1]
    nbd = blk_ray.shape[-1]
    ray_total = rays_dev * n_pix
    pix_total = tiles_dev * n_pix
    width = per_dev * TILE

    vol_send = volume.reshape(tiles_dev, n_grp, width).transpose(1, 0, 2)
    sino_send = sinogram[0].reshape(rays_dev, n_grp, width).transpose(1, 0, 2)
    cells = (blk_ray.reshape(-1) * tiles_dev + blk_pix.reshape(-1)).astype(jnp.float32)
    list_rows = (nbd + width - 1) // width
    lists = jnp.pad(cells, (0, list_rows * width - nbd)).reshape(list_rows, width)
    list_send = jnp.broadcast_to(lists[None], (n_grp, list_rows, width))
    send = jnp.concatenate([vol_send, sino_send, list_send], axis=1)
    recv = lax.all_to_all(send, ("pix", "ang"), 0, 0, tiled=False)
    recv = recv.reshape(n_pix, n_ang, tiles_dev + rays_dev + list_rows, width)

    current = recv[:, 0, :tiles_dev].reshape(pix_total, width)
    measured = recv[:, :, tiles_dev:tiles_dev + rays_dev].transpose(1, 0, 2, 3).reshape(n_ang, ray_total, width)
    cells = recv[:, :, tiles_dev + rays_dev:].reshape(n_pix, n_ang, -1)[:, :, :nbd]
    cells = cells.transpose(1, 0, 2).astype(jnp.int32)
    got = jnp.stack([cells // tiles_dev, cells % tiles_dev])
    per_kind = nbd // KINDS
    offsets = (jnp.arange(n_pix, dtype=jnp.int32) * tiles_dev)[None, :, None, None]
    ray_ids = got[0].reshape(n_ang, n_pix, KINDS, per_kind)
    pix_ids = got[1].reshape(n_ang, n_pix, KINDS, per_kind) + offsets
    ray_ids = ray_ids.transpose(0, 2, 1, 3).reshape(n_ang, KINDS, n_pix * per_kind)
    pix_ids = pix_ids.transpose(0, 2, 1, 3).reshape(n_ang, KINDS, n_pix * per_kind)

    one_ray = (ray_ids[..., None] == jnp.arange(ray_total, dtype=jnp.int32)).astype(jnp.bfloat16)
    one_pix = (pix_ids[..., None] == jnp.arange(pix_total, dtype=jnp.int32)).astype(jnp.bfloat16)
    count_low = jnp.einsum(
        "gkbv,gkbu->gkvu", one_ray, one_pix, preferred_element_type=jnp.float32
    ).astype(jnp.bfloat16)
    count_low = lax.optimization_barrier(count_low)
    counts = count_low.astype(jnp.float32)
    ray_count = jnp.sum(counts, axis=3)
    pix_count = jnp.sum(counts, axis=2)

    pattern = table.reshape(KINDS, TILE, TILE)
    pattern_wide = pattern.astype(jnp.float32)
    hi = lax.Precision.HIGHEST
    ray_weight = jnp.einsum("gkv,ki->gvi", ray_count, jnp.sum(pattern_wide, axis=2), precision=hi)
    pixel_weight = jnp.einsum("gku,kj->uj", pix_count, jnp.sum(pattern_wide, axis=1), precision=hi)
    ray_weight = jnp.tile(ray_weight, (1, 1, per_dev))
    pixel_weight = jnp.tile(pixel_weight, (1, per_dev))

    cur = current.reshape(pix_total, per_dev, TILE)
    meas = measured.reshape(n_ang, ray_total, per_dev, TILE)
    rw = ray_weight.reshape(n_ang, ray_total, per_dev, TILE)
    pw = pixel_weight.reshape(pix_total, per_dev, TILE)
    scaled = meas
    for iteration in range(ITERS):
        low = cur.astype(jnp.bfloat16)
        gathered = jnp.einsum("gkvu,usj->gkvsj", count_low, low, preferred_element_type=jnp.float32)
        proj = jnp.einsum(
            "gkvsj,kij->gvsi", gathered, pattern_wide, precision=lax.Precision.HIGHEST,
            preferred_element_type=jnp.float32,
        )
        scaled = (meas - proj) / rw
        scaled_low = scaled.astype(jnp.bfloat16)
        spread = jnp.einsum("gvsi,kij->gkvsj", scaled_low, pattern, preferred_element_type=jnp.float32)
        update = jnp.einsum(
            "gkvu,gkvsj->usj", counts, spread, precision=lax.Precision.HIGH,
            preferred_element_type=jnp.float32,
        )
        cur = cur + update / pw

    vol_back = cur.reshape(n_pix, tiles_dev, width)
    vol_back = jnp.broadcast_to(vol_back[:, None], (n_pix, n_ang, tiles_dev, width))
    res_back = scaled.reshape(n_ang, n_pix, rays_dev, width).transpose(1, 0, 2, 3)
    back = jnp.concatenate([vol_back, res_back], axis=2).reshape(n_grp, tiles_dev + rays_dev, width)
    got_back = lax.all_to_all(back, ("pix", "ang"), 0, 0, tiled=False)
    vol_out = got_back[:, :tiles_dev].transpose(1, 0, 2).reshape(tiles_dev, slices * TILE)
    res_out = got_back[:, tiles_dev:].transpose(1, 0, 2).reshape(1, rays_dev, slices * TILE)
    return (vol_out, res_out)


def solution(mesh):
    n_pix = mesh.shape["pix"]
    n_ang = mesh.shape["ang"]

    def body(volume, sinogram, table, blk_ray, blk_pix):
        if (volume.shape[1] // TILE) % (n_pix * n_ang) == 0:
            return per_device_split(volume, sinogram, table, blk_ray, blk_pix, n_pix, n_ang)
        return per_device_base(volume, sinogram, table, blk_ray, blk_pix)

    return jax.shard_map(
        body,
        mesh=mesh,
        in_specs=(
            P(("parts", "pix"), "sl"),
            P(("parts", "ang"), "pix", "sl"),
            P(),
            P("ang", "pix", None),
            P("ang", "pix", None),
        ),
        out_specs=(P(("parts", "pix"), "sl"), P(("parts", "ang"), "pix", "sl")),
        check_vma=False,
    )
```

```python
import jax
import jax.numpy as jnp
from jax import lax
from jax.sharding import PartitionSpec as P

TILE = 64
KINDS = 32
ITERS = 2
PER_KIND = 44


def project_local(low_volume, pattern, pixel_list, ray_list, ray_total):
    tiles_dev = low_volume.shape[0]
    slices = low_volume.shape[1] // TILE
    low_tiles = low_volume.reshape(tiles_dev, slices, TILE)
    kinds_each = KINDS // 4

    def project_one_group(running, inputs):
        patterns, pix_ids, ray_ids = inputs
        picked = jnp.take(low_tiles, pix_ids, axis=0).reshape(kinds_each, PER_KIND, slices, TILE)
        images = jnp.einsum("kbsj,kij->kbsi", picked, patterns, preferred_element_type=jnp.float32)
        images = images.reshape(kinds_each * PER_KIND, slices * TILE)
        return (running + jax.ops.segment_sum(images, ray_ids, ray_total), None)

    inputs = (
        pattern.reshape(4, kinds_each, TILE, TILE),
        pixel_list.reshape(4, -1),
        ray_list.reshape(4, -1),
    )
    initial = jnp.zeros((ray_total, slices * TILE), jnp.float32)
    running, unused = lax.scan(project_one_group, initial, inputs)
    return running


def back_local(row_table, pattern, pixel_list, row_index, tiles_dev):
    slices = row_table.shape[1] // TILE
    table_tiles = row_table.reshape(row_table.shape[0], slices, TILE)
    kinds_each = KINDS // 4

    def back_one_group(running, inputs):
        patterns, pix_ids, row_ids = inputs
        picked = jnp.take(table_tiles, row_ids, axis=0).reshape(kinds_each, PER_KIND, slices, TILE)
        images = jnp.einsum("kbsi,kij->kbsj", picked, patterns, preferred_element_type=jnp.float32)
        images = images.reshape(kinds_each * PER_KIND, slices * TILE)
        return (running + jax.ops.segment_sum(images, pix_ids, tiles_dev), None)

    inputs = (
        pattern.reshape(4, kinds_each, TILE, TILE),
        pixel_list.reshape(4, -1),
        row_index.reshape(4, -1),
    )
    initial = jnp.zeros((tiles_dev, slices * TILE), jnp.float32)
    running, unused = lax.scan(back_one_group, initial, inputs)
    return running


def per_device_base(volume, sinogram, table, blk_ray, blk_pix):
    pix_count = lax.axis_size("pix")
    tiles_dev = volume.shape[0]
    row_width = volume.shape[1]
    slices = row_width // TILE
    rays_dev = sinogram.shape[1]
    ray_total = rays_dev * pix_count
    ray_list = blk_ray.reshape(-1)
    pixel_list = blk_pix.reshape(-1)
    pattern = table.reshape(KINDS, TILE, TILE)
    pattern_wide = table.astype(jnp.float32).reshape(KINDS, TILE, TILE)
    row_block = jnp.broadcast_to(
        jnp.sum(pattern_wide, axis=2)[:, None, :], (KINDS, PER_KIND, TILE)
    ).reshape(-1, TILE)
    col_block = jnp.broadcast_to(
        jnp.sum(pattern_wide, axis=1)[:, None, :], (KINDS, PER_KIND, TILE)
    ).reshape(-1, TILE)
    row_part = jax.ops.segment_sum(row_block, ray_list, ray_total)
    col_part = jax.ops.segment_sum(col_block, pixel_list, tiles_dev)
    measured = sinogram[0]
    col_weight = lax.psum(col_part, "ang")
    current = volume
    scaled = measured
    for iteration in range(ITERS):
        low_volume = current.astype(jnp.bfloat16)
        partial_rows = project_local(low_volume, pattern, pixel_list, ray_list, ray_total)
        if iteration == 0:
            summed, row_weight = (
                lax.psum_scatter(partial_rows, "pix", scatter_dimension=0, tiled=True),
                lax.psum_scatter(row_part, "pix", scatter_dimension=0, tiled=True),
            )
        else:
            summed = lax.psum_scatter(partial_rows, "pix", scatter_dimension=0, tiled=True)
        scaled = (measured - summed) / jnp.tile(row_weight, (1, slices))
        scaled_low = scaled.astype(jnp.bfloat16)
        row_table = lax.all_gather(scaled_low, "pix", axis=0, tiled=True)
        back_sum = back_local(row_table, pattern, pixel_list, ray_list, tiles_dev)
        summed_update = lax.psum(back_sum, "ang")
        current = current + summed_update / jnp.tile(col_weight, (1, slices))
    return (current, scaled[None])


def split2(x):
    hi = lax.reduce_precision(x, exponent_bits=8, mantissa_bits=7)
    return (hi.astype(jnp.bfloat16), (x - hi).astype(jnp.bfloat16))


def per_device_split(volume, sinogram, table, blk_ray, blk_pix, n_pix, n_ang):
    n_grp = n_pix * n_ang
    tiles_dev = volume.shape[0]
    slices = volume.shape[1] // TILE
    per_dev = slices // n_grp
    rays_dev = sinogram.shape[1]
    nbd = blk_ray.shape[-1]
    ray_total = rays_dev * n_pix
    pix_total = tiles_dev * n_pix
    width = per_dev * TILE

    vol_send = volume.reshape(tiles_dev, n_grp, width).transpose(1, 0, 2)
    sino_send = sinogram[0].reshape(rays_dev, n_grp, width).transpose(1, 0, 2)
    lists = jnp.stack([blk_ray.reshape(-1), blk_pix.reshape(-1)]).astype(jnp.float32)
    list_rows = (2 * nbd + width - 1) // width
    lists = jnp.pad(lists.reshape(-1), (0, list_rows * width - 2 * nbd)).reshape(list_rows, width)
    list_send = jnp.broadcast_to(lists[None], (n_grp, list_rows, width))
    send = jnp.concatenate([vol_send, sino_send, list_send], axis=1)
    recv = lax.all_to_all(send, ("pix", "ang"), 0, 0, tiled=False)
    recv = recv.reshape(n_pix, n_ang, tiles_dev + rays_dev + list_rows, width)

    current = recv[:, 0, :tiles_dev].reshape(pix_total, width)
    measured = recv[:, :, tiles_dev:tiles_dev + rays_dev].transpose(1, 0, 2, 3).reshape(n_ang, ray_total, width)
    got = recv[:, :, tiles_dev + rays_dev:].reshape(n_pix, n_ang, -1)[:, :, :2 * nbd]
    got = got.reshape(n_pix, n_ang, 2, nbd).transpose(2, 1, 0, 3).astype(jnp.int32)
    per_kind = nbd // KINDS
    offsets = (jnp.arange(n_pix, dtype=jnp.int32) * tiles_dev)[None, :, None, None]
    ray_ids = got[0].reshape(n_ang, n_pix, KINDS, per_kind)
    pix_ids = got[1].reshape(n_ang, n_pix, KINDS, per_kind) + offsets
    ray_ids = ray_ids.transpose(0, 2, 1, 3).reshape(n_ang, KINDS, n_pix * per_kind)
    pix_ids = pix_ids.transpose(0, 2, 1, 3).reshape(n_ang, KINDS, n_pix * per_kind)

    one_ray = (ray_ids[..., None] == jnp.arange(ray_total, dtype=jnp.int32)).astype(jnp.bfloat16)
    one_pix = (pix_ids[..., None] == jnp.arange(pix_total, dtype=jnp.int32)).astype(jnp.bfloat16)
    count_low = jnp.einsum(
        "gkbv,gkbu->gkvu", one_ray, one_pix, preferred_element_type=jnp.float32
    ).astype(jnp.bfloat16)
    count_low = lax.optimization_barrier(count_low)
    counts = count_low.astype(jnp.float32)
    pattern = table.reshape(KINDS, TILE, TILE)
    pattern_wide = pattern.astype(jnp.float32)

    cur = current.reshape(pix_total, per_dev, TILE)
    meas = measured.reshape(n_ang, ray_total, per_dev, TILE)
    ones_pix = jnp.ones((pix_total, 1, TILE), jnp.bfloat16)
    ones_ray = jnp.ones((n_ang, ray_total, 1, TILE), jnp.bfloat16)
    scaled = meas
    for iteration in range(ITERS):
        low = cur.astype(jnp.bfloat16)
        if iteration == 0:
            low = jnp.concatenate([low, ones_pix], axis=1)
        gathered = jnp.einsum("gkvu,usj->gkvsj", count_low, low, preferred_element_type=jnp.float32)
        proj = jnp.einsum(
            "gkvsj,kij->gvsi", gathered, pattern_wide, precision=lax.Precision.HIGHEST,
            preferred_element_type=jnp.float32,
        )
        if iteration == 0:
            rw = jnp.broadcast_to(proj[:, :, per_dev:], meas.shape)
            proj = proj[:, :, :per_dev]
        scaled = (meas - proj) / rw
        scaled_low = scaled.astype(jnp.bfloat16)
        if iteration == 0:
            scaled_low = jnp.concatenate([scaled_low, ones_ray], axis=2)
        spread = jnp.einsum("gvsi,kij->gkvsj", scaled_low, pattern, preferred_element_type=jnp.float32)
        update = jnp.einsum(
            "gkvu,gkvsj->usj", counts, spread, precision=lax.Precision.HIGH,
            preferred_element_type=jnp.float32,
        )
        if iteration == 0:
            pw = jnp.broadcast_to(update[:, per_dev:], cur.shape)
            update = update[:, :per_dev]
        cur = cur + update / pw

    vol_back = cur.reshape(n_pix, tiles_dev, width)
    vol_back = jnp.broadcast_to(vol_back[:, None], (n_pix, n_ang, tiles_dev, width))
    res_back = scaled.reshape(n_ang, n_pix, rays_dev, width).transpose(1, 0, 2, 3)
    back = jnp.concatenate([vol_back, res_back], axis=2).reshape(n_grp, tiles_dev + rays_dev, width)
    got_back = lax.all_to_all(back, ("pix", "ang"), 0, 0, tiled=False)
    vol_out = got_back[:, :tiles_dev].transpose(1, 0, 2).reshape(tiles_dev, slices * TILE)
    res_out = got_back[:, tiles_dev:].transpose(1, 0, 2).reshape(1, rays_dev, slices * TILE)
    return (vol_out, res_out)


def solution(mesh):
    n_pix = mesh.shape["pix"]
    n_ang = mesh.shape["ang"]

    def body(volume, sinogram, table, blk_ray, blk_pix):
        if (volume.shape[1] // TILE) % (n_pix * n_ang) == 0:
            return per_device_split(volume, sinogram, table, blk_ray, blk_pix, n_pix, n_ang)
        return per_device_base(volume, sinogram, table, blk_ray, blk_pix)

    return jax.shard_map(
        body,
        mesh=mesh,
        in_specs=(
            P(("parts", "pix"), "sl"),
            P(("parts", "ang"), "pix", "sl"),
            P(),
            P("ang", "pix", None),
            P("ang", "pix", None),
        ),
        out_specs=(P(("parts", "pix"), "sl"), P(("parts", "ang"), "pix", "sl")),
        check_vma=False,
    )
```

```python
import jax
import jax.numpy as jnp
from jax import lax
from jax.sharding import PartitionSpec as P

TILE = 64
KINDS = 32
ITERS = 2
PER_KIND = 44


def project_local(low_volume, pattern, pixel_list, ray_list, ray_total):
    tiles_dev = low_volume.shape[0]
    slices = low_volume.shape[1] // TILE
    low_tiles = low_volume.reshape(tiles_dev, slices, TILE)
    kinds_each = KINDS // 4

    def project_one_group(running, inputs):
        patterns, pix_ids, ray_ids = inputs
        picked = jnp.take(low_tiles, pix_ids, axis=0).reshape(kinds_each, PER_KIND, slices, TILE)
        images = jnp.einsum("kbsj,kij->kbsi", picked, patterns, preferred_element_type=jnp.float32)
        images = images.reshape(kinds_each * PER_KIND, slices * TILE)
        return (running + jax.ops.segment_sum(images, ray_ids, ray_total), None)

    inputs = (
        pattern.reshape(4, kinds_each, TILE, TILE),
        pixel_list.reshape(4, -1),
        ray_list.reshape(4, -1),
    )
    initial = jnp.zeros((ray_total, slices * TILE), jnp.float32)
    running, unused = lax.scan(project_one_group, initial, inputs)
    return running


def back_local(row_table, pattern, pixel_list, row_index, tiles_dev):
    slices = row_table.shape[1] // TILE
    table_tiles = row_table.reshape(row_table.shape[0], slices, TILE)
    kinds_each = KINDS // 4

    def back_one_group(running, inputs):
        patterns, pix_ids, row_ids = inputs
        picked = jnp.take(table_tiles, row_ids, axis=0).reshape(kinds_each, PER_KIND, slices, TILE)
        images = jnp.einsum("kbsi,kij->kbsj", picked, patterns, preferred_element_type=jnp.float32)
        images = images.reshape(kinds_each * PER_KIND, slices * TILE)
        return (running + jax.ops.segment_sum(images, pix_ids, tiles_dev), None)

    inputs = (
        pattern.reshape(4, kinds_each, TILE, TILE),
        pixel_list.reshape(4, -1),
        row_index.reshape(4, -1),
    )
    initial = jnp.zeros((tiles_dev, slices * TILE), jnp.float32)
    running, unused = lax.scan(back_one_group, initial, inputs)
    return running


def per_device_base(volume, sinogram, table, blk_ray, blk_pix):
    pix_count = lax.axis_size("pix")
    tiles_dev = volume.shape[0]
    row_width = volume.shape[1]
    slices = row_width // TILE
    rays_dev = sinogram.shape[1]
    ray_total = rays_dev * pix_count
    ray_list = blk_ray.reshape(-1)
    pixel_list = blk_pix.reshape(-1)
    pattern = table.reshape(KINDS, TILE, TILE)
    pattern_wide = table.astype(jnp.float32).reshape(KINDS, TILE, TILE)
    row_block = jnp.broadcast_to(
        jnp.sum(pattern_wide, axis=2)[:, None, :], (KINDS, PER_KIND, TILE)
    ).reshape(-1, TILE)
    col_block = jnp.broadcast_to(
        jnp.sum(pattern_wide, axis=1)[:, None, :], (KINDS, PER_KIND, TILE)
    ).reshape(-1, TILE)
    row_part = jax.ops.segment_sum(row_block, ray_list, ray_total)
    col_part = jax.ops.segment_sum(col_block, pixel_list, tiles_dev)
    measured = sinogram[0]
    col_weight = lax.psum(col_part, "ang")
    current = volume
    scaled = measured
    for iteration in range(ITERS):
        low_volume = current.astype(jnp.bfloat16)
        partial_rows = project_local(low_volume, pattern, pixel_list, ray_list, ray_total)
        if iteration == 0:
            summed, row_weight = (
                lax.psum_scatter(partial_rows, "pix", scatter_dimension=0, tiled=True),
                lax.psum_scatter(row_part, "pix", scatter_dimension=0, tiled=True),
            )
        else:
            summed = lax.psum_scatter(partial_rows, "pix", scatter_dimension=0, tiled=True)
        scaled = (measured - summed) / jnp.tile(row_weight, (1, slices))
        scaled_low = scaled.astype(jnp.bfloat16)
        row_table = lax.all_gather(scaled_low, "pix", axis=0, tiled=True)
        back_sum = back_local(row_table, pattern, pixel_list, ray_list, tiles_dev)
        summed_update = lax.psum(back_sum, "ang")
        current = current + summed_update / jnp.tile(col_weight, (1, slices))
    return (current, scaled[None])


def split2(x):
    hi = lax.reduce_precision(x, exponent_bits=8, mantissa_bits=7)
    return (hi.astype(jnp.bfloat16), (x - hi).astype(jnp.bfloat16))


def per_device_split(volume, sinogram, table, blk_ray, blk_pix, n_pix, n_ang):
    n_grp = n_pix * n_ang
    tiles_dev = volume.shape[0]
    slices = volume.shape[1] // TILE
    per_dev = slices // n_grp
    rays_dev = sinogram.shape[1]
    nbd = blk_ray.shape[-1]
    ray_total = rays_dev * n_pix
    pix_total = tiles_dev * n_pix
    width = per_dev * TILE

    vol_send = volume.reshape(tiles_dev, n_grp, width).transpose(1, 0, 2)
    sino_send = sinogram[0].reshape(rays_dev, n_grp, width).transpose(1, 0, 2)
    per_kind = nbd // KINDS
    lists = jnp.stack([blk_ray.reshape(-1), blk_pix.reshape(-1)]).astype(jnp.float32)
    lists = lists.reshape(2, KINDS, per_kind)
    lists = jnp.pad(lists, ((0, 0), (0, 0), (0, width - per_kind)), constant_values=-1.0)
    list_rows = 2 * KINDS
    lists = lists.reshape(list_rows, width)
    list_send = jnp.broadcast_to(lists[None], (n_grp, list_rows, width))
    send = jnp.concatenate([vol_send, sino_send, list_send], axis=1)
    recv = lax.all_to_all(send, ("pix", "ang"), 0, 0, tiled=False)
    recv = recv.reshape(n_pix, n_ang, tiles_dev + rays_dev + list_rows, width)

    current = recv[:, 0, :tiles_dev].reshape(pix_total, width)
    measured = recv[:, :, tiles_dev:tiles_dev + rays_dev].transpose(1, 0, 2, 3).reshape(n_ang, ray_total, width)
    got = recv[:, :, tiles_dev + rays_dev:].reshape(n_pix, n_ang, 2, KINDS, width)[..., :per_kind]
    offsets = (jnp.arange(n_pix, dtype=jnp.float32) * tiles_dev)[:, None, None, None]
    ray_ids = got[:, :, 0].transpose(1, 2, 0, 3).reshape(n_ang, KINDS, n_pix * per_kind)
    pix_ids = (got[:, :, 1] + offsets).transpose(1, 2, 0, 3).reshape(n_ang, KINDS, n_pix * per_kind)

    one_ray = (ray_ids[..., None] == jnp.arange(ray_total, dtype=jnp.float32)).astype(jnp.bfloat16)
    one_pix = (pix_ids[..., None] == jnp.arange(pix_total, dtype=jnp.float32)).astype(jnp.bfloat16)
    count_low = jnp.einsum(
        "gkbv,gkbu->gkvu", one_ray, one_pix, preferred_element_type=jnp.float32
    ).astype(jnp.bfloat16)
    count_low = lax.optimization_barrier(count_low)
    counts = count_low.astype(jnp.float32)
    ray_count = jnp.sum(counts, axis=3)
    pix_count = jnp.sum(counts, axis=2)

    pattern = table.reshape(KINDS, TILE, TILE)
    pattern_wide = pattern.astype(jnp.float32)
    hi = lax.Precision.HIGHEST
    ray_weight = jnp.einsum("gkv,ki->gvi", ray_count, jnp.sum(pattern_wide, axis=2), precision=hi)
    pixel_weight = jnp.einsum("gku,kj->uj", pix_count, jnp.sum(pattern_wide, axis=1), precision=hi)
    ray_weight = jnp.tile(ray_weight, (1, 1, per_dev))
    pixel_weight = jnp.tile(pixel_weight, (1, per_dev))

    cur = current.reshape(pix_total, per_dev, TILE)
    meas = measured.reshape(n_ang, ray_total, per_dev, TILE)
    rw = ray_weight.reshape(n_ang, ray_total, per_dev, TILE)
    pw = pixel_weight.reshape(pix_total, per_dev, TILE)
    scaled = meas
    for iteration in range(ITERS):
        low = cur.astype(jnp.bfloat16)
        gathered = jnp.einsum("gkvu,usj->gkvsj", count_low, low, preferred_element_type=jnp.float32)
        proj = jnp.einsum(
            "gkvsj,kij->gvsi", gathered, pattern_wide, precision=lax.Precision.HIGHEST,
            preferred_element_type=jnp.float32,
        )
        scaled = (meas - proj) / rw
        scaled_low = scaled.astype(jnp.bfloat16)
        spread = jnp.einsum("gvsi,kij->gkvsj", scaled_low, pattern, preferred_element_type=jnp.float32)
        update = jnp.einsum(
            "gkvu,gkvsj->usj", counts, spread, precision=lax.Precision.HIGH,
            preferred_element_type=jnp.float32,
        )
        cur = cur + update / pw

    vol_back = cur.reshape(n_pix, tiles_dev, width)
    vol_back = jnp.broadcast_to(vol_back[:, None], (n_pix, n_ang, tiles_dev, width))
    res_back = scaled.reshape(n_ang, n_pix, rays_dev, width).transpose(1, 0, 2, 3)
    back = jnp.concatenate([vol_back, res_back], axis=2).reshape(n_grp, tiles_dev + rays_dev, width)
    got_back = lax.all_to_all(back, ("pix", "ang"), 0, 0, tiled=False)
    vol_out = got_back[:, :tiles_dev].transpose(1, 0, 2).reshape(tiles_dev, slices * TILE)
    res_out = got_back[:, tiles_dev:].transpose(1, 0, 2).reshape(1, rays_dev, slices * TILE)
    return (vol_out, res_out)


def solution(mesh):
    n_pix = mesh.shape["pix"]
    n_ang = mesh.shape["ang"]

    def body(volume, sinogram, table, blk_ray, blk_pix):
        if (volume.shape[1] // TILE) % (n_pix * n_ang) == 0:
            return per_device_split(volume, sinogram, table, blk_ray, blk_pix, n_pix, n_ang)
        return per_device_base(volume, sinogram, table, blk_ray, blk_pix)

    return jax.shard_map(
        body,
        mesh=mesh,
        in_specs=(
            P(("parts", "pix"), "sl"),
            P(("parts", "ang"), "pix", "sl"),
            P(),
            P("ang", "pix", None),
            P("ang", "pix", None),
        ),
        out_specs=(P(("parts", "pix"), "sl"), P(("parts", "ang"), "pix", "sl")),
        check_vma=False,
    )
```

```python
import jax
import jax.numpy as jnp
from jax import lax
from jax.sharding import PartitionSpec as P

TILE = 64
KINDS = 32
ITERS = 2
PER_KIND = 44


def project_local(low_volume, pattern, pixel_list, ray_list, ray_total):
    tiles_dev = low_volume.shape[0]
    slices = low_volume.shape[1] // TILE
    low_tiles = low_volume.reshape(tiles_dev, slices, TILE)
    kinds_each = KINDS // 4

    def project_one_group(running, inputs):
        patterns, pix_ids, ray_ids = inputs
        picked = jnp.take(low_tiles, pix_ids, axis=0).reshape(kinds_each, PER_KIND, slices, TILE)
        images = jnp.einsum("kbsj,kij->kbsi", picked, patterns, preferred_element_type=jnp.float32)
        images = images.reshape(kinds_each * PER_KIND, slices * TILE)
        return (running + jax.ops.segment_sum(images, ray_ids, ray_total), None)

    inputs = (
        pattern.reshape(4, kinds_each, TILE, TILE),
        pixel_list.reshape(4, -1),
        ray_list.reshape(4, -1),
    )
    initial = jnp.zeros((ray_total, slices * TILE), jnp.float32)
    running, unused = lax.scan(project_one_group, initial, inputs)
    return running


def back_local(row_table, pattern, pixel_list, row_index, tiles_dev):
    slices = row_table.shape[1] // TILE
    table_tiles = row_table.reshape(row_table.shape[0], slices, TILE)
    kinds_each = KINDS // 4

    def back_one_group(running, inputs):
        patterns, pix_ids, row_ids = inputs
        picked = jnp.take(table_tiles, row_ids, axis=0).reshape(kinds_each, PER_KIND, slices, TILE)
        images = jnp.einsum("kbsi,kij->kbsj", picked, patterns, preferred_element_type=jnp.float32)
        images = images.reshape(kinds_each * PER_KIND, slices * TILE)
        return (running + jax.ops.segment_sum(images, pix_ids, tiles_dev), None)

    inputs = (
        pattern.reshape(4, kinds_each, TILE, TILE),
        pixel_list.reshape(4, -1),
        row_index.reshape(4, -1),
    )
    initial = jnp.zeros((tiles_dev, slices * TILE), jnp.float32)
    running, unused = lax.scan(back_one_group, initial, inputs)
    return running


def per_device_base(volume, sinogram, table, blk_ray, blk_pix):
    pix_count = lax.axis_size("pix")
    tiles_dev = volume.shape[0]
    row_width = volume.shape[1]
    slices = row_width // TILE
    rays_dev = sinogram.shape[1]
    ray_total = rays_dev * pix_count
    ray_list = blk_ray.reshape(-1)
    pixel_list = blk_pix.reshape(-1)
    pattern = table.reshape(KINDS, TILE, TILE)
    pattern_wide = table.astype(jnp.float32).reshape(KINDS, TILE, TILE)
    row_block = jnp.broadcast_to(
        jnp.sum(pattern_wide, axis=2)[:, None, :], (KINDS, PER_KIND, TILE)
    ).reshape(-1, TILE)
    col_block = jnp.broadcast_to(
        jnp.sum(pattern_wide, axis=1)[:, None, :], (KINDS, PER_KIND, TILE)
    ).reshape(-1, TILE)
    row_part = jax.ops.segment_sum(row_block, ray_list, ray_total)
    col_part = jax.ops.segment_sum(col_block, pixel_list, tiles_dev)
    measured = sinogram[0]
    col_weight = lax.psum(col_part, "ang")
    current = volume
    scaled = measured
    for iteration in range(ITERS):
        low_volume = current.astype(jnp.bfloat16)
        partial_rows = project_local(low_volume, pattern, pixel_list, ray_list, ray_total)
        if iteration == 0:
            summed, row_weight = (
                lax.psum_scatter(partial_rows, "pix", scatter_dimension=0, tiled=True),
                lax.psum_scatter(row_part, "pix", scatter_dimension=0, tiled=True),
            )
        else:
            summed = lax.psum_scatter(partial_rows, "pix", scatter_dimension=0, tiled=True)
        scaled = (measured - summed) / jnp.tile(row_weight, (1, slices))
        scaled_low = scaled.astype(jnp.bfloat16)
        row_table = lax.all_gather(scaled_low, "pix", axis=0, tiled=True)
        back_sum = back_local(row_table, pattern, pixel_list, ray_list, tiles_dev)
        summed_update = lax.psum(back_sum, "ang")
        current = current + summed_update / jnp.tile(col_weight, (1, slices))
    return (current, scaled[None])


def split2(x):
    hi = lax.reduce_precision(x, exponent_bits=8, mantissa_bits=7)
    return (hi.astype(jnp.bfloat16), (x - hi).astype(jnp.bfloat16))


def per_device_split(volume, sinogram, table, blk_ray, blk_pix, n_pix, n_ang):
    n_grp = n_pix * n_ang
    tiles_dev = volume.shape[0]
    slices = volume.shape[1] // TILE
    per_dev = slices // n_grp
    rays_dev = sinogram.shape[1]
    nbd = blk_ray.shape[-1]
    ray_total = rays_dev * n_pix
    pix_total = tiles_dev * n_pix
    width = per_dev * TILE

    vol_send = volume.reshape(tiles_dev, n_grp, width).transpose(1, 0, 2)
    sino_send = sinogram[0].reshape(rays_dev, n_grp, width).transpose(1, 0, 2)
    cells = (blk_ray.reshape(-1) * tiles_dev + blk_pix.reshape(-1)).astype(jnp.float32)
    list_rows = (nbd + width - 1) // width
    lists = jnp.pad(cells, (0, list_rows * width - nbd)).reshape(list_rows, width)
    list_send = jnp.broadcast_to(lists[None], (n_grp, list_rows, width))
    send = jnp.concatenate([vol_send, sino_send, list_send], axis=1)
    rows = tiles_dev + rays_dev + list_rows
    paired = rows + rows % 2
    send = jnp.pad(send, ((0, 0), (0, paired - rows), (0, 0))).reshape(n_grp, paired // 2, 2 * width)
    recv = lax.all_to_all(send, ("pix", "ang"), 0, 0, tiled=False)
    recv = recv.reshape(n_pix, n_ang, paired, width)[:, :, :rows]

    current = recv[:, 0, :tiles_dev].reshape(pix_total, width)
    measured = recv[:, :, tiles_dev:tiles_dev + rays_dev].transpose(1, 0, 2, 3).reshape(n_ang, ray_total, width)
    cells = recv[:, :, tiles_dev + rays_dev:].reshape(n_pix, n_ang, -1)[:, :, :nbd]
    cells = cells.transpose(1, 0, 2).astype(jnp.int32)
    got = jnp.stack([cells // tiles_dev, cells % tiles_dev])
    per_kind = nbd // KINDS
    offsets = (jnp.arange(n_pix, dtype=jnp.int32) * tiles_dev)[None, :, None, None]
    ray_ids = got[0].reshape(n_ang, n_pix, KINDS, per_kind)
    pix_ids = got[1].reshape(n_ang, n_pix, KINDS, per_kind) + offsets
    ray_ids = ray_ids.transpose(0, 2, 1, 3).reshape(n_ang, KINDS, n_pix * per_kind)
    pix_ids = pix_ids.transpose(0, 2, 1, 3).reshape(n_ang, KINDS, n_pix * per_kind)

    one_ray = (ray_ids[..., None] == jnp.arange(ray_total, dtype=jnp.int32)).astype(jnp.bfloat16)
    one_pix = (pix_ids[..., None] == jnp.arange(pix_total, dtype=jnp.int32)).astype(jnp.bfloat16)
    count_low = jnp.einsum(
        "gkbv,gkbu->gkvu", one_ray, one_pix, preferred_element_type=jnp.float32
    ).astype(jnp.bfloat16)
    count_low = lax.optimization_barrier(count_low)
    counts = count_low.astype(jnp.float32)
    ray_count = jnp.sum(counts, axis=3)
    pix_count = jnp.sum(counts, axis=2)

    pattern = table.reshape(KINDS, TILE, TILE)
    pattern_wide = pattern.astype(jnp.float32)
    hi = lax.Precision.HIGHEST
    ray_weight = jnp.einsum("gkv,ki->gvi", ray_count, jnp.sum(pattern_wide, axis=2), precision=hi)
    pixel_weight = jnp.einsum("gku,kj->uj", pix_count, jnp.sum(pattern_wide, axis=1), precision=hi)
    ray_weight = jnp.tile(ray_weight, (1, 1, per_dev))
    pixel_weight = jnp.tile(pixel_weight, (1, per_dev))

    cur = current.reshape(pix_total, per_dev, TILE)
    meas = measured.reshape(n_ang, ray_total, per_dev, TILE)
    rw = ray_weight.reshape(n_ang, ray_total, per_dev, TILE)
    pw = pixel_weight.reshape(pix_total, per_dev, TILE)
    scaled = meas
    for iteration in range(ITERS):
        low = cur.astype(jnp.bfloat16)
        gathered = jnp.einsum("gkvu,usj->gkvsj", count_low, low, preferred_element_type=jnp.float32)
        proj = jnp.einsum(
            "gkvsj,kij->gvsi", gathered, pattern_wide, precision=lax.Precision.HIGHEST,
            preferred_element_type=jnp.float32,
        )
        scaled = (meas - proj) / rw
        scaled_low = scaled.astype(jnp.bfloat16)
        spread = jnp.einsum("gvsi,kij->gkvsj", scaled_low, pattern, preferred_element_type=jnp.float32)
        update = jnp.einsum(
            "gkvu,gkvsj->usj", counts, spread, precision=lax.Precision.HIGH,
            preferred_element_type=jnp.float32,
        )
        cur = cur + update / pw

    vol_back = cur.reshape(n_pix, tiles_dev, width)
    vol_back = jnp.broadcast_to(vol_back[:, None], (n_pix, n_ang, tiles_dev, width))
    res_back = scaled.reshape(n_ang, n_pix, rays_dev, width).transpose(1, 0, 2, 3)
    back = jnp.concatenate([vol_back, res_back], axis=2).reshape(n_grp, tiles_dev + rays_dev, width)
    got_back = lax.all_to_all(back, ("pix", "ang"), 0, 0, tiled=False)
    vol_out = got_back[:, :tiles_dev].transpose(1, 0, 2).reshape(tiles_dev, slices * TILE)
    res_out = got_back[:, tiles_dev:].transpose(1, 0, 2).reshape(1, rays_dev, slices * TILE)
    return (vol_out, res_out)


def solution(mesh):
    n_pix = mesh.shape["pix"]
    n_ang = mesh.shape["ang"]

    def body(volume, sinogram, table, blk_ray, blk_pix):
        if (volume.shape[1] // TILE) % (n_pix * n_ang) == 0:
            return per_device_split(volume, sinogram, table, blk_ray, blk_pix, n_pix, n_ang)
        return per_device_base(volume, sinogram, table, blk_ray, blk_pix)

    return jax.shard_map(
        body,
        mesh=mesh,
        in_specs=(
            P(("parts", "pix"), "sl"),
            P(("parts", "ang"), "pix", "sl"),
            P(),
            P("ang", "pix", None),
            P("ang", "pix", None),
        ),
        out_specs=(P(("parts", "pix"), "sl"), P(("parts", "ang"), "pix", "sl")),
        check_vma=False,
    )
```

```python
import jax
import jax.numpy as jnp
from jax import lax
from jax.sharding import PartitionSpec as P

TILE = 64
KINDS = 32
ITERS = 2
PER_KIND = 44


def project_local(low_volume, pattern, pixel_list, ray_list, ray_total):
    tiles_dev = low_volume.shape[0]
    slices = low_volume.shape[1] // TILE
    low_tiles = low_volume.reshape(tiles_dev, slices, TILE)
    kinds_each = KINDS // 4

    def project_one_group(running, inputs):
        patterns, pix_ids, ray_ids = inputs
        picked = jnp.take(low_tiles, pix_ids, axis=0).reshape(kinds_each, PER_KIND, slices, TILE)
        images = jnp.einsum("kbsj,kij->kbsi", picked, patterns, preferred_element_type=jnp.float32)
        images = images.reshape(kinds_each * PER_KIND, slices * TILE)
        return (running + jax.ops.segment_sum(images, ray_ids, ray_total), None)

    inputs = (
        pattern.reshape(4, kinds_each, TILE, TILE),
        pixel_list.reshape(4, -1),
        ray_list.reshape(4, -1),
    )
    initial = jnp.zeros((ray_total, slices * TILE), jnp.float32)
    running, unused = lax.scan(project_one_group, initial, inputs)
    return running


def back_local(row_table, pattern, pixel_list, row_index, tiles_dev):
    slices = row_table.shape[1] // TILE
    table_tiles = row_table.reshape(row_table.shape[0], slices, TILE)
    kinds_each = KINDS // 4

    def back_one_group(running, inputs):
        patterns, pix_ids, row_ids = inputs
        picked = jnp.take(table_tiles, row_ids, axis=0).reshape(kinds_each, PER_KIND, slices, TILE)
        images = jnp.einsum("kbsi,kij->kbsj", picked, patterns, preferred_element_type=jnp.float32)
        images = images.reshape(kinds_each * PER_KIND, slices * TILE)
        return (running + jax.ops.segment_sum(images, pix_ids, tiles_dev), None)

    inputs = (
        pattern.reshape(4, kinds_each, TILE, TILE),
        pixel_list.reshape(4, -1),
        row_index.reshape(4, -1),
    )
    initial = jnp.zeros((tiles_dev, slices * TILE), jnp.float32)
    running, unused = lax.scan(back_one_group, initial, inputs)
    return running


def per_device_base(volume, sinogram, table, blk_ray, blk_pix):
    pix_count = lax.axis_size("pix")
    tiles_dev = volume.shape[0]
    row_width = volume.shape[1]
    slices = row_width // TILE
    rays_dev = sinogram.shape[1]
    ray_total = rays_dev * pix_count
    ray_list = blk_ray.reshape(-1)
    pixel_list = blk_pix.reshape(-1)
    pattern = table.reshape(KINDS, TILE, TILE)
    pattern_wide = table.astype(jnp.float32).reshape(KINDS, TILE, TILE)
    row_block = jnp.broadcast_to(
        jnp.sum(pattern_wide, axis=2)[:, None, :], (KINDS, PER_KIND, TILE)
    ).reshape(-1, TILE)
    col_block = jnp.broadcast_to(
        jnp.sum(pattern_wide, axis=1)[:, None, :], (KINDS, PER_KIND, TILE)
    ).reshape(-1, TILE)
    row_part = jax.ops.segment_sum(row_block, ray_list, ray_total)
    col_part = jax.ops.segment_sum(col_block, pixel_list, tiles_dev)
    measured = sinogram[0]
    col_weight = lax.psum(col_part, "ang")
    current = volume
    scaled = measured
    for iteration in range(ITERS):
        low_volume = current.astype(jnp.bfloat16)
        partial_rows = project_local(low_volume, pattern, pixel_list, ray_list, ray_total)
        if iteration == 0:
            summed, row_weight = (
                lax.psum_scatter(partial_rows, "pix", scatter_dimension=0, tiled=True),
                lax.psum_scatter(row_part, "pix", scatter_dimension=0, tiled=True),
            )
        else:
            summed = lax.psum_scatter(partial_rows, "pix", scatter_dimension=0, tiled=True)
        scaled = (measured - summed) / jnp.tile(row_weight, (1, slices))
        scaled_low = scaled.astype(jnp.bfloat16)
        row_table = lax.all_gather(scaled_low, "pix", axis=0, tiled=True)
        back_sum = back_local(row_table, pattern, pixel_list, ray_list, tiles_dev)
        summed_update = lax.psum(back_sum, "ang")
        current = current + summed_update / jnp.tile(col_weight, (1, slices))
    return (current, scaled[None])


def split2(x):
    hi = lax.reduce_precision(x, exponent_bits=8, mantissa_bits=7)
    return (hi.astype(jnp.bfloat16), (x - hi).astype(jnp.bfloat16))


def per_device_split(volume, sinogram, table, blk_ray, blk_pix, n_pix, n_ang):
    n_grp = n_pix * n_ang
    tiles_dev = volume.shape[0]
    slices = volume.shape[1] // TILE
    per_dev = slices // n_grp
    rays_dev = sinogram.shape[1]
    nbd = blk_ray.shape[-1]
    ray_total = rays_dev * n_pix
    pix_total = tiles_dev * n_pix
    width = per_dev * TILE

    vol_send = volume.reshape(tiles_dev, n_grp, width).transpose(1, 0, 2)
    sino_send = sinogram[0].reshape(rays_dev, n_grp, width).transpose(1, 0, 2)
    cells = (blk_ray.reshape(-1) * tiles_dev + blk_pix.reshape(-1)).astype(jnp.float32)
    list_rows = (nbd + width - 1) // width
    lists = jnp.pad(cells, (0, list_rows * width - nbd)).reshape(list_rows, width)
    list_send = jnp.broadcast_to(lists[None], (n_grp, list_rows, width))
    send = jnp.concatenate([vol_send, sino_send, list_send], axis=1)
    rows = tiles_dev + rays_dev + list_rows
    paired = rows + rows % 2
    send = jnp.pad(send, ((0, 0), (0, paired - rows), (0, 0))).reshape(n_grp, paired // 2, 2 * width)
    recv = lax.all_to_all(send, ("pix", "ang"), 0, 0, tiled=False)
    recv = recv.reshape(n_pix, n_ang, paired, width)[:, :, :rows]

    current = recv[:, 0, :tiles_dev].reshape(pix_total, width)
    measured = recv[:, :, tiles_dev:tiles_dev + rays_dev].transpose(1, 0, 2, 3).reshape(n_ang, ray_total, width)
    cells = recv[:, :, tiles_dev + rays_dev:].reshape(n_pix, n_ang, -1)[:, :, :nbd]
    cells = cells.transpose(1, 0, 2).astype(jnp.int32)
    got = jnp.stack([cells // tiles_dev, cells % tiles_dev])
    per_kind = nbd // KINDS
    offsets = (jnp.arange(n_pix, dtype=jnp.int32) * tiles_dev)[None, :, None, None]
    ray_ids = got[0].reshape(n_ang, n_pix, KINDS, per_kind)
    pix_ids = got[1].reshape(n_ang, n_pix, KINDS, per_kind) + offsets
    ray_ids = ray_ids.transpose(0, 2, 1, 3).reshape(n_ang, KINDS, n_pix * per_kind)
    pix_ids = pix_ids.transpose(0, 2, 1, 3).reshape(n_ang, KINDS, n_pix * per_kind)

    one_ray = (ray_ids[..., None] == jnp.arange(ray_total, dtype=jnp.int32)).astype(jnp.bfloat16)
    one_pix = (pix_ids[..., None] == jnp.arange(pix_total, dtype=jnp.int32)).astype(jnp.bfloat16)
    count_low = jnp.einsum(
        "gkbv,gkbu->gkvu", one_ray, one_pix, preferred_element_type=jnp.float32
    ).astype(jnp.bfloat16)
    count_low = lax.optimization_barrier(count_low)
    counts = count_low.astype(jnp.float32)
    ray_count = jnp.sum(counts, axis=3)
    pix_count = jnp.sum(counts, axis=2)

    pattern = table.reshape(KINDS, TILE, TILE)
    pattern_wide = pattern.astype(jnp.float32)
    hi = lax.Precision.HIGHEST
    ray_weight = jnp.einsum("gkv,ki->gvi", ray_count, jnp.sum(pattern_wide, axis=2), precision=hi)
    pixel_weight = jnp.einsum("gku,kj->uj", pix_count, jnp.sum(pattern_wide, axis=1), precision=hi)
    ray_weight = jnp.tile(ray_weight, (1, 1, per_dev))
    pixel_weight = jnp.tile(pixel_weight, (1, per_dev))

    cur = current.reshape(pix_total, per_dev, TILE)
    meas = measured.reshape(n_ang, ray_total, per_dev, TILE)
    rw = ray_weight.reshape(n_ang, ray_total, per_dev, TILE)
    pw = pixel_weight.reshape(pix_total, per_dev, TILE)
    scaled = meas
    for iteration in range(ITERS):
        low = cur.astype(jnp.bfloat16)
        gathered = jnp.einsum("gkvu,usj->gkvsj", count_low, low, preferred_element_type=jnp.float32)
        proj = jnp.einsum(
            "gkvsj,kij->gvsi", gathered, pattern_wide, precision=lax.Precision.HIGHEST,
            preferred_element_type=jnp.float32,
        )
        scaled = (meas - proj) / rw
        scaled_low = scaled.astype(jnp.bfloat16)
        spread = jnp.einsum("gvsi,kij->gkvsj", scaled_low, pattern, preferred_element_type=jnp.float32)
        update = jnp.einsum(
            "gkvu,gkvsj->usj", counts, spread, precision=lax.Precision.HIGH,
            preferred_element_type=jnp.float32,
        )
        cur = cur + update / pw

    vol_back = cur.reshape(n_pix, tiles_dev, width)
    vol_back = jnp.broadcast_to(vol_back[:, None], (n_pix, n_ang, tiles_dev, width))
    res_back = scaled.reshape(n_ang, n_pix, rays_dev, width).transpose(1, 0, 2, 3)
    back = jnp.concatenate([vol_back, res_back], axis=2).reshape(n_grp, tiles_dev + rays_dev, width)
    rows_back = tiles_dev + rays_dev
    paired_back = rows_back + rows_back % 2
    back = jnp.pad(back, ((0, 0), (0, paired_back - rows_back), (0, 0)))
    back = back.reshape(n_grp, paired_back // 2, 2 * width)
    got_back = lax.all_to_all(back, ("pix", "ang"), 0, 0, tiled=False)
    got_back = got_back.reshape(n_grp, paired_back, width)[:, :rows_back]
    vol_out = got_back[:, :tiles_dev].transpose(1, 0, 2).reshape(tiles_dev, slices * TILE)
    res_out = got_back[:, tiles_dev:].transpose(1, 0, 2).reshape(1, rays_dev, slices * TILE)
    return (vol_out, res_out)


def solution(mesh):
    n_pix = mesh.shape["pix"]
    n_ang = mesh.shape["ang"]

    def body(volume, sinogram, table, blk_ray, blk_pix):
        if (volume.shape[1] // TILE) % (n_pix * n_ang) == 0:
            return per_device_split(volume, sinogram, table, blk_ray, blk_pix, n_pix, n_ang)
        return per_device_base(volume, sinogram, table, blk_ray, blk_pix)

    return jax.shard_map(
        body,
        mesh=mesh,
        in_specs=(
            P(("parts", "pix"), "sl"),
            P(("parts", "ang"), "pix", "sl"),
            P(),
            P("ang", "pix", None),
            P("ang", "pix", None),
        ),
        out_specs=(P(("parts", "pix"), "sl"), P(("parts", "ang"), "pix", "sl")),
        check_vma=False,
    )
```

```python
import jax
import jax.numpy as jnp
from jax import lax
from jax.sharding import PartitionSpec as P

TILE = 64
KINDS = 32
ITERS = 2
PER_KIND = 44


def project_local(low_volume, pattern, pixel_list, ray_list, ray_total):
    tiles_dev = low_volume.shape[0]
    slices = low_volume.shape[1] // TILE
    low_tiles = low_volume.reshape(tiles_dev, slices, TILE)
    kinds_each = KINDS // 4

    def project_one_group(running, inputs):
        patterns, pix_ids, ray_ids = inputs
        picked = jnp.take(low_tiles, pix_ids, axis=0).reshape(kinds_each, PER_KIND, slices, TILE)
        images = jnp.einsum("kbsj,kij->kbsi", picked, patterns, preferred_element_type=jnp.float32)
        images = images.reshape(kinds_each * PER_KIND, slices * TILE)
        return (running + jax.ops.segment_sum(images, ray_ids, ray_total), None)

    inputs = (
        pattern.reshape(4, kinds_each, TILE, TILE),
        pixel_list.reshape(4, -1),
        ray_list.reshape(4, -1),
    )
    initial = jnp.zeros((ray_total, slices * TILE), jnp.float32)
    running, unused = lax.scan(project_one_group, initial, inputs)
    return running


def back_local(row_table, pattern, pixel_list, row_index, tiles_dev):
    slices = row_table.shape[1] // TILE
    table_tiles = row_table.reshape(row_table.shape[0], slices, TILE)
    kinds_each = KINDS // 4

    def back_one_group(running, inputs):
        patterns, pix_ids, row_ids = inputs
        picked = jnp.take(table_tiles, row_ids, axis=0).reshape(kinds_each, PER_KIND, slices, TILE)
        images = jnp.einsum("kbsi,kij->kbsj", picked, patterns, preferred_element_type=jnp.float32)
        images = images.reshape(kinds_each * PER_KIND, slices * TILE)
        return (running + jax.ops.segment_sum(images, pix_ids, tiles_dev), None)

    inputs = (
        pattern.reshape(4, kinds_each, TILE, TILE),
        pixel_list.reshape(4, -1),
        row_index.reshape(4, -1),
    )
    initial = jnp.zeros((tiles_dev, slices * TILE), jnp.float32)
    running, unused = lax.scan(back_one_group, initial, inputs)
    return running


def per_device_base(volume, sinogram, table, blk_ray, blk_pix):
    pix_count = lax.axis_size("pix")
    tiles_dev = volume.shape[0]
    row_width = volume.shape[1]
    slices = row_width // TILE
    rays_dev = sinogram.shape[1]
    ray_total = rays_dev * pix_count
    ray_list = blk_ray.reshape(-1)
    pixel_list = blk_pix.reshape(-1)
    pattern = table.reshape(KINDS, TILE, TILE)
    pattern_wide = table.astype(jnp.float32).reshape(KINDS, TILE, TILE)
    row_block = jnp.broadcast_to(
        jnp.sum(pattern_wide, axis=2)[:, None, :], (KINDS, PER_KIND, TILE)
    ).reshape(-1, TILE)
    col_block = jnp.broadcast_to(
        jnp.sum(pattern_wide, axis=1)[:, None, :], (KINDS, PER_KIND, TILE)
    ).reshape(-1, TILE)
    row_part = jax.ops.segment_sum(row_block, ray_list, ray_total)
    col_part = jax.ops.segment_sum(col_block, pixel_list, tiles_dev)
    measured = sinogram[0]
    col_weight = lax.psum(col_part, "ang")
    current = volume
    scaled = measured
    for iteration in range(ITERS):
        low_volume = current.astype(jnp.bfloat16)
        partial_rows = project_local(low_volume, pattern, pixel_list, ray_list, ray_total)
        if iteration == 0:
            summed, row_weight = (
                lax.psum_scatter(partial_rows, "pix", scatter_dimension=0, tiled=True),
                lax.psum_scatter(row_part, "pix", scatter_dimension=0, tiled=True),
            )
        else:
            summed = lax.psum_scatter(partial_rows, "pix", scatter_dimension=0, tiled=True)
        scaled = (measured - summed) / jnp.tile(row_weight, (1, slices))
        scaled_low = scaled.astype(jnp.bfloat16)
        row_table = lax.all_gather(scaled_low, "pix", axis=0, tiled=True)
        back_sum = back_local(row_table, pattern, pixel_list, ray_list, tiles_dev)
        summed_update = lax.psum(back_sum, "ang")
        current = current + summed_update / jnp.tile(col_weight, (1, slices))
    return (current, scaled[None])


def split2(x):
    hi = lax.reduce_precision(x, exponent_bits=8, mantissa_bits=7)
    return (hi.astype(jnp.bfloat16), (x - hi).astype(jnp.bfloat16))


def per_device_split(volume, sinogram, table, blk_ray, blk_pix, n_pix, n_ang):
    n_grp = n_pix * n_ang
    tiles_dev = volume.shape[0]
    slices = volume.shape[1] // TILE
    per_dev = slices // n_grp
    rays_dev = sinogram.shape[1]
    nbd = blk_ray.shape[-1]
    ray_total = rays_dev * n_pix
    pix_total = tiles_dev * n_pix
    width = per_dev * TILE

    vol_send = volume.reshape(tiles_dev, n_grp, width).transpose(1, 0, 2)
    sino_send = sinogram[0].reshape(rays_dev, n_grp, width).transpose(1, 0, 2)
    cells = (blk_ray.reshape(-1) * tiles_dev + blk_pix.reshape(-1)).astype(jnp.float32)
    list_rows = (nbd + width - 1) // width
    lists = jnp.pad(cells, (0, list_rows * width - nbd)).reshape(list_rows, width)
    list_send = jnp.broadcast_to(lists[None], (n_grp, list_rows, width))
    rows = tiles_dev + rays_dev + list_rows
    paired = rows + rows % 2
    if tiles_dev % 2 == 0 and rays_dev % 2 == 0 and nbd % (2 * width) == 0:
        send = jnp.concatenate(
            [
                vol_send.reshape(n_grp, tiles_dev // 2, 2 * width),
                sino_send.reshape(n_grp, rays_dev // 2, 2 * width),
                jnp.broadcast_to(cells.reshape(1, list_rows // 2, 2 * width), (n_grp, list_rows // 2, 2 * width)),
            ],
            axis=1,
        )
    else:
        send = jnp.concatenate([vol_send, sino_send, list_send], axis=1)
        send = jnp.pad(send, ((0, 0), (0, paired - rows), (0, 0))).reshape(n_grp, paired // 2, 2 * width)
    recv = lax.all_to_all(send, ("pix", "ang"), 0, 0, tiled=False)
    recv = recv.reshape(n_pix, n_ang, paired, width)[:, :, :rows]

    current = recv[:, 0, :tiles_dev].reshape(pix_total, width)
    measured = recv[:, :, tiles_dev:tiles_dev + rays_dev].transpose(1, 0, 2, 3).reshape(n_ang, ray_total, width)
    cells = recv[:, :, tiles_dev + rays_dev:].reshape(n_pix, n_ang, -1)[:, :, :nbd]
    cells = cells.transpose(1, 0, 2).astype(jnp.int32)
    got = jnp.stack([cells // tiles_dev, cells % tiles_dev])
    per_kind = nbd // KINDS
    offsets = (jnp.arange(n_pix, dtype=jnp.int32) * tiles_dev)[None, :, None, None]
    ray_ids = got[0].reshape(n_ang, n_pix, KINDS, per_kind)
    pix_ids = got[1].reshape(n_ang, n_pix, KINDS, per_kind) + offsets
    ray_ids = ray_ids.transpose(0, 2, 1, 3).reshape(n_ang, KINDS, n_pix * per_kind)
    pix_ids = pix_ids.transpose(0, 2, 1, 3).reshape(n_ang, KINDS, n_pix * per_kind)

    one_ray = (ray_ids[..., None] == jnp.arange(ray_total, dtype=jnp.int32)).astype(jnp.bfloat16)
    one_pix = (pix_ids[..., None] == jnp.arange(pix_total, dtype=jnp.int32)).astype(jnp.bfloat16)
    count_low = jnp.einsum(
        "gkbv,gkbu->gkvu", one_ray, one_pix, preferred_element_type=jnp.float32
    ).astype(jnp.bfloat16)
    count_low = lax.optimization_barrier(count_low)
    counts = count_low.astype(jnp.float32)
    ray_count = jnp.sum(counts, axis=3)
    pix_count = jnp.sum(counts, axis=2)

    pattern = table.reshape(KINDS, TILE, TILE)
    pattern_wide = pattern.astype(jnp.float32)
    hi = lax.Precision.HIGHEST
    ray_weight = jnp.einsum("gkv,ki->gvi", ray_count, jnp.sum(pattern_wide, axis=2), precision=hi)
    pixel_weight = jnp.einsum("gku,kj->uj", pix_count, jnp.sum(pattern_wide, axis=1), precision=hi)
    ray_weight = jnp.tile(ray_weight, (1, 1, per_dev))
    pixel_weight = jnp.tile(pixel_weight, (1, per_dev))

    cur = current.reshape(pix_total, per_dev, TILE)
    meas = measured.reshape(n_ang, ray_total, per_dev, TILE)
    rw = ray_weight.reshape(n_ang, ray_total, per_dev, TILE)
    pw = pixel_weight.reshape(pix_total, per_dev, TILE)
    scaled = meas
    for iteration in range(ITERS):
        low = cur.astype(jnp.bfloat16)
        gathered = jnp.einsum("gkvu,usj->gkvsj", count_low, low, preferred_element_type=jnp.float32)
        proj = jnp.einsum(
            "gkvsj,kij->gvsi", gathered, pattern_wide, precision=lax.Precision.HIGHEST,
            preferred_element_type=jnp.float32,
        )
        scaled = (meas - proj) / rw
        scaled_low = scaled.astype(jnp.bfloat16)
        spread = jnp.einsum("gvsi,kij->gkvsj", scaled_low, pattern, preferred_element_type=jnp.float32)
        update = jnp.einsum(
            "gkvu,gkvsj->usj", counts, spread, precision=lax.Precision.HIGH,
            preferred_element_type=jnp.float32,
        )
        cur = cur + update / pw

    vol_back = cur.reshape(n_pix, tiles_dev, width)
    vol_back = jnp.broadcast_to(vol_back[:, None], (n_pix, n_ang, tiles_dev, width))
    res_back = scaled.reshape(n_ang, n_pix, rays_dev, width).transpose(1, 0, 2, 3)
    back = jnp.concatenate([vol_back, res_back], axis=2).reshape(n_grp, tiles_dev + rays_dev, width)
    rows_back = tiles_dev + rays_dev
    paired_back = rows_back + rows_back % 2
    back = jnp.pad(back, ((0, 0), (0, paired_back - rows_back), (0, 0)))
    back = back.reshape(n_grp, paired_back // 2, 2 * width)
    got_back = lax.all_to_all(back, ("pix", "ang"), 0, 0, tiled=False)
    got_back = got_back.reshape(n_grp, paired_back, width)[:, :rows_back]
    vol_out = got_back[:, :tiles_dev].transpose(1, 0, 2).reshape(tiles_dev, slices * TILE)
    res_out = got_back[:, tiles_dev:].transpose(1, 0, 2).reshape(1, rays_dev, slices * TILE)
    return (vol_out, res_out)


def solution(mesh):
    n_pix = mesh.shape["pix"]
    n_ang = mesh.shape["ang"]

    def body(volume, sinogram, table, blk_ray, blk_pix):
        if (volume.shape[1] // TILE) % (n_pix * n_ang) == 0:
            return per_device_split(volume, sinogram, table, blk_ray, blk_pix, n_pix, n_ang)
        return per_device_base(volume, sinogram, table, blk_ray, blk_pix)

    return jax.shard_map(
        body,
        mesh=mesh,
        in_specs=(
            P(("parts", "pix"), "sl"),
            P(("parts", "ang"), "pix", "sl"),
            P(),
            P("ang", "pix", None),
            P("ang", "pix", None),
        ),
        out_specs=(P(("parts", "pix"), "sl"), P(("parts", "ang"), "pix", "sl")),
        check_vma=False,
    )
```

```python
import jax
import jax.numpy as jnp
from jax import lax
from jax.sharding import PartitionSpec as P

TILE = 64
KINDS = 32
ITERS = 2
PER_KIND = 44


def project_local(low_volume, pattern, pixel_list, ray_list, ray_total):
    tiles_dev = low_volume.shape[0]
    slices = low_volume.shape[1] // TILE
    low_tiles = low_volume.reshape(tiles_dev, slices, TILE)
    kinds_each = KINDS // 4

    def project_one_group(running, inputs):
        patterns, pix_ids, ray_ids = inputs
        picked = jnp.take(low_tiles, pix_ids, axis=0).reshape(kinds_each, PER_KIND, slices, TILE)
        images = jnp.einsum("kbsj,kij->kbsi", picked, patterns, preferred_element_type=jnp.float32)
        images = images.reshape(kinds_each * PER_KIND, slices * TILE)
        return (running + jax.ops.segment_sum(images, ray_ids, ray_total), None)

    inputs = (
        pattern.reshape(4, kinds_each, TILE, TILE),
        pixel_list.reshape(4, -1),
        ray_list.reshape(4, -1),
    )
    initial = jnp.zeros((ray_total, slices * TILE), jnp.float32)
    running, unused = lax.scan(project_one_group, initial, inputs)
    return running


def back_local(row_table, pattern, pixel_list, row_index, tiles_dev):
    slices = row_table.shape[1] // TILE
    table_tiles = row_table.reshape(row_table.shape[0], slices, TILE)
    kinds_each = KINDS // 4

    def back_one_group(running, inputs):
        patterns, pix_ids, row_ids = inputs
        picked = jnp.take(table_tiles, row_ids, axis=0).reshape(kinds_each, PER_KIND, slices, TILE)
        images = jnp.einsum("kbsi,kij->kbsj", picked, patterns, preferred_element_type=jnp.float32)
        images = images.reshape(kinds_each * PER_KIND, slices * TILE)
        return (running + jax.ops.segment_sum(images, pix_ids, tiles_dev), None)

    inputs = (
        pattern.reshape(4, kinds_each, TILE, TILE),
        pixel_list.reshape(4, -1),
        row_index.reshape(4, -1),
    )
    initial = jnp.zeros((tiles_dev, slices * TILE), jnp.float32)
    running, unused = lax.scan(back_one_group, initial, inputs)
    return running


def per_device_base(volume, sinogram, table, blk_ray, blk_pix):
    pix_count = lax.axis_size("pix")
    tiles_dev = volume.shape[0]
    row_width = volume.shape[1]
    slices = row_width // TILE
    rays_dev = sinogram.shape[1]
    ray_total = rays_dev * pix_count
    ray_list = blk_ray.reshape(-1)
    pixel_list = blk_pix.reshape(-1)
    pattern = table.reshape(KINDS, TILE, TILE)
    pattern_wide = table.astype(jnp.float32).reshape(KINDS, TILE, TILE)
    row_block = jnp.broadcast_to(
        jnp.sum(pattern_wide, axis=2)[:, None, :], (KINDS, PER_KIND, TILE)
    ).reshape(-1, TILE)
    col_block = jnp.broadcast_to(
        jnp.sum(pattern_wide, axis=1)[:, None, :], (KINDS, PER_KIND, TILE)
    ).reshape(-1, TILE)
    row_part = jax.ops.segment_sum(row_block, ray_list, ray_total)
    col_part = jax.ops.segment_sum(col_block, pixel_list, tiles_dev)
    measured = sinogram[0]
    col_weight = lax.psum(col_part, "ang")
    current = volume
    scaled = measured
    for iteration in range(ITERS):
        low_volume = current.astype(jnp.bfloat16)
        partial_rows = project_local(low_volume, pattern, pixel_list, ray_list, ray_total)
        if iteration == 0:
            summed, row_weight = (
                lax.psum_scatter(partial_rows, "pix", scatter_dimension=0, tiled=True),
                lax.psum_scatter(row_part, "pix", scatter_dimension=0, tiled=True),
            )
        else:
            summed = lax.psum_scatter(partial_rows, "pix", scatter_dimension=0, tiled=True)
        scaled = (measured - summed) / jnp.tile(row_weight, (1, slices))
        scaled_low = scaled.astype(jnp.bfloat16)
        row_table = lax.all_gather(scaled_low, "pix", axis=0, tiled=True)
        back_sum = back_local(row_table, pattern, pixel_list, ray_list, tiles_dev)
        summed_update = lax.psum(back_sum, "ang")
        current = current + summed_update / jnp.tile(col_weight, (1, slices))
    return (current, scaled[None])


def split2(x):
    hi = lax.reduce_precision(x, exponent_bits=8, mantissa_bits=7)
    return (hi.astype(jnp.bfloat16), (x - hi).astype(jnp.bfloat16))


def per_device_split(volume, sinogram, table, blk_ray, blk_pix, n_pix, n_ang):
    n_grp = n_pix * n_ang
    tiles_dev = volume.shape[0]
    slices = volume.shape[1] // TILE
    per_dev = slices // n_grp
    rays_dev = sinogram.shape[1]
    nbd = blk_ray.shape[-1]
    ray_total = rays_dev * n_pix
    pix_total = tiles_dev * n_pix
    width = per_dev * TILE

    vol_send = volume.reshape(tiles_dev, n_grp, width).transpose(1, 0, 2)
    sino_send = sinogram[0].reshape(rays_dev, n_grp, width).transpose(1, 0, 2)
    cells = (blk_ray.reshape(-1) * tiles_dev + blk_pix.reshape(-1)).astype(jnp.float32)
    list_rows = (nbd + width - 1) // width
    lists = jnp.pad(cells, (0, list_rows * width - nbd)).reshape(list_rows, width)
    list_send = jnp.broadcast_to(lists[None], (n_grp, list_rows, width))
    rows = tiles_dev + rays_dev + list_rows
    paired = rows + rows % 2
    if tiles_dev % 2 == 0 and rays_dev % 2 == 0 and nbd % (2 * width) == 0:
        send = jnp.concatenate(
            [
                vol_send.reshape(n_grp, tiles_dev // 2, 2 * width),
                sino_send.reshape(n_grp, rays_dev // 2, 2 * width),
                jnp.broadcast_to(cells.reshape(1, list_rows // 2, 2 * width), (n_grp, list_rows // 2, 2 * width)),
            ],
            axis=1,
        )
    else:
        send = jnp.concatenate([vol_send, sino_send, list_send], axis=1)
        send = jnp.pad(send, ((0, 0), (0, paired - rows), (0, 0))).reshape(n_grp, paired // 2, 2 * width)
    recv = lax.all_to_all(send, ("pix", "ang"), 0, 0, tiled=False)
    recv = recv.reshape(n_pix, n_ang, paired, width)[:, :, :rows]

    current = recv[:, 0, :tiles_dev].reshape(pix_total, width)
    measured = recv[:, :, tiles_dev:tiles_dev + rays_dev].transpose(1, 0, 2, 3).reshape(n_ang, ray_total, width)
    cells = recv[:, :, tiles_dev + rays_dev:].reshape(n_pix, n_ang, -1)[:, :, :nbd]
    cells = cells.transpose(1, 0, 2).astype(jnp.int32)
    got = jnp.stack([cells // tiles_dev, cells % tiles_dev])
    per_kind = nbd // KINDS
    offsets = (jnp.arange(n_pix, dtype=jnp.int32) * tiles_dev)[None, :, None, None]
    ray_ids = got[0].reshape(n_ang, n_pix, KINDS, per_kind)
    pix_ids = got[1].reshape(n_ang, n_pix, KINDS, per_kind) + offsets
    ray_ids = ray_ids.transpose(0, 2, 1, 3).reshape(n_ang, KINDS, n_pix * per_kind)
    pix_ids = pix_ids.transpose(0, 2, 1, 3).reshape(n_ang, KINDS, n_pix * per_kind)

    one_ray = (ray_ids[..., None] == jnp.arange(ray_total, dtype=jnp.int32)).astype(jnp.bfloat16)
    one_pix = (pix_ids[..., None] == jnp.arange(pix_total, dtype=jnp.int32)).astype(jnp.bfloat16)
    count_low = jnp.einsum(
        "gkbv,gkbu->gkvu", one_ray, one_pix, preferred_element_type=jnp.float32
    ).astype(jnp.bfloat16)
    count_low = lax.optimization_barrier(count_low)
    counts = count_low.astype(jnp.float32)
    ray_count = jnp.sum(counts, axis=3)
    pix_count = jnp.sum(counts, axis=2)

    pattern = table.reshape(KINDS, TILE, TILE)
    pattern_wide = pattern.astype(jnp.float32)
    hi = lax.Precision.HIGHEST
    ray_weight = jnp.einsum("gkv,ki->gvi", ray_count, jnp.sum(pattern_wide, axis=2), precision=hi)
    pixel_weight = jnp.einsum("gku,kj->uj", pix_count, jnp.sum(pattern_wide, axis=1), precision=hi)
    ray_weight = jnp.tile(ray_weight, (1, 1, per_dev))
    pixel_weight = jnp.tile(pixel_weight, (1, per_dev))

    cur = current.reshape(pix_total, per_dev, TILE)
    meas = measured.reshape(n_ang, ray_total, per_dev, TILE)
    rw = ray_weight.reshape(n_ang, ray_total, per_dev, TILE)
    pw = pixel_weight.reshape(pix_total, per_dev, TILE)
    scaled = meas
    for iteration in range(ITERS):
        low = cur.astype(jnp.bfloat16)
        gathered = jnp.einsum("gkvu,usj->gkvsj", count_low, low, preferred_element_type=jnp.float32)
        proj = jnp.einsum(
            "gkvsj,kij->gvsi", gathered, pattern_wide, precision=lax.Precision.HIGHEST,
            preferred_element_type=jnp.float32,
        )
        scaled = (meas - proj) / rw
        scaled_low = scaled.astype(jnp.bfloat16)
        spread = jnp.einsum("gvsi,kij->gkvsj", scaled_low, pattern, preferred_element_type=jnp.float32)
        update = jnp.einsum(
            "gkvu,gkvsj->usj", counts, spread, precision=lax.Precision.HIGH,
            preferred_element_type=jnp.float32,
        )
        cur = cur + update / pw

    vol_back = cur.reshape(n_pix, tiles_dev, width)
    vol_back = jnp.broadcast_to(vol_back[:, None], (n_pix, n_ang, tiles_dev, width))
    res_back = scaled.reshape(n_ang, n_pix, rays_dev, width).transpose(1, 0, 2, 3)
    back = jnp.concatenate([vol_back, res_back], axis=2).reshape(n_grp, tiles_dev + rays_dev, width)
    rows_back = tiles_dev + rays_dev
    paired_back = rows_back + rows_back % 2
    back = jnp.pad(back, ((0, 0), (0, paired_back - rows_back), (0, 0)))
    back = back.reshape(n_grp, paired_back // 2, 2 * width)
    got_back = lax.all_to_all(back, ("pix", "ang"), 0, 0, tiled=False)
    got_back = got_back.reshape(n_grp, paired_back, width)[:, :rows_back]
    both = got_back.transpose(1, 0, 2).reshape(rows_back, slices * TILE)
    vol_out = both[:tiles_dev]
    res_out = both[tiles_dev:].reshape(1, rays_dev, slices * TILE)
    return (vol_out, res_out)


def solution(mesh):
    n_pix = mesh.shape["pix"]
    n_ang = mesh.shape["ang"]

    def body(volume, sinogram, table, blk_ray, blk_pix):
        if (volume.shape[1] // TILE) % (n_pix * n_ang) == 0:
            return per_device_split(volume, sinogram, table, blk_ray, blk_pix, n_pix, n_ang)
        return per_device_base(volume, sinogram, table, blk_ray, blk_pix)

    return jax.shard_map(
        body,
        mesh=mesh,
        in_specs=(
            P(("parts", "pix"), "sl"),
            P(("parts", "ang"), "pix", "sl"),
            P(),
            P("ang", "pix", None),
            P("ang", "pix", None),
        ),
        out_specs=(P(("parts", "pix"), "sl"), P(("parts", "ang"), "pix", "sl")),
        check_vma=False,
    )
```

```python
import jax
import jax.numpy as jnp
from jax import lax
from jax.sharding import PartitionSpec as P

TILE = 64
KINDS = 32
ITERS = 2
PER_KIND = 44


def project_local(low_volume, pattern, pixel_list, ray_list, ray_total):
    tiles_dev = low_volume.shape[0]
    slices = low_volume.shape[1] // TILE
    low_tiles = low_volume.reshape(tiles_dev, slices, TILE)
    kinds_each = KINDS // 4

    def project_one_group(running, inputs):
        patterns, pix_ids, ray_ids = inputs
        picked = jnp.take(low_tiles, pix_ids, axis=0).reshape(kinds_each, PER_KIND, slices, TILE)
        images = jnp.einsum("kbsj,kij->kbsi", picked, patterns, preferred_element_type=jnp.float32)
        images = images.reshape(kinds_each * PER_KIND, slices * TILE)
        return (running + jax.ops.segment_sum(images, ray_ids, ray_total), None)

    inputs = (
        pattern.reshape(4, kinds_each, TILE, TILE),
        pixel_list.reshape(4, -1),
        ray_list.reshape(4, -1),
    )
    initial = jnp.zeros((ray_total, slices * TILE), jnp.float32)
    running, unused = lax.scan(project_one_group, initial, inputs)
    return running


def back_local(row_table, pattern, pixel_list, row_index, tiles_dev):
    slices = row_table.shape[1] // TILE
    table_tiles = row_table.reshape(row_table.shape[0], slices, TILE)
    kinds_each = KINDS // 4

    def back_one_group(running, inputs):
        patterns, pix_ids, row_ids = inputs
        picked = jnp.take(table_tiles, row_ids, axis=0).reshape(kinds_each, PER_KIND, slices, TILE)
        images = jnp.einsum("kbsi,kij->kbsj", picked, patterns, preferred_element_type=jnp.float32)
        images = images.reshape(kinds_each * PER_KIND, slices * TILE)
        return (running + jax.ops.segment_sum(images, pix_ids, tiles_dev), None)

    inputs = (
        pattern.reshape(4, kinds_each, TILE, TILE),
        pixel_list.reshape(4, -1),
        row_index.reshape(4, -1),
    )
    initial = jnp.zeros((tiles_dev, slices * TILE), jnp.float32)
    running, unused = lax.scan(back_one_group, initial, inputs)
    return running


def per_device_base(volume, sinogram, table, blk_ray, blk_pix):
    pix_count = lax.axis_size("pix")
    tiles_dev = volume.shape[0]
    row_width = volume.shape[1]
    slices = row_width // TILE
    rays_dev = sinogram.shape[1]
    ray_total = rays_dev * pix_count
    ray_list = blk_ray.reshape(-1)
    pixel_list = blk_pix.reshape(-1)
    pattern = table.reshape(KINDS, TILE, TILE)
    pattern_wide = table.astype(jnp.float32).reshape(KINDS, TILE, TILE)
    row_block = jnp.broadcast_to(
        jnp.sum(pattern_wide, axis=2)[:, None, :], (KINDS, PER_KIND, TILE)
    ).reshape(-1, TILE)
    col_block = jnp.broadcast_to(
        jnp.sum(pattern_wide, axis=1)[:, None, :], (KINDS, PER_KIND, TILE)
    ).reshape(-1, TILE)
    row_part = jax.ops.segment_sum(row_block, ray_list, ray_total)
    col_part = jax.ops.segment_sum(col_block, pixel_list, tiles_dev)
    measured = sinogram[0]
    col_weight = lax.psum(col_part, "ang")
    current = volume
    scaled = measured
    for iteration in range(ITERS):
        low_volume = current.astype(jnp.bfloat16)
        partial_rows = project_local(low_volume, pattern, pixel_list, ray_list, ray_total)
        if iteration == 0:
            summed, row_weight = (
                lax.psum_scatter(partial_rows, "pix", scatter_dimension=0, tiled=True),
                lax.psum_scatter(row_part, "pix", scatter_dimension=0, tiled=True),
            )
        else:
            summed = lax.psum_scatter(partial_rows, "pix", scatter_dimension=0, tiled=True)
        scaled = (measured - summed) / jnp.tile(row_weight, (1, slices))
        scaled_low = scaled.astype(jnp.bfloat16)
        row_table = lax.all_gather(scaled_low, "pix", axis=0, tiled=True)
        back_sum = back_local(row_table, pattern, pixel_list, ray_list, tiles_dev)
        summed_update = lax.psum(back_sum, "ang")
        current = current + summed_update / jnp.tile(col_weight, (1, slices))
    return (current, scaled[None])


def split2(x):
    hi = lax.reduce_precision(x, exponent_bits=8, mantissa_bits=7)
    return (hi.astype(jnp.bfloat16), (x - hi).astype(jnp.bfloat16))


def per_device_split(volume, sinogram, table, blk_ray, blk_pix, n_pix, n_ang):
    n_grp = n_pix * n_ang
    tiles_dev = volume.shape[0]
    slices = volume.shape[1] // TILE
    per_dev = slices // n_grp
    rays_dev = sinogram.shape[1]
    nbd = blk_ray.shape[-1]
    ray_total = rays_dev * n_pix
    pix_total = tiles_dev * n_pix
    width = per_dev * TILE

    vol_send = volume.reshape(tiles_dev, n_grp, width).transpose(1, 0, 2)
    sino_send = sinogram[0].reshape(rays_dev, n_grp, width).transpose(1, 0, 2)
    cells = (blk_ray.reshape(-1) * tiles_dev + blk_pix.reshape(-1)).astype(jnp.float32)
    list_rows = (nbd + width - 1) // width
    lists = jnp.pad(cells, (0, list_rows * width - nbd)).reshape(list_rows, width)
    list_send = jnp.broadcast_to(lists[None], (n_grp, list_rows, width))
    rows = tiles_dev + rays_dev + list_rows
    paired = rows + rows % 2
    if tiles_dev % 2 == 0 and rays_dev % 2 == 0 and nbd % (2 * width) == 0:
        joined = jnp.concatenate([volume, sinogram[0]], axis=0)
        joined = joined.reshape(tiles_dev + rays_dev, n_grp, width).transpose(1, 0, 2)
        send = jnp.concatenate(
            [
                joined.reshape(n_grp, (tiles_dev + rays_dev) // 2, 2 * width),
                jnp.broadcast_to(cells.reshape(1, list_rows // 2, 2 * width), (n_grp, list_rows // 2, 2 * width)),
            ],
            axis=1,
        )
    else:
        send = jnp.concatenate([vol_send, sino_send, list_send], axis=1)
        send = jnp.pad(send, ((0, 0), (0, paired - rows), (0, 0))).reshape(n_grp, paired // 2, 2 * width)
    recv = lax.all_to_all(send, ("pix", "ang"), 0, 0, tiled=False)
    recv = recv.reshape(n_pix, n_ang, paired, width)[:, :, :rows]

    current = recv[:, 0, :tiles_dev].reshape(pix_total, width)
    measured = recv[:, :, tiles_dev:tiles_dev + rays_dev].transpose(1, 0, 2, 3).reshape(n_ang, ray_total, width)
    cells = recv[:, :, tiles_dev + rays_dev:].reshape(n_pix, n_ang, -1)[:, :, :nbd]
    cells = cells.transpose(1, 0, 2).astype(jnp.int32)
    got = jnp.stack([cells // tiles_dev, cells % tiles_dev])
    per_kind = nbd // KINDS
    offsets = (jnp.arange(n_pix, dtype=jnp.int32) * tiles_dev)[None, :, None, None]
    ray_ids = got[0].reshape(n_ang, n_pix, KINDS, per_kind)
    pix_ids = got[1].reshape(n_ang, n_pix, KINDS, per_kind) + offsets
    ray_ids = ray_ids.transpose(0, 2, 1, 3).reshape(n_ang, KINDS, n_pix * per_kind)
    pix_ids = pix_ids.transpose(0, 2, 1, 3).reshape(n_ang, KINDS, n_pix * per_kind)

    one_ray = (ray_ids[..., None] == jnp.arange(ray_total, dtype=jnp.int32)).astype(jnp.bfloat16)
    one_pix = (pix_ids[..., None] == jnp.arange(pix_total, dtype=jnp.int32)).astype(jnp.bfloat16)
    count_low = jnp.einsum(
        "gkbv,gkbu->gkvu", one_ray, one_pix, preferred_element_type=jnp.float32
    ).astype(jnp.bfloat16)
    count_low = lax.optimization_barrier(count_low)
    counts = count_low.astype(jnp.float32)
    ray_count = jnp.sum(counts, axis=3)
    pix_count = jnp.sum(counts, axis=2)

    pattern = table.reshape(KINDS, TILE, TILE)
    pattern_wide = pattern.astype(jnp.float32)
    hi = lax.Precision.HIGHEST
    ray_weight = jnp.einsum("gkv,ki->gvi", ray_count, jnp.sum(pattern_wide, axis=2), precision=hi)
    pixel_weight = jnp.einsum("gku,kj->uj", pix_count, jnp.sum(pattern_wide, axis=1), precision=hi)
    ray_weight = jnp.tile(ray_weight, (1, 1, per_dev))
    pixel_weight = jnp.tile(pixel_weight, (1, per_dev))

    cur = current.reshape(pix_total, per_dev, TILE)
    meas = measured.reshape(n_ang, ray_total, per_dev, TILE)
    rw = ray_weight.reshape(n_ang, ray_total, per_dev, TILE)
    pw = pixel_weight.reshape(pix_total, per_dev, TILE)
    scaled = meas
    for iteration in range(ITERS):
        low = cur.astype(jnp.bfloat16)
        gathered = jnp.einsum("gkvu,usj->gkvsj", count_low, low, preferred_element_type=jnp.float32)
        proj = jnp.einsum(
            "gkvsj,kij->gvsi", gathered, pattern_wide, precision=lax.Precision.HIGHEST,
            preferred_element_type=jnp.float32,
        )
        scaled = (meas - proj) / rw
        scaled_low = scaled.astype(jnp.bfloat16)
        spread = jnp.einsum("gvsi,kij->gkvsj", scaled_low, pattern, preferred_element_type=jnp.float32)
        update = jnp.einsum(
            "gkvu,gkvsj->usj", counts, spread, precision=lax.Precision.HIGH,
            preferred_element_type=jnp.float32,
        )
        cur = cur + update / pw

    vol_back = cur.reshape(n_pix, tiles_dev, width)
    vol_back = jnp.broadcast_to(vol_back[:, None], (n_pix, n_ang, tiles_dev, width))
    res_back = scaled.reshape(n_ang, n_pix, rays_dev, width).transpose(1, 0, 2, 3)
    back = jnp.concatenate([vol_back, res_back], axis=2).reshape(n_grp, tiles_dev + rays_dev, width)
    rows_back = tiles_dev + rays_dev
    paired_back = rows_back + rows_back % 2
    back = jnp.pad(back, ((0, 0), (0, paired_back - rows_back), (0, 0)))
    back = back.reshape(n_grp, paired_back // 2, 2 * width)
    got_back = lax.all_to_all(back, ("pix", "ang"), 0, 0, tiled=False)
    got_back = got_back.reshape(n_grp, paired_back, width)[:, :rows_back]
    both = got_back.transpose(1, 0, 2).reshape(rows_back, slices * TILE)
    vol_out = both[:tiles_dev]
    res_out = both[tiles_dev:].reshape(1, rays_dev, slices * TILE)
    return (vol_out, res_out)


def solution(mesh):
    n_pix = mesh.shape["pix"]
    n_ang = mesh.shape["ang"]

    def body(volume, sinogram, table, blk_ray, blk_pix):
        if (volume.shape[1] // TILE) % (n_pix * n_ang) == 0:
            return per_device_split(volume, sinogram, table, blk_ray, blk_pix, n_pix, n_ang)
        return per_device_base(volume, sinogram, table, blk_ray, blk_pix)

    return jax.shard_map(
        body,
        mesh=mesh,
        in_specs=(
            P(("parts", "pix"), "sl"),
            P(("parts", "ang"), "pix", "sl"),
            P(),
            P("ang", "pix", None),
            P("ang", "pix", None),
        ),
        out_specs=(P(("parts", "pix"), "sl"), P(("parts", "ang"), "pix", "sl")),
        check_vma=False,
    )
```

```python
import jax
import jax.numpy as jnp
from jax import lax
from jax.sharding import PartitionSpec as P

TILE = 64
KINDS = 32
ITERS = 2
PER_KIND = 44


def project_local(low_volume, pattern, pixel_list, ray_list, ray_total):
    tiles_dev = low_volume.shape[0]
    slices = low_volume.shape[1] // TILE
    low_tiles = low_volume.reshape(tiles_dev, slices, TILE)
    kinds_each = KINDS // 4

    def project_one_group(running, inputs):
        patterns, pix_ids, ray_ids = inputs
        picked = jnp.take(low_tiles, pix_ids, axis=0).reshape(kinds_each, PER_KIND, slices, TILE)
        images = jnp.einsum("kbsj,kij->kbsi", picked, patterns, preferred_element_type=jnp.float32)
        images = images.reshape(kinds_each * PER_KIND, slices * TILE)
        return (running + jax.ops.segment_sum(images, ray_ids, ray_total), None)

    inputs = (
        pattern.reshape(4, kinds_each, TILE, TILE),
        pixel_list.reshape(4, -1),
        ray_list.reshape(4, -1),
    )
    initial = jnp.zeros((ray_total, slices * TILE), jnp.float32)
    running, unused = lax.scan(project_one_group, initial, inputs)
    return running


def back_local(row_table, pattern, pixel_list, row_index, tiles_dev):
    slices = row_table.shape[1] // TILE
    table_tiles = row_table.reshape(row_table.shape[0], slices, TILE)
    kinds_each = KINDS // 4

    def back_one_group(running, inputs):
        patterns, pix_ids, row_ids = inputs
        picked = jnp.take(table_tiles, row_ids, axis=0).reshape(kinds_each, PER_KIND, slices, TILE)
        images = jnp.einsum("kbsi,kij->kbsj", picked, patterns, preferred_element_type=jnp.float32)
        images = images.reshape(kinds_each * PER_KIND, slices * TILE)
        return (running + jax.ops.segment_sum(images, pix_ids, tiles_dev), None)

    inputs = (
        pattern.reshape(4, kinds_each, TILE, TILE),
        pixel_list.reshape(4, -1),
        row_index.reshape(4, -1),
    )
    initial = jnp.zeros((tiles_dev, slices * TILE), jnp.float32)
    running, unused = lax.scan(back_one_group, initial, inputs)
    return running


def per_device_base(volume, sinogram, table, blk_ray, blk_pix):
    pix_count = lax.axis_size("pix")
    tiles_dev = volume.shape[0]
    row_width = volume.shape[1]
    slices = row_width // TILE
    rays_dev = sinogram.shape[1]
    ray_total = rays_dev * pix_count
    ray_list = blk_ray.reshape(-1)
    pixel_list = blk_pix.reshape(-1)
    pattern = table.reshape(KINDS, TILE, TILE)
    pattern_wide = table.astype(jnp.float32).reshape(KINDS, TILE, TILE)
    row_block = jnp.broadcast_to(
        jnp.sum(pattern_wide, axis=2)[:, None, :], (KINDS, PER_KIND, TILE)
    ).reshape(-1, TILE)
    col_block = jnp.broadcast_to(
        jnp.sum(pattern_wide, axis=1)[:, None, :], (KINDS, PER_KIND, TILE)
    ).reshape(-1, TILE)
    row_part = jax.ops.segment_sum(row_block, ray_list, ray_total)
    col_part = jax.ops.segment_sum(col_block, pixel_list, tiles_dev)
    measured = sinogram[0]
    col_weight = lax.psum(col_part, "ang")
    current = volume
    scaled = measured
    for iteration in range(ITERS):
        low_volume = current.astype(jnp.bfloat16)
        partial_rows = project_local(low_volume, pattern, pixel_list, ray_list, ray_total)
        if iteration == 0:
            summed, row_weight = (
                lax.psum_scatter(partial_rows, "pix", scatter_dimension=0, tiled=True),
                lax.psum_scatter(row_part, "pix", scatter_dimension=0, tiled=True),
            )
        else:
            summed = lax.psum_scatter(partial_rows, "pix", scatter_dimension=0, tiled=True)
        scaled = (measured - summed) / jnp.tile(row_weight, (1, slices))
        scaled_low = scaled.astype(jnp.bfloat16)
        row_table = lax.all_gather(scaled_low, "pix", axis=0, tiled=True)
        back_sum = back_local(row_table, pattern, pixel_list, ray_list, tiles_dev)
        summed_update = lax.psum(back_sum, "ang")
        current = current + summed_update / jnp.tile(col_weight, (1, slices))
    return (current, scaled[None])


def split2(x):
    hi = lax.reduce_precision(x, exponent_bits=8, mantissa_bits=7)
    return (hi.astype(jnp.bfloat16), (x - hi).astype(jnp.bfloat16))


def per_device_split(volume, sinogram, table, blk_ray, blk_pix, n_pix, n_ang):
    n_grp = n_pix * n_ang
    tiles_dev = volume.shape[0]
    slices = volume.shape[1] // TILE
    per_dev = slices // n_grp
    rays_dev = sinogram.shape[1]
    nbd = blk_ray.shape[-1]
    ray_total = rays_dev * n_pix
    pix_total = tiles_dev * n_pix
    width = per_dev * TILE

    vol_send = volume.reshape(tiles_dev, n_grp, width).transpose(1, 0, 2)
    sino_send = sinogram[0].reshape(rays_dev, n_grp, width).transpose(1, 0, 2)
    cells = (blk_ray.reshape(-1) * tiles_dev + blk_pix.reshape(-1)).astype(jnp.float32)
    list_rows = (nbd + width - 1) // width
    lists = jnp.pad(cells, (0, list_rows * width - nbd)).reshape(list_rows, width)
    list_send = jnp.broadcast_to(lists[None], (n_grp, list_rows, width))
    rows = tiles_dev + rays_dev + list_rows
    paired = rows + rows % 2
    if tiles_dev % 2 == 0 and rays_dev % 2 == 0 and nbd % (2 * width) == 0:
        send = jnp.concatenate(
            [
                vol_send.reshape(n_grp, tiles_dev // 2, 2 * width),
                sino_send.reshape(n_grp, rays_dev // 2, 2 * width),
                jnp.broadcast_to(cells.reshape(1, list_rows // 2, 2 * width), (n_grp, list_rows // 2, 2 * width)),
            ],
            axis=1,
        )
    else:
        send = jnp.concatenate([vol_send, sino_send, list_send], axis=1)
        send = jnp.pad(send, ((0, 0), (0, paired - rows), (0, 0))).reshape(n_grp, paired // 2, 2 * width)
    recv = lax.all_to_all(send, ("pix", "ang"), 0, 0, tiled=False)
    recv = recv.reshape(n_pix, n_ang, paired, width)[:, :, :rows]

    current = recv[:, 0, :tiles_dev].reshape(pix_total, width)
    measured = recv[:, :, tiles_dev:tiles_dev + rays_dev].transpose(1, 0, 2, 3).reshape(n_ang, ray_total, width)
    cells = recv[:, :, tiles_dev + rays_dev:].reshape(n_pix, n_ang, -1)[:, :, :nbd]
    cells = cells.transpose(1, 0, 2)
    ray_of = jnp.floor(cells / tiles_dev)
    got = jnp.stack([ray_of, cells - ray_of * tiles_dev])
    per_kind = nbd // KINDS
    offsets = (jnp.arange(n_pix, dtype=jnp.float32) * tiles_dev)[None, :, None, None]
    ray_ids = got[0].reshape(n_ang, n_pix, KINDS, per_kind)
    pix_ids = got[1].reshape(n_ang, n_pix, KINDS, per_kind) + offsets
    ray_ids = ray_ids.transpose(0, 2, 1, 3).reshape(n_ang, KINDS, n_pix * per_kind)
    pix_ids = pix_ids.transpose(0, 2, 1, 3).reshape(n_ang, KINDS, n_pix * per_kind)

    one_ray = (ray_ids[..., None] == jnp.arange(ray_total, dtype=jnp.float32)).astype(jnp.bfloat16)
    one_pix = (pix_ids[..., None] == jnp.arange(pix_total, dtype=jnp.float32)).astype(jnp.bfloat16)
    count_low = jnp.einsum(
        "gkbv,gkbu->gkvu", one_ray, one_pix, preferred_element_type=jnp.float32
    ).astype(jnp.bfloat16)
    count_low = lax.optimization_barrier(count_low)
    counts = count_low.astype(jnp.float32)
    ray_count = jnp.sum(counts, axis=3)
    pix_count = jnp.sum(counts, axis=2)

    pattern = table.reshape(KINDS, TILE, TILE)
    pattern_wide = pattern.astype(jnp.float32)
    hi = lax.Precision.HIGHEST
    ray_weight = jnp.einsum("gkv,ki->gvi", ray_count, jnp.sum(pattern_wide, axis=2), precision=hi)
    pixel_weight = jnp.einsum("gku,kj->uj", pix_count, jnp.sum(pattern_wide, axis=1), precision=hi)
    ray_weight = jnp.tile(ray_weight, (1, 1, per_dev))
    pixel_weight = jnp.tile(pixel_weight, (1, per_dev))

    cur = current.reshape(pix_total, per_dev, TILE)
    meas = measured.reshape(n_ang, ray_total, per_dev, TILE)
    rw = ray_weight.reshape(n_ang, ray_total, per_dev, TILE)
    pw = pixel_weight.reshape(pix_total, per_dev, TILE)
    scaled = meas
    for iteration in range(ITERS):
        low = cur.astype(jnp.bfloat16)
        gathered = jnp.einsum("gkvu,usj->gkvsj", count_low, low, preferred_element_type=jnp.float32)
        proj = jnp.einsum(
            "gkvsj,kij->gvsi", gathered, pattern_wide, precision=lax.Precision.HIGHEST,
            preferred_element_type=jnp.float32,
        )
        scaled = (meas - proj) / rw
        scaled_low = scaled.astype(jnp.bfloat16)
        spread = jnp.einsum("gvsi,kij->gkvsj", scaled_low, pattern, preferred_element_type=jnp.float32)
        update = jnp.einsum(
            "gkvu,gkvsj->usj", counts, spread, precision=lax.Precision.HIGH,
            preferred_element_type=jnp.float32,
        )
        cur = cur + update / pw

    vol_back = cur.reshape(n_pix, tiles_dev, width)
    vol_back = jnp.broadcast_to(vol_back[:, None], (n_pix, n_ang, tiles_dev, width))
    res_back = scaled.reshape(n_ang, n_pix, rays_dev, width).transpose(1, 0, 2, 3)
    back = jnp.concatenate([vol_back, res_back], axis=2).reshape(n_grp, tiles_dev + rays_dev, width)
    rows_back = tiles_dev + rays_dev
    paired_back = rows_back + rows_back % 2
    back = jnp.pad(back, ((0, 0), (0, paired_back - rows_back), (0, 0)))
    back = back.reshape(n_grp, paired_back // 2, 2 * width)
    got_back = lax.all_to_all(back, ("pix", "ang"), 0, 0, tiled=False)
    got_back = got_back.reshape(n_grp, paired_back, width)[:, :rows_back]
    both = got_back.transpose(1, 0, 2).reshape(rows_back, slices * TILE)
    vol_out = both[:tiles_dev]
    res_out = both[tiles_dev:].reshape(1, rays_dev, slices * TILE)
    return (vol_out, res_out)


def solution(mesh):
    n_pix = mesh.shape["pix"]
    n_ang = mesh.shape["ang"]

    def body(volume, sinogram, table, blk_ray, blk_pix):
        if (volume.shape[1] // TILE) % (n_pix * n_ang) == 0:
            return per_device_split(volume, sinogram, table, blk_ray, blk_pix, n_pix, n_ang)
        return per_device_base(volume, sinogram, table, blk_ray, blk_pix)

    return jax.shard_map(
        body,
        mesh=mesh,
        in_specs=(
            P(("parts", "pix"), "sl"),
            P(("parts", "ang"), "pix", "sl"),
            P(),
            P("ang", "pix", None),
            P("ang", "pix", None),
        ),
        out_specs=(P(("parts", "pix"), "sl"), P(("parts", "ang"), "pix", "sl")),
        check_vma=False,
    )
```

```python
import jax
import jax.numpy as jnp
from jax import lax
from jax.sharding import PartitionSpec as P

TILE = 64
KINDS = 32
ITERS = 2
PER_KIND = 44


def project_local(low_volume, pattern, pixel_list, ray_list, ray_total):
    tiles_dev = low_volume.shape[0]
    slices = low_volume.shape[1] // TILE
    low_tiles = low_volume.reshape(tiles_dev, slices, TILE)
    kinds_each = KINDS // 4

    def project_one_group(running, inputs):
        patterns, pix_ids, ray_ids = inputs
        picked = jnp.take(low_tiles, pix_ids, axis=0).reshape(kinds_each, PER_KIND, slices, TILE)
        images = jnp.einsum("kbsj,kij->kbsi", picked, patterns, preferred_element_type=jnp.float32)
        images = images.reshape(kinds_each * PER_KIND, slices * TILE)
        return (running + jax.ops.segment_sum(images, ray_ids, ray_total), None)

    inputs = (
        pattern.reshape(4, kinds_each, TILE, TILE),
        pixel_list.reshape(4, -1),
        ray_list.reshape(4, -1),
    )
    initial = jnp.zeros((ray_total, slices * TILE), jnp.float32)
    running, unused = lax.scan(project_one_group, initial, inputs)
    return running


def back_local(row_table, pattern, pixel_list, row_index, tiles_dev):
    slices = row_table.shape[1] // TILE
    table_tiles = row_table.reshape(row_table.shape[0], slices, TILE)
    kinds_each = KINDS // 4

    def back_one_group(running, inputs):
        patterns, pix_ids, row_ids = inputs
        picked = jnp.take(table_tiles, row_ids, axis=0).reshape(kinds_each, PER_KIND, slices, TILE)
        images = jnp.einsum("kbsi,kij->kbsj", picked, patterns, preferred_element_type=jnp.float32)
        images = images.reshape(kinds_each * PER_KIND, slices * TILE)
        return (running + jax.ops.segment_sum(images, pix_ids, tiles_dev), None)

    inputs = (
        pattern.reshape(4, kinds_each, TILE, TILE),
        pixel_list.reshape(4, -1),
        row_index.reshape(4, -1),
    )
    initial = jnp.zeros((tiles_dev, slices * TILE), jnp.float32)
    running, unused = lax.scan(back_one_group, initial, inputs)
    return running


def per_device_base(volume, sinogram, table, blk_ray, blk_pix):
    pix_count = lax.axis_size("pix")
    tiles_dev = volume.shape[0]
    row_width = volume.shape[1]
    slices = row_width // TILE
    rays_dev = sinogram.shape[1]
    ray_total = rays_dev * pix_count
    ray_list = blk_ray.reshape(-1)
    pixel_list = blk_pix.reshape(-1)
    pattern = table.reshape(KINDS, TILE, TILE)
    pattern_wide = table.astype(jnp.float32).reshape(KINDS, TILE, TILE)
    row_block = jnp.broadcast_to(
        jnp.sum(pattern_wide, axis=2)[:, None, :], (KINDS, PER_KIND, TILE)
    ).reshape(-1, TILE)
    col_block = jnp.broadcast_to(
        jnp.sum(pattern_wide, axis=1)[:, None, :], (KINDS, PER_KIND, TILE)
    ).reshape(-1, TILE)
    row_part = jax.ops.segment_sum(row_block, ray_list, ray_total)
    col_part = jax.ops.segment_sum(col_block, pixel_list, tiles_dev)
    measured = sinogram[0]
    col_weight = lax.psum(col_part, "ang")
    current = volume
    scaled = measured
    for iteration in range(ITERS):
        low_volume = current.astype(jnp.bfloat16)
        partial_rows = project_local(low_volume, pattern, pixel_list, ray_list, ray_total)
        if iteration == 0:
            summed, row_weight = (
                lax.psum_scatter(partial_rows, "pix", scatter_dimension=0, tiled=True),
                lax.psum_scatter(row_part, "pix", scatter_dimension=0, tiled=True),
            )
        else:
            summed = lax.psum_scatter(partial_rows, "pix", scatter_dimension=0, tiled=True)
        scaled = (measured - summed) / jnp.tile(row_weight, (1, slices))
        scaled_low = scaled.astype(jnp.bfloat16)
        row_table = lax.all_gather(scaled_low, "pix", axis=0, tiled=True)
        back_sum = back_local(row_table, pattern, pixel_list, ray_list, tiles_dev)
        summed_update = lax.psum(back_sum, "ang")
        current = current + summed_update / jnp.tile(col_weight, (1, slices))
    return (current, scaled[None])


def split2(x):
    hi = lax.reduce_precision(x, exponent_bits=8, mantissa_bits=7)
    return (hi.astype(jnp.bfloat16), (x - hi).astype(jnp.bfloat16))


def per_device_split(volume, sinogram, table, blk_ray, blk_pix, n_pix, n_ang):
    n_grp = n_pix * n_ang
    tiles_dev = volume.shape[0]
    slices = volume.shape[1] // TILE
    per_dev = slices // n_grp
    rays_dev = sinogram.shape[1]
    nbd = blk_ray.shape[-1]
    ray_total = rays_dev * n_pix
    pix_total = tiles_dev * n_pix
    width = per_dev * TILE

    vol_send = volume.reshape(tiles_dev, n_grp, width).transpose(1, 0, 2)
    sino_send = sinogram[0].reshape(rays_dev, n_grp, width).transpose(1, 0, 2)
    cells = (blk_ray.reshape(-1) * tiles_dev + blk_pix.reshape(-1)).astype(jnp.float32)
    list_rows = (nbd + width - 1) // width
    lists = jnp.pad(cells, (0, list_rows * width - nbd)).reshape(list_rows, width)
    list_send = jnp.broadcast_to(lists[None], (n_grp, list_rows, width))
    rows = tiles_dev + rays_dev + list_rows
    paired = rows + rows % 2
    if tiles_dev % 2 == 0 and rays_dev % 2 == 0 and nbd % (2 * width) == 0:
        cell_rows = (
            blk_ray.reshape(list_rows // 2, 2 * width).astype(jnp.float32) * tiles_dev
            + blk_pix.reshape(list_rows // 2, 2 * width).astype(jnp.float32)
        )
        send = jnp.concatenate(
            [
                vol_send.reshape(n_grp, tiles_dev // 2, 2 * width),
                sino_send.reshape(n_grp, rays_dev // 2, 2 * width),
                jnp.broadcast_to(cell_rows[None], (n_grp, list_rows // 2, 2 * width)),
            ],
            axis=1,
        )
    else:
        send = jnp.concatenate([vol_send, sino_send, list_send], axis=1)
        send = jnp.pad(send, ((0, 0), (0, paired - rows), (0, 0))).reshape(n_grp, paired // 2, 2 * width)
    recv = lax.all_to_all(send, ("pix", "ang"), 0, 0, tiled=False)
    recv = recv.reshape(n_pix, n_ang, paired, width)[:, :, :rows]

    current = recv[:, 0, :tiles_dev].reshape(pix_total, width)
    measured = recv[:, :, tiles_dev:tiles_dev + rays_dev].transpose(1, 0, 2, 3).reshape(n_ang, ray_total, width)
    cells = recv[:, :, tiles_dev + rays_dev:].reshape(n_pix, n_ang, -1)[:, :, :nbd]
    cells = cells.transpose(1, 0, 2)
    ray_of = jnp.floor(cells / tiles_dev)
    got = jnp.stack([ray_of, cells - ray_of * tiles_dev])
    per_kind = nbd // KINDS
    offsets = (jnp.arange(n_pix, dtype=jnp.float32) * tiles_dev)[None, :, None, None]
    ray_ids = got[0].reshape(n_ang, n_pix, KINDS, per_kind)
    pix_ids = got[1].reshape(n_ang, n_pix, KINDS, per_kind) + offsets
    ray_ids = ray_ids.transpose(0, 2, 1, 3).reshape(n_ang, KINDS, n_pix * per_kind)
    pix_ids = pix_ids.transpose(0, 2, 1, 3).reshape(n_ang, KINDS, n_pix * per_kind)

    one_ray = (ray_ids[..., None] == jnp.arange(ray_total, dtype=jnp.float32)).astype(jnp.bfloat16)
    one_pix = (pix_ids[..., None] == jnp.arange(pix_total, dtype=jnp.float32)).astype(jnp.bfloat16)
    count_low = jnp.einsum(
        "gkbv,gkbu->gkvu", one_ray, one_pix, preferred_element_type=jnp.float32
    ).astype(jnp.bfloat16)
    count_low = lax.optimization_barrier(count_low)
    counts = count_low.astype(jnp.float32)
    ray_count = jnp.sum(counts, axis=3)
    pix_count = jnp.sum(counts, axis=2)

    pattern = table.reshape(KINDS, TILE, TILE)
    pattern_wide = pattern.astype(jnp.float32)
    hi = lax.Precision.HIGHEST
    ray_weight = jnp.einsum("gkv,ki->gvi", ray_count, jnp.sum(pattern_wide, axis=2), precision=hi)
    pixel_weight = jnp.einsum("gku,kj->uj", pix_count, jnp.sum(pattern_wide, axis=1), precision=hi)
    ray_weight = jnp.tile(ray_weight, (1, 1, per_dev))
    pixel_weight = jnp.tile(pixel_weight, (1, per_dev))

    cur = current.reshape(pix_total, per_dev, TILE)
    meas = measured.reshape(n_ang, ray_total, per_dev, TILE)
    rw = ray_weight.reshape(n_ang, ray_total, per_dev, TILE)
    pw = pixel_weight.reshape(pix_total, per_dev, TILE)
    scaled = meas
    for iteration in range(ITERS):
        low = cur.astype(jnp.bfloat16)
        gathered = jnp.einsum("gkvu,usj->gkvsj", count_low, low, preferred_element_type=jnp.float32)
        proj = jnp.einsum(
            "gkvsj,kij->gvsi", gathered, pattern_wide, precision=lax.Precision.HIGHEST,
            preferred_element_type=jnp.float32,
        )
        scaled = (meas - proj) / rw
        scaled_low = scaled.astype(jnp.bfloat16)
        spread = jnp.einsum("gvsi,kij->gkvsj", scaled_low, pattern, preferred_element_type=jnp.float32)
        update = jnp.einsum(
            "gkvu,gkvsj->usj", counts, spread, precision=lax.Precision.HIGH,
            preferred_element_type=jnp.float32,
        )
        cur = cur + update / pw

    vol_back = cur.reshape(n_pix, tiles_dev, width)
    vol_back = jnp.broadcast_to(vol_back[:, None], (n_pix, n_ang, tiles_dev, width))
    res_back = scaled.reshape(n_ang, n_pix, rays_dev, width).transpose(1, 0, 2, 3)
    back = jnp.concatenate([vol_back, res_back], axis=2).reshape(n_grp, tiles_dev + rays_dev, width)
    rows_back = tiles_dev + rays_dev
    paired_back = rows_back + rows_back % 2
    back = jnp.pad(back, ((0, 0), (0, paired_back - rows_back), (0, 0)))
    back = back.reshape(n_grp, paired_back // 2, 2 * width)
    got_back = lax.all_to_all(back, ("pix", "ang"), 0, 0, tiled=False)
    got_back = got_back.reshape(n_grp, paired_back, width)[:, :rows_back]
    both = got_back.transpose(1, 0, 2).reshape(rows_back, slices * TILE)
    vol_out = both[:tiles_dev]
    res_out = both[tiles_dev:].reshape(1, rays_dev, slices * TILE)
    return (vol_out, res_out)


def solution(mesh):
    n_pix = mesh.shape["pix"]
    n_ang = mesh.shape["ang"]

    def body(volume, sinogram, table, blk_ray, blk_pix):
        if (volume.shape[1] // TILE) % (n_pix * n_ang) == 0:
            return per_device_split(volume, sinogram, table, blk_ray, blk_pix, n_pix, n_ang)
        return per_device_base(volume, sinogram, table, blk_ray, blk_pix)

    return jax.shard_map(
        body,
        mesh=mesh,
        in_specs=(
            P(("parts", "pix"), "sl"),
            P(("parts", "ang"), "pix", "sl"),
            P(),
            P("ang", "pix", None),
            P("ang", "pix", None),
        ),
        out_specs=(P(("parts", "pix"), "sl"), P(("parts", "ang"), "pix", "sl")),
        check_vma=False,
    )
```

```python
import jax
import jax.numpy as jnp
from jax import lax
from jax.sharding import PartitionSpec as P

TILE = 64
KINDS = 32
ITERS = 2
PER_KIND = 44


def project_local(low_volume, pattern, pixel_list, ray_list, ray_total):
    tiles_dev = low_volume.shape[0]
    slices = low_volume.shape[1] // TILE
    low_tiles = low_volume.reshape(tiles_dev, slices, TILE)
    kinds_each = KINDS // 4

    def project_one_group(running, inputs):
        patterns, pix_ids, ray_ids = inputs
        picked = jnp.take(low_tiles, pix_ids, axis=0).reshape(kinds_each, PER_KIND, slices, TILE)
        images = jnp.einsum("kbsj,kij->kbsi", picked, patterns, preferred_element_type=jnp.float32)
        images = images.reshape(kinds_each * PER_KIND, slices * TILE)
        return (running + jax.ops.segment_sum(images, ray_ids, ray_total), None)

    inputs = (
        pattern.reshape(4, kinds_each, TILE, TILE),
        pixel_list.reshape(4, -1),
        ray_list.reshape(4, -1),
    )
    initial = jnp.zeros((ray_total, slices * TILE), jnp.float32)
    running, unused = lax.scan(project_one_group, initial, inputs)
    return running


def back_local(row_table, pattern, pixel_list, row_index, tiles_dev):
    slices = row_table.shape[1] // TILE
    table_tiles = row_table.reshape(row_table.shape[0], slices, TILE)
    kinds_each = KINDS // 4

    def back_one_group(running, inputs):
        patterns, pix_ids, row_ids = inputs
        picked = jnp.take(table_tiles, row_ids, axis=0).reshape(kinds_each, PER_KIND, slices, TILE)
        images = jnp.einsum("kbsi,kij->kbsj", picked, patterns, preferred_element_type=jnp.float32)
        images = images.reshape(kinds_each * PER_KIND, slices * TILE)
        return (running + jax.ops.segment_sum(images, pix_ids, tiles_dev), None)

    inputs = (
        pattern.reshape(4, kinds_each, TILE, TILE),
        pixel_list.reshape(4, -1),
        row_index.reshape(4, -1),
    )
    initial = jnp.zeros((tiles_dev, slices * TILE), jnp.float32)
    running, unused = lax.scan(back_one_group, initial, inputs)
    return running


def per_device_base(volume, sinogram, table, blk_ray, blk_pix):
    pix_count = lax.axis_size("pix")
    tiles_dev = volume.shape[0]
    row_width = volume.shape[1]
    slices = row_width // TILE
    rays_dev = sinogram.shape[1]
    ray_total = rays_dev * pix_count
    ray_list = blk_ray.reshape(-1)
    pixel_list = blk_pix.reshape(-1)
    pattern = table.reshape(KINDS, TILE, TILE)
    pattern_wide = table.astype(jnp.float32).reshape(KINDS, TILE, TILE)
    row_block = jnp.broadcast_to(
        jnp.sum(pattern_wide, axis=2)[:, None, :], (KINDS, PER_KIND, TILE)
    ).reshape(-1, TILE)
    col_block = jnp.broadcast_to(
        jnp.sum(pattern_wide, axis=1)[:, None, :], (KINDS, PER_KIND, TILE)
    ).reshape(-1, TILE)
    row_part = jax.ops.segment_sum(row_block, ray_list, ray_total)
    col_part = jax.ops.segment_sum(col_block, pixel_list, tiles_dev)
    measured = sinogram[0]
    col_weight = lax.psum(col_part, "ang")
    current = volume
    scaled = measured
    for iteration in range(ITERS):
        low_volume = current.astype(jnp.bfloat16)
        partial_rows = project_local(low_volume, pattern, pixel_list, ray_list, ray_total)
        if iteration == 0:
            summed, row_weight = (
                lax.psum_scatter(partial_rows, "pix", scatter_dimension=0, tiled=True),
                lax.psum_scatter(row_part, "pix", scatter_dimension=0, tiled=True),
            )
        else:
            summed = lax.psum_scatter(partial_rows, "pix", scatter_dimension=0, tiled=True)
        scaled = (measured - summed) / jnp.tile(row_weight, (1, slices))
        scaled_low = scaled.astype(jnp.bfloat16)
        row_table = lax.all_gather(scaled_low, "pix", axis=0, tiled=True)
        back_sum = back_local(row_table, pattern, pixel_list, ray_list, tiles_dev)
        summed_update = lax.psum(back_sum, "ang")
        current = current + summed_update / jnp.tile(col_weight, (1, slices))
    return (current, scaled[None])


def split2(x):
    hi = lax.reduce_precision(x, exponent_bits=8, mantissa_bits=7)
    return (hi.astype(jnp.bfloat16), (x - hi).astype(jnp.bfloat16))


def per_device_split(volume, sinogram, table, blk_ray, blk_pix, n_pix, n_ang):
    n_grp = n_pix * n_ang
    tiles_dev = volume.shape[0]
    slices = volume.shape[1] // TILE
    per_dev = slices // n_grp
    rays_dev = sinogram.shape[1]
    nbd = blk_ray.shape[-1]
    ray_total = rays_dev * n_pix
    pix_total = tiles_dev * n_pix
    width = per_dev * TILE

    vol_send = volume.reshape(tiles_dev, n_grp, width).transpose(1, 0, 2)
    sino_send = sinogram[0].reshape(rays_dev, n_grp, width).transpose(1, 0, 2)
    cells = (blk_ray.reshape(-1) * tiles_dev + blk_pix.reshape(-1)).astype(jnp.float32)
    list_rows = (nbd + width - 1) // width
    lists = jnp.pad(cells, (0, list_rows * width - nbd)).reshape(list_rows, width)
    list_send = jnp.broadcast_to(lists[None], (n_grp, list_rows, width))
    rows = tiles_dev + rays_dev + list_rows
    paired = rows + rows % 2
    if tiles_dev % 2 == 0 and rays_dev % 2 == 0 and nbd % (2 * width) == 0:
        send = jnp.concatenate(
            [
                vol_send.reshape(n_grp, tiles_dev // 2, 2 * width),
                sino_send.reshape(n_grp, rays_dev // 2, 2 * width),
                jnp.broadcast_to(cells.reshape(1, list_rows // 2, 2 * width), (n_grp, list_rows // 2, 2 * width)),
            ],
            axis=1,
        )
    else:
        send = jnp.concatenate([vol_send, sino_send, list_send], axis=1)
        send = jnp.pad(send, ((0, 0), (0, paired - rows), (0, 0))).reshape(n_grp, paired // 2, 2 * width)
    recv = lax.all_to_all(send, ("pix", "ang"), 0, 0, tiled=False)
    recv = recv.reshape(n_pix, n_ang, paired, width)[:, :, :rows]

    current = recv[:, 0, :tiles_dev].reshape(pix_total, width)
    measured = recv[:, :, tiles_dev:tiles_dev + rays_dev].transpose(1, 0, 2, 3).reshape(n_ang, ray_total, width)
    cells = recv[:, :, tiles_dev + rays_dev:].reshape(n_pix, n_ang, -1)[:, :, :nbd]
    cells = cells.transpose(1, 0, 2)
    ray_of = jnp.floor(cells / tiles_dev)
    got = jnp.stack([ray_of, cells - ray_of * tiles_dev])
    per_kind = nbd // KINDS
    offsets = (jnp.arange(n_pix, dtype=jnp.float32) * tiles_dev)[None, :, None, None]
    ray_ids = got[0].reshape(n_ang, n_pix, KINDS, per_kind)
    pix_ids = got[1].reshape(n_ang, n_pix, KINDS, per_kind) + offsets
    ray_ids = ray_ids.transpose(0, 2, 1, 3).reshape(n_ang, KINDS, n_pix * per_kind)
    pix_ids = pix_ids.transpose(0, 2, 1, 3).reshape(n_ang, KINDS, n_pix * per_kind)

    one_ray = (ray_ids[..., None] == jnp.arange(ray_total, dtype=jnp.float32)).astype(jnp.bfloat16)
    one_pix = (pix_ids[..., None] == jnp.arange(pix_total, dtype=jnp.float32)).astype(jnp.bfloat16)
    count_low = jnp.einsum(
        "gkbv,gkbu->gkvu", one_ray, one_pix, preferred_element_type=jnp.float32
    ).astype(jnp.bfloat16)
    count_low = lax.optimization_barrier(count_low)
    counts = count_low.astype(jnp.float32)
    ray_count = jnp.sum(counts, axis=3)
    pix_count = jnp.sum(counts, axis=2)

    pattern = table.reshape(KINDS, TILE, TILE)
    pattern_wide = pattern.astype(jnp.float32)
    hi = lax.Precision.HIGHEST
    ray_weight = jnp.einsum("gkv,ki->gvi", ray_count, jnp.sum(pattern_wide, axis=2), precision=hi)
    pixel_weight = jnp.einsum("gku,kj->uj", pix_count, jnp.sum(pattern_wide, axis=1), precision=hi)
    ray_weight = jnp.tile(ray_weight, (1, 1, per_dev))
    pixel_weight = jnp.tile(pixel_weight, (1, per_dev))

    cur = current.reshape(pix_total, per_dev, TILE)
    meas = measured.reshape(n_ang, ray_total, per_dev, TILE)
    rw = ray_weight.reshape(n_ang, ray_total, per_dev, TILE)
    pw = pixel_weight.reshape(pix_total, per_dev, TILE)
    scaled = meas
    for iteration in range(ITERS):
        low = cur.astype(jnp.bfloat16)
        gathered = jnp.einsum("gkvu,usj->gkvsj", count_low, low, preferred_element_type=jnp.float32)
        proj = jnp.einsum(
            "gkvsj,kij->gvsi", gathered, pattern_wide, precision=lax.Precision.HIGHEST,
            preferred_element_type=jnp.float32,
        )
        scaled = (meas - proj) / rw
        scaled_low = scaled.astype(jnp.bfloat16)
        spread = jnp.einsum("gvsi,kij->gkvsj", scaled_low, pattern, preferred_element_type=jnp.float32)
        update = jnp.einsum(
            "gkvu,gkvsj->usj", counts, spread, precision=lax.Precision.HIGH,
            preferred_element_type=jnp.float32,
        )
        cur = cur + update / pw

    vol_back = cur.reshape(n_pix, tiles_dev, width)
    vol_back = jnp.broadcast_to(vol_back[:, None], (n_pix, n_ang, tiles_dev, width))
    res_back = scaled.reshape(n_ang, n_pix, rays_dev, width).transpose(1, 0, 2, 3)
    rows_back = tiles_dev + rays_dev
    paired_back = rows_back + rows_back % 2
    if tiles_dev % 2 == 0 and rays_dev % 2 == 0:
        back = jnp.concatenate(
            [
                vol_back.reshape(n_pix, n_ang, tiles_dev // 2, 2 * width),
                res_back.reshape(n_pix, n_ang, rays_dev // 2, 2 * width),
            ],
            axis=2,
        ).reshape(n_grp, paired_back // 2, 2 * width)
    else:
        back = jnp.concatenate([vol_back, res_back], axis=2).reshape(n_grp, rows_back, width)
        back = jnp.pad(back, ((0, 0), (0, paired_back - rows_back), (0, 0)))
        back = back.reshape(n_grp, paired_back // 2, 2 * width)
    got_back = lax.all_to_all(back, ("pix", "ang"), 0, 0, tiled=False)
    got_back = got_back.reshape(n_grp, paired_back, width)[:, :rows_back]
    both = got_back.transpose(1, 0, 2).reshape(rows_back, slices * TILE)
    vol_out = both[:tiles_dev]
    res_out = both[tiles_dev:].reshape(1, rays_dev, slices * TILE)
    return (vol_out, res_out)


def solution(mesh):
    n_pix = mesh.shape["pix"]
    n_ang = mesh.shape["ang"]

    def body(volume, sinogram, table, blk_ray, blk_pix):
        if (volume.shape[1] // TILE) % (n_pix * n_ang) == 0:
            return per_device_split(volume, sinogram, table, blk_ray, blk_pix, n_pix, n_ang)
        return per_device_base(volume, sinogram, table, blk_ray, blk_pix)

    return jax.shard_map(
        body,
        mesh=mesh,
        in_specs=(
            P(("parts", "pix"), "sl"),
            P(("parts", "ang"), "pix", "sl"),
            P(),
            P("ang", "pix", None),
            P("ang", "pix", None),
        ),
        out_specs=(P(("parts", "pix"), "sl"), P(("parts", "ang"), "pix", "sl")),
        check_vma=False,
    )
```

```python
import jax
import jax.numpy as jnp
from jax import lax
from jax.sharding import PartitionSpec as P

TILE = 64
KINDS = 32
ITERS = 2
PER_KIND = 44


def project_local(low_volume, pattern, pixel_list, ray_list, ray_total):
    tiles_dev = low_volume.shape[0]
    slices = low_volume.shape[1] // TILE
    low_tiles = low_volume.reshape(tiles_dev, slices, TILE)
    kinds_each = KINDS // 4

    def project_one_group(running, inputs):
        patterns, pix_ids, ray_ids = inputs
        picked = jnp.take(low_tiles, pix_ids, axis=0).reshape(kinds_each, PER_KIND, slices, TILE)
        images = jnp.einsum("kbsj,kij->kbsi", picked, patterns, preferred_element_type=jnp.float32)
        images = images.reshape(kinds_each * PER_KIND, slices * TILE)
        return (running + jax.ops.segment_sum(images, ray_ids, ray_total), None)

    inputs = (
        pattern.reshape(4, kinds_each, TILE, TILE),
        pixel_list.reshape(4, -1),
        ray_list.reshape(4, -1),
    )
    initial = jnp.zeros((ray_total, slices * TILE), jnp.float32)
    running, unused = lax.scan(project_one_group, initial, inputs)
    return running


def back_local(row_table, pattern, pixel_list, row_index, tiles_dev):
    slices = row_table.shape[1] // TILE
    table_tiles = row_table.reshape(row_table.shape[0], slices, TILE)
    kinds_each = KINDS // 4

    def back_one_group(running, inputs):
        patterns, pix_ids, row_ids = inputs
        picked = jnp.take(table_tiles, row_ids, axis=0).reshape(kinds_each, PER_KIND, slices, TILE)
        images = jnp.einsum("kbsi,kij->kbsj", picked, patterns, preferred_element_type=jnp.float32)
        images = images.reshape(kinds_each * PER_KIND, slices * TILE)
        return (running + jax.ops.segment_sum(images, pix_ids, tiles_dev), None)

    inputs = (
        pattern.reshape(4, kinds_each, TILE, TILE),
        pixel_list.reshape(4, -1),
        row_index.reshape(4, -1),
    )
    initial = jnp.zeros((tiles_dev, slices * TILE), jnp.float32)
    running, unused = lax.scan(back_one_group, initial, inputs)
    return running


def per_device_base(volume, sinogram, table, blk_ray, blk_pix):
    pix_count = lax.axis_size("pix")
    tiles_dev = volume.shape[0]
    row_width = volume.shape[1]
    slices = row_width // TILE
    rays_dev = sinogram.shape[1]
    ray_total = rays_dev * pix_count
    ray_list = blk_ray.reshape(-1)
    pixel_list = blk_pix.reshape(-1)
    pattern = table.reshape(KINDS, TILE, TILE)
    pattern_wide = table.astype(jnp.float32).reshape(KINDS, TILE, TILE)
    row_block = jnp.broadcast_to(
        jnp.sum(pattern_wide, axis=2)[:, None, :], (KINDS, PER_KIND, TILE)
    ).reshape(-1, TILE)
    col_block = jnp.broadcast_to(
        jnp.sum(pattern_wide, axis=1)[:, None, :], (KINDS, PER_KIND, TILE)
    ).reshape(-1, TILE)
    row_part = jax.ops.segment_sum(row_block, ray_list, ray_total)
    col_part = jax.ops.segment_sum(col_block, pixel_list, tiles_dev)
    measured = sinogram[0]
    col_weight = lax.psum(col_part, "ang")
    current = volume
    scaled = measured
    for iteration in range(ITERS):
        low_volume = current.astype(jnp.bfloat16)
        partial_rows = project_local(low_volume, pattern, pixel_list, ray_list, ray_total)
        if iteration == 0:
            summed, row_weight = (
                lax.psum_scatter(partial_rows, "pix", scatter_dimension=0, tiled=True),
                lax.psum_scatter(row_part, "pix", scatter_dimension=0, tiled=True),
            )
        else:
            summed = lax.psum_scatter(partial_rows, "pix", scatter_dimension=0, tiled=True)
        scaled = (measured - summed) / jnp.tile(row_weight, (1, slices))
        scaled_low = scaled.astype(jnp.bfloat16)
        row_table = lax.all_gather(scaled_low, "pix", axis=0, tiled=True)
        back_sum = back_local(row_table, pattern, pixel_list, ray_list, tiles_dev)
        summed_update = lax.psum(back_sum, "ang")
        current = current + summed_update / jnp.tile(col_weight, (1, slices))
    return (current, scaled[None])


def split2(x):
    hi = lax.reduce_precision(x, exponent_bits=8, mantissa_bits=7)
    return (hi.astype(jnp.bfloat16), (x - hi).astype(jnp.bfloat16))


def per_device_split(volume, sinogram, table, blk_ray, blk_pix, n_pix, n_ang):
    n_grp = n_pix * n_ang
    tiles_dev = volume.shape[0]
    slices = volume.shape[1] // TILE
    per_dev = slices // n_grp
    rays_dev = sinogram.shape[1]
    nbd = blk_ray.shape[-1]
    ray_total = rays_dev * n_pix
    pix_total = tiles_dev * n_pix
    width = per_dev * TILE

    vol_send = volume.reshape(tiles_dev, n_grp, width).transpose(1, 0, 2)
    sino_send = sinogram[0].reshape(rays_dev, n_grp, width).transpose(1, 0, 2)
    cells = (blk_ray.reshape(-1) * tiles_dev + blk_pix.reshape(-1)).astype(jnp.float32)
    list_rows = (nbd + width - 1) // width
    lists = jnp.pad(cells, (0, list_rows * width - nbd)).reshape(list_rows, width)
    list_send = jnp.broadcast_to(lists[None], (n_grp, list_rows, width))
    rows = tiles_dev + rays_dev + list_rows
    paired = rows + rows % 2
    if tiles_dev % 2 == 0 and rays_dev % 2 == 0 and nbd % (2 * width) == 0:
        send = jnp.concatenate(
            [
                vol_send.reshape(n_grp, tiles_dev // 2, 2 * width),
                sino_send.reshape(n_grp, rays_dev // 2, 2 * width),
                jnp.broadcast_to(cells.reshape(1, list_rows // 2, 2 * width), (n_grp, list_rows // 2, 2 * width)),
            ],
            axis=1,
        )
    else:
        send = jnp.concatenate([vol_send, sino_send, list_send], axis=1)
        send = jnp.pad(send, ((0, 0), (0, paired - rows), (0, 0))).reshape(n_grp, paired // 2, 2 * width)
    recv = lax.all_to_all(send, ("pix", "ang"), 0, 0, tiled=False)
    recv = recv.reshape(n_pix, n_ang, paired, width)[:, :, :rows]

    current = recv[:, 0, :tiles_dev].reshape(pix_total, width)
    measured = recv[:, :, tiles_dev:tiles_dev + rays_dev].transpose(1, 0, 2, 3).reshape(n_ang, ray_total, width)
    cells = recv[:, :, tiles_dev + rays_dev:].reshape(n_pix, n_ang, -1)[:, :, :nbd]
    cells = cells.transpose(1, 0, 2)
    ray_of = jnp.floor(cells / tiles_dev)
    got = jnp.stack([ray_of, cells - ray_of * tiles_dev])
    per_kind = nbd // KINDS
    offsets = (jnp.arange(n_pix, dtype=jnp.float32) * tiles_dev)[None, :, None, None]
    ray_ids = got[0].reshape(n_ang, n_pix, KINDS, per_kind)
    pix_ids = got[1].reshape(n_ang, n_pix, KINDS, per_kind) + offsets
    ray_ids = ray_ids.transpose(0, 2, 1, 3).reshape(n_ang, KINDS, n_pix * per_kind)
    pix_ids = pix_ids.transpose(0, 2, 1, 3).reshape(n_ang, KINDS, n_pix * per_kind)

    one_ray = (ray_ids[..., None] == jnp.arange(ray_total, dtype=jnp.float32)).astype(jnp.bfloat16)
    one_pix = (pix_ids[..., None] == jnp.arange(pix_total, dtype=jnp.float32)).astype(jnp.bfloat16)
    count_low = jnp.einsum(
        "gkbv,gkbu->gkvu", one_ray, one_pix, preferred_element_type=jnp.float32
    ).astype(jnp.bfloat16)

    counts = count_low.astype(jnp.float32)
    ray_count = jnp.sum(counts, axis=3)
    pix_count = jnp.sum(counts, axis=2)

    pattern = table.reshape(KINDS, TILE, TILE)
    pattern_wide = pattern.astype(jnp.float32)
    hi = lax.Precision.HIGHEST
    ray_weight = jnp.einsum("gkv,ki->gvi", ray_count, jnp.sum(pattern_wide, axis=2), precision=hi)
    pixel_weight = jnp.einsum("gku,kj->uj", pix_count, jnp.sum(pattern_wide, axis=1), precision=hi)
    ray_weight = jnp.tile(ray_weight, (1, 1, per_dev))
    pixel_weight = jnp.tile(pixel_weight, (1, per_dev))

    cur = current.reshape(pix_total, per_dev, TILE)
    meas = measured.reshape(n_ang, ray_total, per_dev, TILE)
    rw = ray_weight.reshape(n_ang, ray_total, per_dev, TILE)
    pw = pixel_weight.reshape(pix_total, per_dev, TILE)
    scaled = meas
    for iteration in range(ITERS):
        low = cur.astype(jnp.bfloat16)
        gathered = jnp.einsum("gkvu,usj->gkvsj", count_low, low, preferred_element_type=jnp.float32)
        proj = jnp.einsum(
            "gkvsj,kij->gvsi", gathered, pattern_wide, precision=lax.Precision.HIGHEST,
            preferred_element_type=jnp.float32,
        )
        scaled = (meas - proj) / rw
        scaled_low = scaled.astype(jnp.bfloat16)
        spread = jnp.einsum("gvsi,kij->gkvsj", scaled_low, pattern, preferred_element_type=jnp.float32)
        update = jnp.einsum(
            "gkvu,gkvsj->usj", counts, spread, precision=lax.Precision.HIGH,
            preferred_element_type=jnp.float32,
        )
        cur = cur + update / pw

    vol_back = cur.reshape(n_pix, tiles_dev, width)
    vol_back = jnp.broadcast_to(vol_back[:, None], (n_pix, n_ang, tiles_dev, width))
    res_back = scaled.reshape(n_ang, n_pix, rays_dev, width).transpose(1, 0, 2, 3)
    back = jnp.concatenate([vol_back, res_back], axis=2).reshape(n_grp, tiles_dev + rays_dev, width)
    rows_back = tiles_dev + rays_dev
    paired_back = rows_back + rows_back % 2
    back = jnp.pad(back, ((0, 0), (0, paired_back - rows_back), (0, 0)))
    back = back.reshape(n_grp, paired_back // 2, 2 * width)
    got_back = lax.all_to_all(back, ("pix", "ang"), 0, 0, tiled=False)
    got_back = got_back.reshape(n_grp, paired_back, width)[:, :rows_back]
    both = got_back.transpose(1, 0, 2).reshape(rows_back, slices * TILE)
    vol_out = both[:tiles_dev]
    res_out = both[tiles_dev:].reshape(1, rays_dev, slices * TILE)
    return (vol_out, res_out)


def solution(mesh):
    n_pix = mesh.shape["pix"]
    n_ang = mesh.shape["ang"]

    def body(volume, sinogram, table, blk_ray, blk_pix):
        if (volume.shape[1] // TILE) % (n_pix * n_ang) == 0:
            return per_device_split(volume, sinogram, table, blk_ray, blk_pix, n_pix, n_ang)
        return per_device_base(volume, sinogram, table, blk_ray, blk_pix)

    return jax.shard_map(
        body,
        mesh=mesh,
        in_specs=(
            P(("parts", "pix"), "sl"),
            P(("parts", "ang"), "pix", "sl"),
            P(),
            P("ang", "pix", None),
            P("ang", "pix", None),
        ),
        out_specs=(P(("parts", "pix"), "sl"), P(("parts", "ang"), "pix", "sl")),
        check_vma=False,
    )
```
